256 devices in a mesh: req: 32 (over y, z), head: 8 (over x, core).
Axes of the slice: x: 4, y: 4, z: 8, core: 2. Of those that a mesh axis runs over, the one named last changes fastest.
Arguments:
- tokens: bfloat16 [2048, 1024], P(('req', 'head')), may hold values from -6 to 6
- gains: float32 [2, 1024], replicated, may hold values from 0.1 to 1.9
- qkv_weight: bfloat16 [3, 1024, 1024], P(None, None, 'head'), may hold values from -0.1875 to 0.1875
- out_weight: bfloat16 [1024, 1024], replicated, may hold values from -0.1875 to 0.1875
- gate_up_weight: bfloat16 [2, 1024, 4096], P(None, None, 'head'), may hold values from -0.1875 to 0.1875
- down_weight: bfloat16 [4096, 1024], P('head'), may hold values from -0.09375 to 0.09375
- variate_bias: float32 [2, 16], replicated, may hold values from -4 to 4
- page_cache: bfloat16 [2, 640, 128, 1024], P(None, 'req', None, 'head'), may hold values from -210 to 210
- page_variates: int32 [640, 128], P('req'), may hold values from 0 to 3
- token_variates: int32 [2048], replicated, may hold values from 0 to 3
- cache_len: int32 [32], replicated, may hold values from 64 to 4096, as said below
- page_table: int32 [32, 32], replicated, may hold values from -1 to 639, as said below
- parents: int32 [32, 64], P('req'), may hold values from -1 to 55, as said below
- accepted: int32 [32, 8], P('req'), may hold values from -1 to 63, as said below
Outputs:
- mixed: bfloat16 [2048, 1024], P(('req', 'head'))
- attended: bfloat16 [2048, 1024], P('req', 'head')
- new_kv: bfloat16 [2, 32, 8, 1024], P(None, 'req', None, 'head')
The draws below stay inside these ranges and needn't reach their ends.
Inputs may be any that keep to these rules, and one draw needn't show every extreme that they name: `cache_len`: exactly half of the requests have 128 // 2 to 128 cached positions, the others 4096 // 2 + 1 to 4096. `page_table`: entry [r, b] is the page holding request r's positions b * 128 to b * 128 + 127 for b below ceil(cache_len[r] / 128), and -1 from there on; no page is listed twice. `parents`: node i lies on level i // 8; nodes of level 0 have parent -1, every other node's parent lies on the level before. `accepted`: row r lists a path of request r's tree from a level-0 node downward, one node a level, then -1; its length is 1 to 8, and 8 in some row.
All inputs are finite; a program needn't handle non-finite values.
Results may differ from the reference program's by a relative error of at most 0.015.
The reference program's roundings to bfloat16 on the way (of `normed`, `weights`, `hidden_state`, `normed_two` and `activated`) count: a program that leaves them out, or rounds other values in their place, can miss the bound.
Values may be sent and summed in bfloat16 or wider, within the bound.
No kernel may reach another device: no remote copies, remote signals or barrier semaphores. Data moves between devices by JAX's collectives and lax.ppermute only.
A program may use at most 192 MiB of HBM per device.

```python
import math
import jax
import jax.numpy as jnp
from jax import lax

D = 1024
HEADS = 16
HD = 64
FF = 4096
BRANCH = 8
LEVELS = 8
PAGE = 128
MAXP = 32
NVAR = 4
TREE = 64
QD = 1024
CACHE = 4096
REQUESTS = 32
TOKENS = 2048
PAGES = 640


def lengths_and_table(key):
    base = jax.random.fold_in(key, 11)
    key_order, key_short, key_long, key_pages = jax.random.split(base, 4)
    order = jax.random.permutation(key_order, REQUESTS)
    short_len = jax.random.randint(key_short, (REQUESTS,), PAGE // 2, PAGE + 1)
    long_len = jax.random.randint(key_long, (REQUESTS,), CACHE // 2 + 1, CACHE + 1)
    lengths = jnp.where(order < REQUESTS // 2, long_len, short_len)
    lengths = jnp.where(order == 0, CACHE, lengths)
    lengths = jnp.where(order == REQUESTS - 1, PAGE // 2, lengths)
    counts = (lengths + PAGE - 1) // PAGE
    offsets = jnp.cumsum(counts) - counts
    shuffled = jax.random.permutation(key_pages, PAGES).astype(jnp.int32)
    first_page = shuffled[0]
    place = jnp.arange(PAGES, dtype=jnp.int32)
    shuffled = jnp.where(place == 0, PAGES - 1, jnp.where(shuffled == PAGES - 1, first_page, shuffled))
    column = jnp.arange(MAXP, dtype=jnp.int32)
    index = jnp.clip(offsets[:, None] + column[None, :], 0, PAGES - 1)
    table = jnp.where(column[None, :] < counts[:, None], shuffled[index], -1)
    return (lengths.astype(jnp.int32), table.astype(jnp.int32))


def draw_cache_len(key, part):
    return lengths_and_table(key)[0]


def draw_page_table(key, part):
    return lengths_and_table(key)[1]


def tree_and_path(key):
    base = jax.random.fold_in(key, 23)
    key_pick, key_depth, key_forced, key_leaf = jax.random.split(base, 4)
    nodes = jnp.arange(TREE, dtype=jnp.int32)
    level = nodes // BRANCH
    pick = jax.random.randint(key_pick, (REQUESTS, TREE), 0, BRANCH)
    request_ids = jnp.arange(REQUESTS, dtype=jnp.int32)
    pick = jnp.where((request_ids[:, None] == 0) & (nodes[None, :] == TREE - 1), BRANCH - 1, pick)
    parent_rows = jnp.where(level[None, :] >= 1, (level[None, :] - 1) * BRANCH + pick, -1)
    depth = jax.random.randint(key_depth, (REQUESTS,), 1, LEVELS + 1)
    forced = jax.random.randint(key_forced, (), 0, REQUESTS)
    shallow = (forced + 1) % REQUESTS
    depth = jnp.where(request_ids == shallow, 1, depth)
    depth = jnp.where(request_ids == forced, LEVELS, depth)
    leaf = jax.random.randint(key_leaf, (REQUESTS,), 0, BRANCH)
    leaf = jnp.where(request_ids == forced, BRANCH - 1, leaf)
    current = (depth - 1) * BRANCH + leaf
    upward = []
    for step in range(LEVELS):
        upward.append(current)
        above = jnp.take_along_axis(parent_rows, jnp.maximum(current, 0)[:, None], axis=1)[:, 0]
        current = jnp.where(current >= 0, above, -1)
    climb = jnp.stack(upward, axis=1)
    column = jnp.arange(LEVELS, dtype=jnp.int32)
    source = depth[:, None] - 1 - column[None, :]
    path = jnp.where(source >= 0, jnp.take_along_axis(climb, jnp.maximum(source, 0), axis=1), -1)
    return (parent_rows.astype(jnp.int32), path.astype(jnp.int32))


def draw_parents(key, part):
    return tree_and_path(key)[0]


def draw_accepted(key, part):
    return tree_and_path(key)[1]


def draw_page_cache(key, part):
    key_base = jax.random.fold_in(key, 0)
    shape = (2, PAGES, PAGE, QD)
    result = jnp.clip(jax.random.normal(key_base, shape, jnp.float32) * 2.0, -12.0, 12.0)
    return result.astype(jnp.bfloat16)


def touch_ends(values, key, low, top_value):
    extent = values.shape
    spot = [jax.random.randint(jax.random.fold_in(key, axis), (), 0, extent[axis]) for axis in range(len(extent))]
    values = values.at[tuple(spot)].set(low)
    longest = extent.index(max(extent))
    spot[longest] = (spot[longest] + 1) % extent[longest]
    return values.at[tuple(spot)].set(top_value)


def levels(stream_key, dims, shards, low, largest):
    factor_of, own = 1.0, jax.random.fold_in(stream_key, 6)
    for dim, shards_of in shards:
        steps = jnp.exp(jax.random.uniform(jax.random.fold_in(own, dim), (shards_of,), jnp.float32, low / len(shards), largest / len(shards)))
        factor_of = factor_of * jnp.repeat(steps, dims[dim] // shards_of).reshape([-1 if axis == dim else 1 for axis in range(len(dims))])
    return factor_of


def scatter_about(stream_key, shape, scale, most, cuts=(), held_as=jnp.bfloat16):
    array = jax.random.normal(stream_key, shape, jnp.float32) * scale
    if len(cuts) > 0:
        array = levels(stream_key, shape, cuts, -0.22, 0.18) * array
    return jnp.clip(array, min=-most, max=most).astype(held_as)


def setup_inputs(seed: int = 0) -> dict:
    arg_keys = jax.random.split(jax.random.key(seed), 15)
    tokens = scatter_about(arg_keys[0], (TOKENS, D), 1.0, 6.0, ((0, 256),))
    gains = jnp.clip(1.0 + 0.18 * jax.random.normal(arg_keys[1], (2, D), jnp.float32), 0.1, 1.9)
    qkv_weight = scatter_about(arg_keys[2], (3, D, QD), D ** -0.5, 0.1875, ((2, 8),))
    out_weight = scatter_about(arg_keys[3], (QD, D), QD ** -0.5, 0.1875)
    gate_up_weight = scatter_about(arg_keys[4], (2, D, FF), D ** -0.5, 0.1875, ((2, 8),))
    down_weight = scatter_about(arg_keys[5], (FF, D), FF ** -0.5, 0.09375, ((0, 8),))
    variate_bias = scatter_about(arg_keys[6], (2, HEADS), 1.0, 4.0, (), jnp.float32)
    page_cache = draw_page_cache(jax.random.fold_in(arg_keys[14], 71), 0)
    page_variates = touch_ends(jax.random.randint(arg_keys[8], (PAGES, PAGE), 0, NVAR), jax.random.fold_in(arg_keys[8], 1), 0, NVAR - 1).astype(jnp.int32)
    token_variates = touch_ends(jax.random.randint(arg_keys[9], (TOKENS,), 0, NVAR), jax.random.fold_in(arg_keys[9], 1), 0, NVAR - 1).astype(jnp.int32)
    cache_len = draw_cache_len(jax.random.fold_in(arg_keys[14], 71), 0)
    page_table = draw_page_table(jax.random.fold_in(arg_keys[14], 71), 0)
    parents = draw_parents(jax.random.fold_in(arg_keys[14], 71), 0)
    accepted = draw_accepted(jax.random.fold_in(arg_keys[14], 71), 0)
    return dict(tokens=tokens, gains=gains, qkv_weight=qkv_weight, out_weight=out_weight, gate_up_weight=gate_up_weight, down_weight=down_weight, variate_bias=variate_bias, page_cache=page_cache, page_variates=page_variates, token_variates=token_variates, cache_len=cache_len, page_table=page_table, parents=parents, accepted=accepted)


epsilon = 1e-06
masked_score = -1e+30
highest = lax.Precision.HIGHEST

def rms_scaled(rows, gain):
    values = rows.astype(jnp.float32)
    return values * lax.rsqrt(lax.optimization_barrier(jnp.mean(values * values, axis=-1, keepdims=True)) + epsilon) * gain

def ancestry(parent_row):
    width = parent_row.shape[0]
    nodes = jnp.arange(width, dtype=jnp.int32)
    reach = (parent_row[:, None] == nodes[None, :]).astype(jnp.float32) + jnp.eye(width, dtype=jnp.float32)
    for step in range(LEVELS.bit_length()):
        reach = jnp.minimum(jnp.dot(reach, reach, precision=highest), 1.0)
    return reach > 0.5

def reference(tokens, gains, qkv_weight, out_weight, gate_up_weight, down_weight, variate_bias, page_cache, page_variates, token_variates, cache_len, page_table, parents, accepted):
    scale = 1.0 / math.sqrt(HD)
    normed = rms_scaled(tokens, gains[0]).astype(jnp.bfloat16)
    query = jnp.dot(normed, qkv_weight[0], preferred_element_type=jnp.float32).astype(jnp.bfloat16)
    key_rows = jnp.dot(normed, qkv_weight[1], preferred_element_type=jnp.float32).astype(jnp.bfloat16)
    value_rows = jnp.dot(normed, qkv_weight[2], preferred_element_type=jnp.float32).astype(jnp.bfloat16)
    same_bias = variate_bias[0]
    other_bias = variate_bias[1]

    def one_request(inputs):
        request_query, request_key, request_value, table, length, parent_row, variates = inputs
        slots = jnp.where(table >= 0, table, 0)
        page_keys = jnp.take(page_cache[0], slots, axis=0).reshape(MAXP, PAGE, HEADS, HD).astype(jnp.float32)
        page_values = jnp.take(page_cache[1], slots, axis=0).reshape(MAXP, PAGE, HEADS, HD).astype(jnp.float32)
        cached_variates = jnp.take(page_variates, slots, axis=0)
        positions = jnp.arange(MAXP)[:, None] * PAGE + jnp.arange(PAGE)[None, :]
        valid = positions < length
        scores = jnp.einsum('thd,pkhd->pthk', request_query.astype(jnp.float32), page_keys, precision=highest) * scale
        same_page = variates[None, :, None] == cached_variates[:, None, :]
        scores = scores + jnp.where(same_page[:, :, None, :], same_bias[None, None, :, None], other_bias[None, None, :, None])
        keep = valid[:, None, None, :]
        page_max = lax.optimization_barrier(jnp.max(jnp.where(keep, scores, masked_score), axis=-1))
        weights = jnp.where(keep, jnp.exp(scores - page_max[..., None]), 0.0).astype(jnp.bfloat16)
        weights = lax.optimization_barrier(weights).astype(jnp.float32)
        page_total = lax.optimization_barrier(jnp.sum(weights, axis=-1))
        page_out = jnp.einsum('pthk,pkhd->pthd', weights, page_values, precision=highest)
        allowed = ancestry(parent_row)
        tree_scores = jnp.einsum('ihd,jhd->ihj', request_query.astype(jnp.float32), request_key.astype(jnp.float32), precision=highest) * scale
        same_tree = variates[:, None] == variates[None, :]
        tree_scores = tree_scores + jnp.where(same_tree[:, None, :], same_bias[None, :, None], other_bias[None, :, None])
        keep_tree = allowed[:, None, :]
        tree_max = lax.optimization_barrier(jnp.max(jnp.where(keep_tree, tree_scores, masked_score), axis=-1))
        tree_weights = jnp.where(keep_tree, jnp.exp(tree_scores - tree_max[..., None]), 0.0).astype(jnp.bfloat16)
        tree_weights = lax.optimization_barrier(tree_weights).astype(jnp.float32)
        tree_total = lax.optimization_barrier(jnp.sum(tree_weights, axis=-1))
        tree_out = jnp.einsum('ihj,jhd->ihd', tree_weights, request_value.astype(jnp.float32), precision=highest)
        overall = jnp.maximum(lax.optimization_barrier(jnp.max(page_max, axis=0)), tree_max)
        page_factor = jnp.exp(page_max - overall[None])
        tree_factor = jnp.exp(tree_max - overall)
        total = lax.optimization_barrier(jnp.sum(page_total * page_factor, axis=0)) + tree_total * tree_factor
        combined = lax.optimization_barrier(jnp.sum(page_out * page_factor[..., None], axis=0)) + tree_out * tree_factor[..., None]
        return (combined / total[..., None]).astype(jnp.bfloat16).reshape(TREE, QD)
    attended = lax.map(one_request, (query.reshape(REQUESTS, TREE, HEADS, HD), key_rows.reshape(REQUESTS, TREE, HEADS, HD), value_rows.reshape(REQUESTS, TREE, HEADS, HD), page_table, cache_len, parents, token_variates.reshape(REQUESTS, TREE)))
    attended = attended.reshape(TOKENS, QD)
    hidden_state = (tokens.astype(jnp.float32) + jnp.dot(attended, out_weight, preferred_element_type=jnp.float32)).astype(jnp.bfloat16)
    normed_two = rms_scaled(hidden_state, gains[1]).astype(jnp.bfloat16)
    gate = jnp.dot(normed_two, gate_up_weight[0], preferred_element_type=jnp.float32)
    upward = jnp.dot(normed_two, gate_up_weight[1], preferred_element_type=jnp.float32)
    activated = (jax.nn.silu(gate) * upward).astype(jnp.bfloat16)
    mixed = (hidden_state.astype(jnp.float32) + jnp.dot(activated, down_weight, preferred_element_type=jnp.float32)).astype(jnp.bfloat16)
    nodes = jnp.arange(TREE, dtype=jnp.int32)
    chosen = (accepted[:, :, None] == nodes[None, None, :]).astype(jnp.float32)
    new_keys = jnp.einsum('rat,rtq->raq', chosen, key_rows.reshape(REQUESTS, TREE, QD).astype(jnp.float32), precision=highest)
    new_values = jnp.einsum('rat,rtq->raq', chosen, value_rows.reshape(REQUESTS, TREE, QD).astype(jnp.float32), precision=highest)
    new_kv = jnp.stack([new_keys, new_values]).astype(jnp.bfloat16)
    return (mixed, attended, new_kv)
```

```python
import math

import jax
import jax.numpy as jnp
from jax import lax
from jax.sharding import PartitionSpec as P

HD = 64
LEVELS = 8


epsilon = 1e-06
masked_score = -1e30
highest = lax.Precision.HIGHEST


def rms_scaled(rows, gain):
    values = rows.astype(jnp.float32)
    return values * lax.rsqrt(jnp.mean(values * values, axis=-1, keepdims=True) + epsilon) * gain


def merge_parts(first, second):
    max_one, total_one, out_one = first
    max_two, total_two, out_two = second
    highest_max = jnp.maximum(max_one, max_two)
    factor_one = jnp.exp(max_one - highest_max)
    factor_two = jnp.exp(max_two - highest_max)
    return (
        highest_max,
        total_one * factor_one + total_two * factor_two,
        out_one * factor_one[..., None] + out_two * factor_two[..., None],
    )


def gather_rows(rows, axis_name, parts):
    spread = jnp.broadcast_to(rows[None], (parts,) + rows.shape)
    return lax.all_to_all(spread, axis_name, 0, 0, tiled=True)


def shards(
    tokens,
    gains,
    qkv_weight,
    out_weight,
    gate_up_weight,
    down_weight,
    variate_bias,
    page_cache,
    page_variates,
    token_variates,
    cache_len,
    page_table,
    parents,
    accepted,
):
    scale = 1.0 / math.sqrt(HD)
    local_req, tree = parents.shape
    pool, page = page_variates.shape
    requests = cache_len.shape[0]
    qdl = qkv_weight.shape[2]
    head_local = qdl // HD
    head_slot = lax.axis_index("head")
    req_slot = lax.axis_index("req")
    bias_local = lax.dynamic_slice_in_dim(variate_bias, head_slot * head_local, head_local, 1)
    same_bias = bias_local[0]
    other_bias = bias_local[1]
    head_parts = lax.axis_size("head")
    group_tokens = gather_rows(tokens, "head", head_parts).reshape(-1, tokens.shape[1])
    normed = rms_scaled(group_tokens, gains[0]).astype(jnp.bfloat16)
    projected = jnp.einsum(
        "td,cdq->ctq",
        normed,
        qkv_weight,
        preferred_element_type=jnp.float32,
    ).astype(jnp.bfloat16)
    query = projected[0]
    key_new = projected[1]
    value_new = projected[2]
    all_queries = gather_rows(query, "req", requests // local_req)
    global_ids = req_slot * pool + jnp.arange(pool, dtype=jnp.int32)
    matching = (page_table[:, :, None] == global_ids[None, None, :]).astype(jnp.int32)
    owner = jnp.sum(matching * jnp.arange(requests, dtype=jnp.int32)[:, None, None], axis=(0, 1))
    page_order = jnp.sum(
        matching * jnp.arange(page_table.shape[1], dtype=jnp.int32)[None, :, None], axis=(0, 1)
    )
    owner_len = jnp.sum(matching * cache_len[:, None, None], axis=(0, 1))
    in_use = jnp.sum(matching, axis=(0, 1))
    filled = jnp.clip(owner_len - page_order * page, 0, page) * in_use
    valid = jnp.arange(page, dtype=jnp.int32)[None, :] < filled[:, None]
    page_queries = jnp.take(all_queries.reshape(requests, tree, head_local, HD), owner, axis=0)
    query_variates = jnp.take(token_variates.reshape(requests, tree), owner, axis=0)
    cache_keys = page_cache[0].reshape(pool, page, head_local, HD)
    cache_values = page_cache[1].reshape(pool, page, head_local, HD)
    scores = (
        jnp.einsum("pthd,pkhd->pthk", page_queries, cache_keys, preferred_element_type=jnp.float32)
        * scale
    )
    same_page = query_variates[:, :, None] == page_variates[:, None, :]
    scores = scores + jnp.where(
        same_page[:, :, None, :], same_bias[None, None, :, None], other_bias[None, None, :, None]
    )
    keep = valid[:, None, None, :]
    page_max = jnp.max(jnp.where(keep, scores, masked_score), axis=-1)
    weights = jnp.where(keep, jnp.exp(scores - page_max[..., None]), 0.0).astype(jnp.bfloat16)
    page_total = jnp.sum(weights, axis=-1, dtype=jnp.float32)
    page_out = jnp.einsum(
        "pthk,pkhd->pthd", weights, cache_values, preferred_element_type=jnp.float32
    )
    member = (owner[None, :] == jnp.arange(requests, dtype=jnp.int32)[:, None]) & (
        in_use[None, :] > 0
    )
    request_max = jnp.max(jnp.where(member[:, :, None, None], page_max[None], masked_score), axis=1)
    owner_max = jnp.take(request_max, owner, axis=0)
    factor = jnp.where(in_use[:, None, None] > 0, jnp.exp(page_max - owner_max), 0.0)
    member_float = member.astype(jnp.float32)
    request_total = jnp.dot(
        member_float, (page_total * factor).reshape(pool, -1), precision=highest
    ).reshape(requests, tree, head_local)
    request_out = jnp.dot(
        member_float, (page_out * factor[..., None]).reshape(pool, -1), precision=highest
    ).reshape(requests, tree, head_local, HD)
    packed = jnp.concatenate(
        [request_out, request_total[..., None], request_max[..., None]], axis=-1
    )
    received = lax.all_to_all(packed, "req", split_axis=0, concat_axis=0, tiled=True)
    sources = lax.axis_size("req")
    received = received.reshape((sources, local_req) + received.shape[1:])
    source_out = received[..., :HD]
    source_total = received[..., HD]
    source_max = received[..., HD + 1]
    largest = jnp.max(source_max, axis=0)
    source_factor = jnp.exp(source_max - largest[None])
    cached_part = (
        largest,
        jnp.sum(source_total * source_factor, axis=0),
        jnp.sum(source_out * source_factor[..., None], axis=0),
    )
    tree_query = query.reshape(local_req, tree, head_local, HD)
    tree_key = key_new.reshape(local_req, tree, head_local, HD)
    tree_value = value_new.reshape(local_req, tree, head_local, HD)
    nodes = jnp.arange(tree, dtype=jnp.int32)
    reach = (parents[:, :, None] == nodes[None, None, :]).astype(jnp.float32) + jnp.eye(
        tree, dtype=jnp.float32
    )[None]
    for step in range(LEVELS.bit_length()):
        reach = jnp.minimum(jnp.einsum("rij,rjk->rik", reach, reach, precision=highest), 1.0)
    allowed = reach > 0.5
    group_variates = lax.dynamic_slice_in_dim(
        token_variates, req_slot * local_req * tree, local_req * tree, 0
    ).reshape(local_req, tree)
    tree_scores = (
        jnp.einsum("rihd,rjhd->rihj", tree_query, tree_key, preferred_element_type=jnp.float32)
        * scale
    )
    same_tree = group_variates[:, :, None] == group_variates[:, None, :]
    tree_scores = tree_scores + jnp.where(
        same_tree[:, :, None, :], same_bias[None, None, :, None], other_bias[None, None, :, None]
    )
    keep_tree = allowed[:, :, None, :]
    tree_max = jnp.max(jnp.where(keep_tree, tree_scores, masked_score), axis=-1)
    tree_weights = jnp.where(keep_tree, jnp.exp(tree_scores - tree_max[..., None]), 0.0).astype(
        jnp.bfloat16
    )
    tree_total = jnp.sum(tree_weights, axis=-1, dtype=jnp.float32)
    tree_out = jnp.einsum(
        "rihj,rjhd->rihd", tree_weights, tree_value, preferred_element_type=jnp.float32
    )
    final_max, final_total, final_out = merge_parts(cached_part, (tree_max, tree_total, tree_out))
    attended = (
        (final_out / final_total[..., None]).astype(jnp.bfloat16).reshape(local_req * tree, qdl)
    )
    group_rows = local_req * tree
    token_heads = (
        gather_rows(attended, "head", head_parts).transpose(1, 0, 2).reshape(group_rows, -1)
    )
    attention_rows = jnp.dot(token_heads, out_weight, preferred_element_type=jnp.float32)
    hidden_state = (group_tokens.astype(jnp.float32) + attention_rows).astype(jnp.bfloat16)
    normed_two = rms_scaled(hidden_state, gains[1]).astype(jnp.bfloat16)
    both_parts = jnp.einsum(
        "td,cdf->ctf",
        normed_two,
        gate_up_weight,
        preferred_element_type=jnp.float32,
    )
    activated = (jax.nn.silu(both_parts[0]) * both_parts[1]).astype(jnp.bfloat16)
    down_part = jnp.dot(activated, down_weight, preferred_element_type=jnp.float32).astype(
        jnp.bfloat16
    )
    own_rows = tokens.shape[0]
    down_parts = lax.all_to_all(
        down_part.reshape(head_parts, own_rows, -1), "head", 0, 0, tiled=True
    )
    ffn_rows = jnp.sum(down_parts.astype(jnp.float32), axis=0)
    own_hidden = lax.dynamic_slice_in_dim(hidden_state, head_slot * own_rows, own_rows, 0)
    mixed = (own_hidden.astype(jnp.float32) + ffn_rows).astype(jnp.bfloat16)
    chosen = (accepted[:, :, None] == nodes[None, None, :]).astype(jnp.bfloat16)
    stacked = jnp.stack([key_new, value_new]).reshape(2, local_req, tree, qdl)
    new_kv = jnp.einsum(
        "rat,crtq->craq", chosen, stacked, preferred_element_type=jnp.float32
    ).astype(jnp.bfloat16)
    return (mixed, attended, new_kv)


def solution(mesh):
    return jax.shard_map(
        shards,
        mesh=mesh,
        in_specs=(
            P(("req", "head"), None),
            P(),
            P(None, None, "head"),
            P(),
            P(None, None, "head"),
            P("head", None),
            P(),
            P(None, "req", None, "head"),
            P("req", None),
            P(),
            P(),
            P(),
            P("req", None),
            P("req", None),
        ),
        out_specs=(P(("req", "head"), None), P("req", "head"), P(None, "req", None, "head")),
        check_vma=False,
    )
```

```python
import math

import jax
import jax.numpy as jnp
from jax import lax
from jax.sharding import PartitionSpec as P

HD = 64
LEVELS = 8


epsilon = 1e-06
masked_score = -1e30
highest = lax.Precision.HIGHEST


def rms_scaled(rows, gain):
    values = rows.astype(jnp.float32)
    return values * lax.rsqrt(jnp.mean(values * values, axis=-1, keepdims=True) + epsilon) * gain


def merge_parts(first, second):
    max_one, total_one, out_one = first
    max_two, total_two, out_two = second
    highest_max = jnp.maximum(max_one, max_two)
    factor_one = jnp.exp(max_one - highest_max)
    factor_two = jnp.exp(max_two - highest_max)
    return (
        highest_max,
        total_one * factor_one + total_two * factor_two,
        out_one * factor_one[..., None] + out_two * factor_two[..., None],
    )


def gather_rows(rows, axis_name, parts):
    spread = jnp.broadcast_to(rows[None], (parts,) + rows.shape)
    return lax.all_to_all(spread, axis_name, 0, 0, tiled=True)


def shards(
    tokens,
    gains,
    qkv_weight,
    out_weight,
    gate_up_weight,
    down_weight,
    variate_bias,
    page_cache,
    page_variates,
    token_variates,
    cache_len,
    page_table,
    parents,
    accepted,
):
    scale = 1.0 / math.sqrt(HD)
    local_req, tree = parents.shape
    pool, page = page_variates.shape
    requests = cache_len.shape[0]
    qdl = qkv_weight.shape[2]
    head_local = qdl // HD
    head_slot = lax.axis_index("head")
    req_slot = lax.axis_index("req")
    bias_local = lax.dynamic_slice_in_dim(variate_bias, head_slot * head_local, head_local, 1)
    same_bias = bias_local[0]
    other_bias = bias_local[1]
    head_parts = lax.axis_size("head")
    group_tokens = gather_rows(tokens, "head", head_parts).reshape(-1, tokens.shape[1])
    normed = rms_scaled(group_tokens, gains[0]).astype(jnp.bfloat16)
    projected = jnp.einsum(
        "td,cdq->ctq",
        normed,
        qkv_weight,
        preferred_element_type=jnp.float32,
    ).astype(jnp.bfloat16)
    query = projected[0]
    key_new = projected[1]
    value_new = projected[2]
    all_queries = gather_rows(query, "req", requests // local_req)
    global_ids = req_slot * pool + jnp.arange(pool, dtype=jnp.int32)
    matching = (page_table[:, :, None] == global_ids[None, None, :]).astype(jnp.int32)
    owner = jnp.sum(matching * jnp.arange(requests, dtype=jnp.int32)[:, None, None], axis=(0, 1))
    page_order = jnp.sum(
        matching * jnp.arange(page_table.shape[1], dtype=jnp.int32)[None, :, None], axis=(0, 1)
    )
    owner_len = jnp.sum(matching * cache_len[:, None, None], axis=(0, 1))
    in_use = jnp.sum(matching, axis=(0, 1))
    filled = jnp.clip(owner_len - page_order * page, 0, page) * in_use
    valid = jnp.arange(page, dtype=jnp.int32)[None, :] < filled[:, None]
    page_queries = jnp.take(all_queries.reshape(requests, tree, head_local, HD), owner, axis=0)
    query_variates = jnp.take(token_variates.reshape(requests, tree), owner, axis=0)
    cache_keys = page_cache[0].reshape(pool, page, head_local, HD)
    cache_values = page_cache[1].reshape(pool, page, head_local, HD)
    scores = (
        jnp.einsum("pthd,pkhd->pthk", page_queries, cache_keys, preferred_element_type=jnp.float32)
        * scale
    )
    same_page = query_variates[:, :, None] == page_variates[:, None, :]
    scores = scores + jnp.where(
        same_page[:, :, None, :], same_bias[None, None, :, None], other_bias[None, None, :, None]
    )
    keep = valid[:, None, None, :]
    page_max = jnp.max(jnp.where(keep, scores, masked_score), axis=-1)
    weights = jnp.where(keep, jnp.exp(scores - page_max[..., None]), 0.0).astype(jnp.bfloat16)
    page_total = jnp.sum(weights, axis=-1, dtype=jnp.float32)
    page_out = jnp.einsum(
        "pthk,pkhd->pthd", weights, cache_values, preferred_element_type=jnp.float32
    )
    member = (owner[None, :] == jnp.arange(requests, dtype=jnp.int32)[:, None]) & (
        in_use[None, :] > 0
    )
    request_max = jnp.max(jnp.where(member[:, :, None, None], page_max[None], masked_score), axis=1)
    owner_max = jnp.take(request_max, owner, axis=0)
    factor = jnp.where(in_use[:, None, None] > 0, jnp.exp(page_max - owner_max), 0.0)
    member_float = member.astype(jnp.float32)
    request_total = jnp.dot(
        member_float, (page_total * factor).reshape(pool, -1), precision=highest
    ).reshape(requests, tree, head_local)
    request_out = jnp.dot(
        member_float, (page_out * factor[..., None]).reshape(pool, -1), precision=highest
    ).reshape(requests, tree, head_local, HD)
    out_width = tree * head_local * HD
    stat_width = tree * head_local
    packed = jnp.concatenate(
        [
            request_out.reshape(requests, out_width),
            request_total.reshape(requests, stat_width),
            request_max.reshape(requests, stat_width),
        ],
        axis=-1,
    )
    received = lax.all_to_all(packed, "req", split_axis=0, concat_axis=0, tiled=True)
    sources = lax.axis_size("req")
    received = received.reshape(sources, local_req, -1)
    source_out = received[..., :out_width].reshape(sources, local_req, tree, head_local, HD)
    source_total = received[..., out_width : out_width + stat_width].reshape(
        sources, local_req, tree, head_local
    )
    source_max = received[..., out_width + stat_width :].reshape(
        sources, local_req, tree, head_local
    )
    largest = jnp.max(source_max, axis=0)
    source_factor = jnp.exp(source_max - largest[None])
    cached_part = (
        largest,
        jnp.sum(source_total * source_factor, axis=0),
        jnp.sum(source_out * source_factor[..., None], axis=0),
    )
    tree_query = query.reshape(local_req, tree, head_local, HD)
    tree_key = key_new.reshape(local_req, tree, head_local, HD)
    tree_value = value_new.reshape(local_req, tree, head_local, HD)
    nodes = jnp.arange(tree, dtype=jnp.int32)
    reach = (parents[:, :, None] == nodes[None, None, :]).astype(jnp.float32) + jnp.eye(
        tree, dtype=jnp.float32
    )[None]
    for step in range(LEVELS.bit_length()):
        reach = jnp.minimum(jnp.einsum("rij,rjk->rik", reach, reach, precision=highest), 1.0)
    allowed = reach > 0.5
    group_variates = lax.dynamic_slice_in_dim(
        token_variates, req_slot * local_req * tree, local_req * tree, 0
    ).reshape(local_req, tree)
    tree_scores = (
        jnp.einsum("rihd,rjhd->rihj", tree_query, tree_key, preferred_element_type=jnp.float32)
        * scale
    )
    same_tree = group_variates[:, :, None] == group_variates[:, None, :]
    tree_scores = tree_scores + jnp.where(
        same_tree[:, :, None, :], same_bias[None, None, :, None], other_bias[None, None, :, None]
    )
    keep_tree = allowed[:, :, None, :]
    tree_max = jnp.max(jnp.where(keep_tree, tree_scores, masked_score), axis=-1)
    tree_weights = jnp.where(keep_tree, jnp.exp(tree_scores - tree_max[..., None]), 0.0).astype(
        jnp.bfloat16
    )
    tree_total = jnp.sum(tree_weights, axis=-1, dtype=jnp.float32)
    tree_out = jnp.einsum(
        "rihj,rjhd->rihd", tree_weights, tree_value, preferred_element_type=jnp.float32
    )
    final_max, final_total, final_out = merge_parts(cached_part, (tree_max, tree_total, tree_out))
    attended = (
        (final_out / final_total[..., None]).astype(jnp.bfloat16).reshape(local_req * tree, qdl)
    )
    group_rows = local_req * tree
    token_heads = (
        gather_rows(attended, "head", head_parts).transpose(1, 0, 2).reshape(group_rows, -1)
    )
    attention_rows = jnp.dot(token_heads, out_weight, preferred_element_type=jnp.float32)
    hidden_state = (group_tokens.astype(jnp.float32) + attention_rows).astype(jnp.bfloat16)
    normed_two = rms_scaled(hidden_state, gains[1]).astype(jnp.bfloat16)
    both_parts = jnp.einsum(
        "td,cdf->ctf",
        normed_two,
        gate_up_weight,
        preferred_element_type=jnp.float32,
    )
    activated = (jax.nn.silu(both_parts[0]) * both_parts[1]).astype(jnp.bfloat16)
    down_part = jnp.dot(activated, down_weight, preferred_element_type=jnp.float32).astype(
        jnp.bfloat16
    )
    own_rows = tokens.shape[0]
    down_parts = lax.all_to_all(
        down_part.reshape(head_parts, own_rows, -1), "head", 0, 0, tiled=True
    )
    ffn_rows = jnp.sum(down_parts.astype(jnp.float32), axis=0)
    own_hidden = lax.dynamic_slice_in_dim(hidden_state, head_slot * own_rows, own_rows, 0)
    mixed = (own_hidden.astype(jnp.float32) + ffn_rows).astype(jnp.bfloat16)
    chosen = (accepted[:, :, None] == nodes[None, None, :]).astype(jnp.bfloat16)
    stacked = jnp.stack([key_new, value_new]).reshape(2, local_req, tree, qdl)
    new_kv = jnp.einsum(
        "rat,crtq->craq", chosen, stacked, preferred_element_type=jnp.float32
    ).astype(jnp.bfloat16)
    return (mixed, attended, new_kv)


def solution(mesh):
    return jax.shard_map(
        shards,
        mesh=mesh,
        in_specs=(
            P(("req", "head"), None),
            P(),
            P(None, None, "head"),
            P(),
            P(None, None, "head"),
            P("head", None),
            P(),
            P(None, "req", None, "head"),
            P("req", None),
            P(),
            P(),
            P(),
            P("req", None),
            P("req", None),
        ),
        out_specs=(P(("req", "head"), None), P("req", "head"), P(None, "req", None, "head")),
        check_vma=False,
    )
```

```python
import math

import jax
import jax.numpy as jnp
from jax import lax
from jax.sharding import PartitionSpec as P

HD = 64
LEVELS = 8


epsilon = 1e-06
masked_score = -1e30
highest = lax.Precision.HIGHEST


def rms_scaled(rows, gain):
    values = rows.astype(jnp.float32)
    return values * lax.rsqrt(jnp.mean(values * values, axis=-1, keepdims=True) + epsilon) * gain


def merge_parts(first, second):
    max_one, total_one, out_one = first
    max_two, total_two, out_two = second
    highest_max = jnp.maximum(max_one, max_two)
    factor_one = jnp.exp(max_one - highest_max)
    factor_two = jnp.exp(max_two - highest_max)
    return (
        highest_max,
        total_one * factor_one + total_two * factor_two,
        out_one * factor_one[..., None] + out_two * factor_two[..., None],
    )


def gather_rows(rows, axis_name, parts):
    spread = jnp.broadcast_to(rows[None], (parts,) + rows.shape)
    return lax.all_to_all(spread, axis_name, 0, 0, tiled=True)


def shards(
    tokens,
    gains,
    qkv_weight,
    out_weight,
    gate_up_weight,
    down_weight,
    variate_bias,
    page_cache,
    page_variates,
    token_variates,
    cache_len,
    page_table,
    parents,
    accepted,
):
    scale = 1.0 / math.sqrt(HD)
    local_req, tree = parents.shape
    pool, page = page_variates.shape
    requests = cache_len.shape[0]
    qdl = qkv_weight.shape[2]
    head_local = qdl // HD
    head_slot = lax.axis_index("head")
    req_slot = lax.axis_index("req")
    bias_local = lax.dynamic_slice_in_dim(variate_bias, head_slot * head_local, head_local, 1)
    same_bias = bias_local[0]
    other_bias = bias_local[1]
    head_parts = lax.axis_size("head")
    group_tokens = gather_rows(tokens, "head", head_parts).reshape(-1, tokens.shape[1])
    normed = rms_scaled(group_tokens, gains[0]).astype(jnp.bfloat16)
    projected = jnp.einsum(
        "td,cdq->ctq",
        normed,
        qkv_weight,
        preferred_element_type=jnp.float32,
    ).astype(jnp.bfloat16)
    query = projected[0]
    key_new = projected[1]
    value_new = projected[2]
    all_queries = gather_rows(query, "req", requests // local_req)
    global_ids = req_slot * pool + jnp.arange(pool, dtype=jnp.int32)
    matching = (page_table[:, :, None] == global_ids[None, None, :]).astype(jnp.int32)
    owner = jnp.sum(matching * jnp.arange(requests, dtype=jnp.int32)[:, None, None], axis=(0, 1))
    page_order = jnp.sum(
        matching * jnp.arange(page_table.shape[1], dtype=jnp.int32)[None, :, None], axis=(0, 1)
    )
    owner_len = jnp.sum(matching * cache_len[:, None, None], axis=(0, 1))
    in_use = jnp.sum(matching, axis=(0, 1))
    filled = jnp.clip(owner_len - page_order * page, 0, page) * in_use
    valid = jnp.arange(page, dtype=jnp.int32)[None, :] < filled[:, None]
    head_of_column = jnp.arange(qdl, dtype=jnp.int32) // HD
    head_mask = jnp.arange(head_local, dtype=jnp.int32)[:, None] == head_of_column[None, :]
    split_rows = head_local * tree
    page_queries = jnp.take(all_queries.reshape(requests, tree, qdl), owner, axis=0)
    split_queries = jnp.where(
        head_mask[None, :, None, :], page_queries[:, None], jnp.zeros((), page_queries.dtype)
    ).reshape(pool, split_rows, qdl)
    query_variates = jnp.take(token_variates.reshape(requests, tree), owner, axis=0)
    scores = (
        jnp.einsum(
            "prd,pkd->prk", split_queries, page_cache[0], preferred_element_type=jnp.float32
        )
        * scale
    )
    same_page = query_variates[:, :, None] == page_variates[:, None, :]
    page_bias = jnp.where(
        same_page[:, None], same_bias[None, :, None, None], other_bias[None, :, None, None]
    ).reshape(pool, split_rows, page)
    scores = scores + page_bias
    keep = valid[:, None, :]
    page_max = jnp.max(jnp.where(keep, scores, masked_score), axis=-1)
    weights = jnp.where(keep, jnp.exp(scores - page_max[..., None]), 0.0).astype(jnp.bfloat16)
    page_total = jnp.sum(weights, axis=-1, dtype=jnp.float32)
    crossed_out = jnp.einsum(
        "prk,pkc->prc", weights, page_cache[1], preferred_element_type=jnp.float32
    ).reshape(pool, head_local, tree, qdl)
    member = (owner[None, :] == jnp.arange(requests, dtype=jnp.int32)[:, None]) & (
        in_use[None, :] > 0
    )
    request_max = jnp.max(jnp.where(member[:, :, None], page_max[None], masked_score), axis=1)
    owner_max = jnp.take(request_max, owner, axis=0)
    factor = jnp.where(in_use[:, None] > 0, jnp.exp(page_max - owner_max), 0.0)
    member_float = member.astype(jnp.float32)
    request_total = jnp.dot(member_float, page_total * factor, precision=highest)
    scaled_out = jnp.sum(
        jnp.where(
            head_mask[None, :, None, :],
            crossed_out * factor.reshape(pool, head_local, tree)[..., None],
            0.0,
        ),
        axis=1,
    )
    request_out = jnp.dot(member_float, scaled_out.reshape(pool, -1), precision=highest)
    out_width = tree * qdl
    stat_width = tree * head_local
    packed = jnp.concatenate([request_out, request_total, request_max], axis=-1)
    received = lax.all_to_all(packed, "req", split_axis=0, concat_axis=0, tiled=True)
    sources = lax.axis_size("req")
    received = received.reshape(sources, local_req, -1)
    source_out = received[..., :out_width]
    source_total = received[..., out_width : out_width + stat_width].reshape(
        sources, local_req, head_local, tree
    )
    source_max = received[..., out_width + stat_width :].reshape(
        sources, local_req, head_local, tree
    )
    largest = jnp.max(source_max, axis=0)
    source_factor = jnp.exp(source_max - largest[None])
    spread_factor = jnp.broadcast_to(
        source_factor.transpose(0, 1, 3, 2)[..., None], (sources, local_req, tree, head_local, HD)
    ).reshape(sources, local_req, out_width)
    cached_part = (
        largest.transpose(0, 2, 1),
        jnp.sum(source_total * source_factor, axis=0).transpose(0, 2, 1),
        jnp.sum(source_out * spread_factor, axis=0).reshape(local_req, tree, head_local, HD),
    )
    tree_query = query.reshape(local_req, tree, head_local, HD)
    tree_key = key_new.reshape(local_req, tree, head_local, HD)
    tree_value = value_new.reshape(local_req, tree, head_local, HD)
    nodes = jnp.arange(tree, dtype=jnp.int32)
    reach = (parents[:, :, None] == nodes[None, None, :]).astype(jnp.float32) + jnp.eye(
        tree, dtype=jnp.float32
    )[None]
    for step in range(LEVELS.bit_length()):
        reach = jnp.minimum(jnp.einsum("rij,rjk->rik", reach, reach, precision=highest), 1.0)
    allowed = reach > 0.5
    group_variates = lax.dynamic_slice_in_dim(
        token_variates, req_slot * local_req * tree, local_req * tree, 0
    ).reshape(local_req, tree)
    tree_scores = (
        jnp.einsum("rihd,rjhd->rihj", tree_query, tree_key, preferred_element_type=jnp.float32)
        * scale
    )
    same_tree = group_variates[:, :, None] == group_variates[:, None, :]
    tree_scores = tree_scores + jnp.where(
        same_tree[:, :, None, :], same_bias[None, None, :, None], other_bias[None, None, :, None]
    )
    keep_tree = allowed[:, :, None, :]
    tree_max = jnp.max(jnp.where(keep_tree, tree_scores, masked_score), axis=-1)
    tree_weights = jnp.where(keep_tree, jnp.exp(tree_scores - tree_max[..., None]), 0.0).astype(
        jnp.bfloat16
    )
    tree_total = jnp.sum(tree_weights, axis=-1, dtype=jnp.float32)
    tree_out = jnp.einsum(
        "rihj,rjhd->rihd", tree_weights, tree_value, preferred_element_type=jnp.float32
    )
    final_max, final_total, final_out = merge_parts(cached_part, (tree_max, tree_total, tree_out))
    attended = (
        (final_out / final_total[..., None]).astype(jnp.bfloat16).reshape(local_req * tree, qdl)
    )
    group_rows = local_req * tree
    token_heads = (
        gather_rows(attended, "head", head_parts).transpose(1, 0, 2).reshape(group_rows, -1)
    )
    attention_rows = jnp.dot(token_heads, out_weight, preferred_element_type=jnp.float32)
    hidden_state = (group_tokens.astype(jnp.float32) + attention_rows).astype(jnp.bfloat16)
    normed_two = rms_scaled(hidden_state, gains[1]).astype(jnp.bfloat16)
    both_parts = jnp.einsum(
        "td,cdf->ctf",
        normed_two,
        gate_up_weight,
        preferred_element_type=jnp.float32,
    )
    activated = (jax.nn.silu(both_parts[0]) * both_parts[1]).astype(jnp.bfloat16)
    down_part = jnp.dot(activated, down_weight, preferred_element_type=jnp.float32).astype(
        jnp.bfloat16
    )
    own_rows = tokens.shape[0]
    down_parts = lax.all_to_all(
        down_part.reshape(head_parts, own_rows, -1), "head", 0, 0, tiled=True
    )
    ffn_rows = jnp.sum(down_parts.astype(jnp.float32), axis=0)
    own_hidden = lax.dynamic_slice_in_dim(hidden_state, head_slot * own_rows, own_rows, 0)
    mixed = (own_hidden.astype(jnp.float32) + ffn_rows).astype(jnp.bfloat16)
    chosen = (accepted[:, :, None] == nodes[None, None, :]).astype(jnp.bfloat16)
    stacked = jnp.stack([key_new, value_new]).reshape(2, local_req, tree, qdl)
    new_kv = jnp.einsum(
        "rat,crtq->craq", chosen, stacked, preferred_element_type=jnp.float32
    ).astype(jnp.bfloat16)
    return (mixed, attended, new_kv)


def solution(mesh):
    return jax.shard_map(
        shards,
        mesh=mesh,
        in_specs=(
            P(("req", "head"), None),
            P(),
            P(None, None, "head"),
            P(),
            P(None, None, "head"),
            P("head", None),
            P(),
            P(None, "req", None, "head"),
            P("req", None),
            P(),
            P(),
            P(),
            P("req", None),
            P("req", None),
        ),
        out_specs=(P(("req", "head"), None), P("req", "head"), P(None, "req", None, "head")),
        check_vma=False,
    )
```

```python
import math

import jax
import jax.numpy as jnp
from jax import lax
from jax.sharding import PartitionSpec as P

HD = 64
LEVELS = 8


epsilon = 1e-06
masked_score = -1e30
highest = lax.Precision.HIGHEST


def rms_scaled(rows, gain):
    values = rows.astype(jnp.float32)
    return values * lax.rsqrt(jnp.mean(values * values, axis=-1, keepdims=True) + epsilon) * gain


def merge_parts(first, second):
    max_one, total_one, out_one = first
    max_two, total_two, out_two = second
    highest_max = jnp.maximum(max_one, max_two)
    factor_one = jnp.exp(max_one - highest_max)
    factor_two = jnp.exp(max_two - highest_max)
    return (
        highest_max,
        total_one * factor_one + total_two * factor_two,
        out_one * factor_one[..., None] + out_two * factor_two[..., None],
    )


def split_three(values):
    high = lax.reduce_precision(values, exponent_bits=8, mantissa_bits=7)
    rest = values - high
    middle = lax.reduce_precision(rest, exponent_bits=8, mantissa_bits=7)
    low = rest - middle
    return [part.astype(jnp.bfloat16) for part in (high, middle, low)]


def join_three(high, middle, low):
    return (high.astype(jnp.float32) + middle.astype(jnp.float32)) + low.astype(jnp.float32)


def gather_rows(rows, axis_name, parts):
    spread = jnp.broadcast_to(rows[None], (parts,) + rows.shape)
    return lax.all_to_all(spread, axis_name, 0, 0, tiled=True)


def shards(
    tokens,
    gains,
    qkv_weight,
    out_weight,
    gate_up_weight,
    down_weight,
    variate_bias,
    page_cache,
    page_variates,
    token_variates,
    cache_len,
    page_table,
    parents,
    accepted,
):
    scale = 1.0 / math.sqrt(HD)
    local_req, tree = parents.shape
    pool, page = page_variates.shape
    requests = cache_len.shape[0]
    qdl = qkv_weight.shape[2]
    head_local = qdl // HD
    head_slot = lax.axis_index("head")
    req_slot = lax.axis_index("req")
    bias_local = lax.dynamic_slice_in_dim(variate_bias, head_slot * head_local, head_local, 1)
    same_bias = bias_local[0]
    other_bias = bias_local[1]
    head_parts = lax.axis_size("head")
    group_tokens = gather_rows(tokens, "head", head_parts).reshape(-1, tokens.shape[1])
    normed = rms_scaled(group_tokens, gains[0]).astype(jnp.bfloat16)
    projected = jnp.einsum(
        "td,cdq->ctq",
        normed,
        qkv_weight,
        preferred_element_type=jnp.float32,
    ).astype(jnp.bfloat16)
    query = projected[0]
    key_new = projected[1]
    value_new = projected[2]
    all_queries = gather_rows(query, "req", requests // local_req)
    global_ids = req_slot * pool + jnp.arange(pool, dtype=jnp.int32)
    matching = (page_table[:, :, None] == global_ids[None, None, :]).astype(jnp.int32)
    owner = jnp.sum(matching * jnp.arange(requests, dtype=jnp.int32)[:, None, None], axis=(0, 1))
    page_order = jnp.sum(
        matching * jnp.arange(page_table.shape[1], dtype=jnp.int32)[None, :, None], axis=(0, 1)
    )
    owner_len = jnp.sum(matching * cache_len[:, None, None], axis=(0, 1))
    in_use = jnp.sum(matching, axis=(0, 1))
    filled = jnp.clip(owner_len - page_order * page, 0, page) * in_use
    valid = jnp.arange(page, dtype=jnp.int32)[None, :] < filled[:, None]
    head_of_column = jnp.arange(qdl, dtype=jnp.int32) // HD
    head_mask = jnp.arange(head_local, dtype=jnp.int32)[:, None] == head_of_column[None, :]
    split_rows = head_local * tree
    page_queries = jnp.take(all_queries.reshape(requests, tree, qdl), owner, axis=0)
    split_queries = jnp.where(
        head_mask[None, :, None, :], page_queries[:, None], jnp.zeros((), page_queries.dtype)
    ).reshape(pool, split_rows, qdl)
    query_variates = jnp.take(token_variates.reshape(requests, tree), owner, axis=0)
    scores = (
        jnp.einsum(
            "prd,pkd->prk", split_queries, page_cache[0], preferred_element_type=jnp.float32
        )
        * scale
    )
    same_page = query_variates[:, :, None] == page_variates[:, None, :]
    page_bias = jnp.where(
        same_page[:, None], same_bias[None, :, None, None], other_bias[None, :, None, None]
    ).reshape(pool, split_rows, page)
    scores = scores + page_bias
    keep = valid[:, None, :]
    page_max = jnp.max(jnp.where(keep, scores, masked_score), axis=-1)
    weights = jnp.where(keep, jnp.exp(scores - page_max[..., None]), 0.0).astype(jnp.bfloat16)
    page_total = jnp.sum(weights, axis=-1, dtype=jnp.float32)
    crossed_out = jnp.einsum(
        "prk,pkc->prc", weights, page_cache[1], preferred_element_type=jnp.float32
    ).reshape(pool, head_local, tree, qdl)
    member = (owner[None, :] == jnp.arange(requests, dtype=jnp.int32)[:, None]) & (
        in_use[None, :] > 0
    )
    request_max = jnp.max(jnp.where(member[:, :, None], page_max[None], masked_score), axis=1)
    owner_max = jnp.take(request_max, owner, axis=0)
    factor = jnp.where(in_use[:, None] > 0, jnp.exp(page_max - owner_max), 0.0)
    member_float = member.astype(jnp.float32)
    request_total = jnp.dot(member_float, page_total * factor, precision=highest)
    scaled_out = jnp.sum(
        jnp.where(
            head_mask[None, :, None, :],
            crossed_out * factor.reshape(pool, head_local, tree)[..., None],
            0.0,
        ),
        axis=1,
    )
    request_out = jnp.dot(member_float, scaled_out.reshape(pool, -1), precision=highest)
    out_width = tree * qdl
    stat_width = tree * head_local
    stats = jnp.concatenate([request_total, request_max], axis=-1)
    packed = jnp.concatenate([request_out.astype(jnp.bfloat16)] + split_three(stats), axis=-1)
    received = lax.all_to_all(packed, "req", split_axis=0, concat_axis=0, tiled=True)
    sources = lax.axis_size("req")
    received = received.reshape(sources, local_req, -1)
    source_out = received[..., :out_width].astype(jnp.float32).reshape(
        sources, local_req, tree, qdl
    )
    both_width = 2 * stat_width
    got_stats = join_three(
        *[
            received[..., out_width + part * both_width : out_width + (part + 1) * both_width]
            for part in range(3)
        ]
    )
    source_total = got_stats[..., :stat_width].reshape(sources, local_req, head_local, tree)
    source_max = got_stats[..., stat_width:].reshape(sources, local_req, head_local, tree)
    largest = jnp.max(source_max, axis=0)
    source_factor = jnp.exp(source_max - largest[None])
    column_factor = jnp.sum(
        jnp.where(head_mask[None, None, :, None, :], source_factor[..., None], 0.0), axis=2
    )
    cached_part = (
        largest.transpose(0, 2, 1),
        jnp.sum(source_total * source_factor, axis=0).transpose(0, 2, 1),
        jnp.sum(source_out * column_factor, axis=0).reshape(local_req, tree, head_local, HD),
    )
    tree_query = query.reshape(local_req, tree, head_local, HD)
    tree_key = key_new.reshape(local_req, tree, head_local, HD)
    tree_value = value_new.reshape(local_req, tree, head_local, HD)
    nodes = jnp.arange(tree, dtype=jnp.int32)
    reach = (parents[:, :, None] == nodes[None, None, :]).astype(jnp.float32) + jnp.eye(
        tree, dtype=jnp.float32
    )[None]
    for step in range(LEVELS.bit_length()):
        reach = jnp.minimum(jnp.einsum("rij,rjk->rik", reach, reach, precision=highest), 1.0)
    allowed = reach > 0.5
    group_variates = lax.dynamic_slice_in_dim(
        token_variates, req_slot * local_req * tree, local_req * tree, 0
    ).reshape(local_req, tree)
    tree_scores = (
        jnp.einsum("rihd,rjhd->rihj", tree_query, tree_key, preferred_element_type=jnp.float32)
        * scale
    )
    same_tree = group_variates[:, :, None] == group_variates[:, None, :]
    tree_scores = tree_scores + jnp.where(
        same_tree[:, :, None, :], same_bias[None, None, :, None], other_bias[None, None, :, None]
    )
    keep_tree = allowed[:, :, None, :]
    tree_max = jnp.max(jnp.where(keep_tree, tree_scores, masked_score), axis=-1)
    tree_weights = jnp.where(keep_tree, jnp.exp(tree_scores - tree_max[..., None]), 0.0).astype(
        jnp.bfloat16
    )
    tree_total = jnp.sum(tree_weights, axis=-1, dtype=jnp.float32)
    tree_out = jnp.einsum(
        "rihj,rjhd->rihd", tree_weights, tree_value, preferred_element_type=jnp.float32
    )
    final_max, final_total, final_out = merge_parts(cached_part, (tree_max, tree_total, tree_out))
    attended = (
        (final_out / final_total[..., None]).astype(jnp.bfloat16).reshape(local_req * tree, qdl)
    )
    group_rows = local_req * tree
    token_heads = (
        gather_rows(attended, "head", head_parts).transpose(1, 0, 2).reshape(group_rows, -1)
    )
    attention_rows = jnp.dot(token_heads, out_weight, preferred_element_type=jnp.float32)
    hidden_state = (group_tokens.astype(jnp.float32) + attention_rows).astype(jnp.bfloat16)
    normed_two = rms_scaled(hidden_state, gains[1]).astype(jnp.bfloat16)
    both_parts = jnp.einsum(
        "td,cdf->ctf",
        normed_two,
        gate_up_weight,
        preferred_element_type=jnp.float32,
    )
    activated = (jax.nn.silu(both_parts[0]) * both_parts[1]).astype(jnp.bfloat16)
    down_part = jnp.dot(activated, down_weight, preferred_element_type=jnp.float32).astype(
        jnp.bfloat16
    )
    own_rows = tokens.shape[0]
    down_parts = lax.all_to_all(
        down_part.reshape(head_parts, own_rows, -1), "head", 0, 0, tiled=True
    )
    ffn_rows = jnp.sum(down_parts.astype(jnp.float32), axis=0)
    own_hidden = lax.dynamic_slice_in_dim(hidden_state, head_slot * own_rows, own_rows, 0)
    mixed = (own_hidden.astype(jnp.float32) + ffn_rows).astype(jnp.bfloat16)
    chosen = (accepted[:, :, None] == nodes[None, None, :]).astype(jnp.bfloat16)
    stacked = jnp.stack([key_new, value_new]).reshape(2, local_req, tree, qdl)
    new_kv = jnp.einsum(
        "rat,crtq->craq", chosen, stacked, preferred_element_type=jnp.float32
    ).astype(jnp.bfloat16)
    return (mixed, attended, new_kv)


def solution(mesh):
    return jax.shard_map(
        shards,
        mesh=mesh,
        in_specs=(
            P(("req", "head"), None),
            P(),
            P(None, None, "head"),
            P(),
            P(None, None, "head"),
            P("head", None),
            P(),
            P(None, "req", None, "head"),
            P("req", None),
            P(),
            P(),
            P(),
            P("req", None),
            P("req", None),
        ),
        out_specs=(P(("req", "head"), None), P("req", "head"), P(None, "req", None, "head")),
        check_vma=False,
    )
```

```python
import math

import jax
import jax.numpy as jnp
from jax import lax
from jax.sharding import PartitionSpec as P

HD = 64
LEVELS = 8


epsilon = 1e-06
masked_score = -1e30
highest = lax.Precision.HIGHEST


def rms_scaled(rows, gain):
    values = rows.astype(jnp.float32)
    return values * lax.rsqrt(jnp.mean(values * values, axis=-1, keepdims=True) + epsilon) * gain


def merge_parts(first, second):
    max_one, total_one, out_one = first
    max_two, total_two, out_two = second
    highest_max = jnp.maximum(max_one, max_two)
    factor_one = jnp.exp(max_one - highest_max)
    factor_two = jnp.exp(max_two - highest_max)
    return (
        highest_max,
        total_one * factor_one + total_two * factor_two,
        out_one * factor_one[..., None] + out_two * factor_two[..., None],
    )


def split_three(values):
    high = lax.reduce_precision(values, exponent_bits=8, mantissa_bits=7)
    rest = values - high
    middle = lax.reduce_precision(rest, exponent_bits=8, mantissa_bits=7)
    low = rest - middle
    return [part.astype(jnp.bfloat16) for part in (high, middle, low)]


def join_three(high, middle, low):
    return (high.astype(jnp.float32) + middle.astype(jnp.float32)) + low.astype(jnp.float32)


def gather_rows(rows, axis_name, parts):
    spread = jnp.broadcast_to(rows[None], (parts,) + rows.shape)
    return lax.all_to_all(spread, axis_name, 0, 0, tiled=True)


def shards(
    tokens,
    gains,
    qkv_weight,
    out_weight,
    gate_up_weight,
    down_weight,
    variate_bias,
    page_cache,
    page_variates,
    token_variates,
    cache_len,
    page_table,
    parents,
    accepted,
):
    scale = 1.0 / math.sqrt(HD)
    local_req, tree = parents.shape
    pool, page = page_variates.shape
    requests = cache_len.shape[0]
    qdl = qkv_weight.shape[2]
    head_local = qdl // HD
    head_slot = lax.axis_index("head")
    req_slot = lax.axis_index("req")
    bias_local = lax.dynamic_slice_in_dim(variate_bias, head_slot * head_local, head_local, 1)
    same_bias = bias_local[0]
    other_bias = bias_local[1]
    head_parts = lax.axis_size("head")
    group_tokens = gather_rows(tokens, "head", head_parts).reshape(-1, tokens.shape[1])
    normed = rms_scaled(group_tokens, gains[0]).astype(jnp.bfloat16)
    projected = jnp.einsum(
        "td,cdq->ctq",
        normed,
        qkv_weight,
        preferred_element_type=jnp.float32,
    ).astype(jnp.bfloat16)
    query = projected[0]
    key_new = projected[1]
    value_new = projected[2]
    all_queries = gather_rows(query, "req", requests // local_req)
    global_ids = req_slot * pool + jnp.arange(pool, dtype=jnp.int32)
    matching = (page_table[:, :, None] == global_ids[None, None, :]).astype(jnp.int32)
    owner = jnp.sum(matching * jnp.arange(requests, dtype=jnp.int32)[:, None, None], axis=(0, 1))
    page_order = jnp.sum(
        matching * jnp.arange(page_table.shape[1], dtype=jnp.int32)[None, :, None], axis=(0, 1)
    )
    owner_len = jnp.sum(matching * cache_len[:, None, None], axis=(0, 1))
    in_use = jnp.sum(matching, axis=(0, 1))
    filled = jnp.clip(owner_len - page_order * page, 0, page) * in_use
    valid = jnp.arange(page, dtype=jnp.int32)[None, :] < filled[:, None]
    head_of_column = jnp.arange(qdl, dtype=jnp.int32) // HD
    head_mask = jnp.arange(head_local, dtype=jnp.int32)[:, None] == head_of_column[None, :]
    split_rows = head_local * tree
    page_queries = jnp.take(all_queries.reshape(requests, tree, qdl), owner, axis=0)
    split_queries = jnp.where(
        head_mask[None, :, None, :], page_queries[:, None], jnp.zeros((), page_queries.dtype)
    ).reshape(pool, split_rows, qdl)
    query_variates = jnp.take(token_variates.reshape(requests, tree), owner, axis=0)
    scores = (
        jnp.einsum(
            "prd,pkd->prk", split_queries, page_cache[0], preferred_element_type=jnp.float32
        )
        * scale
    )
    same_page = query_variates[:, :, None] == page_variates[:, None, :]
    page_bias = jnp.where(
        same_page[:, None], same_bias[None, :, None, None], other_bias[None, :, None, None]
    ).reshape(pool, split_rows, page)
    scores = scores + page_bias
    keep = valid[:, None, :]
    page_max = jnp.max(jnp.where(keep, scores, masked_score), axis=-1)
    weights = jnp.where(keep, jnp.exp(scores - page_max[..., None]), 0.0).astype(jnp.bfloat16)
    page_total = jnp.sum(weights, axis=-1, dtype=jnp.float32)
    crossed_out = jnp.einsum(
        "prk,pkc->prc", weights, page_cache[1], preferred_element_type=jnp.float32
    ).reshape(pool, head_local, tree, qdl)
    member = (owner[None, :] == jnp.arange(requests, dtype=jnp.int32)[:, None]) & (
        in_use[None, :] > 0
    )
    request_max = jnp.max(jnp.where(member[:, :, None], page_max[None], masked_score), axis=1)
    owner_max = jnp.take(request_max, owner, axis=0)
    factor = jnp.where(in_use[:, None] > 0, jnp.exp(page_max - owner_max), 0.0)
    member_float = member.astype(jnp.float32)
    request_total = jnp.dot(member_float, page_total * factor, precision=highest)
    scaled_out = jnp.sum(
        jnp.where(
            head_mask[None, :, None, :],
            crossed_out * factor.reshape(pool, head_local, tree)[..., None],
            0.0,
        ),
        axis=1,
    )
    request_out = jnp.dot(member_float, scaled_out.reshape(pool, -1), precision=highest)
    stats = jnp.stack([request_total, request_max], axis=1)
    packed = jnp.concatenate(
        [request_out.astype(jnp.bfloat16).reshape(requests, tree, qdl)] + split_three(stats),
        axis=1,
    )
    received = lax.all_to_all(packed, "req", split_axis=0, concat_axis=0, tiled=True)
    sources = lax.axis_size("req")
    received = received.reshape((sources, local_req) + packed.shape[1:])
    source_out = received[:, :, :tree].astype(jnp.float32)
    got_stats = join_three(
        *[received[:, :, tree + 2 * part : tree + 2 * part + 2] for part in range(3)]
    )
    source_total = got_stats[:, :, 0].reshape(sources, local_req, head_local, tree)
    source_max = got_stats[:, :, 1].reshape(sources, local_req, head_local, tree)
    largest = jnp.max(source_max, axis=0)
    source_factor = jnp.exp(source_max - largest[None])
    column_factor = jnp.sum(
        jnp.where(head_mask[None, None, :, None, :], source_factor[..., None], 0.0), axis=2
    )
    cached_part = (
        largest.transpose(0, 2, 1),
        jnp.sum(source_total * source_factor, axis=0).transpose(0, 2, 1),
        jnp.sum(source_out * column_factor, axis=0).reshape(local_req, tree, head_local, HD),
    )
    tree_query = query.reshape(local_req, tree, head_local, HD)
    tree_key = key_new.reshape(local_req, tree, head_local, HD)
    tree_value = value_new.reshape(local_req, tree, head_local, HD)
    nodes = jnp.arange(tree, dtype=jnp.int32)
    reach = (parents[:, :, None] == nodes[None, None, :]).astype(jnp.float32) + jnp.eye(
        tree, dtype=jnp.float32
    )[None]
    for step in range(LEVELS.bit_length()):
        reach = jnp.minimum(jnp.einsum("rij,rjk->rik", reach, reach, precision=highest), 1.0)
    allowed = reach > 0.5
    group_variates = lax.dynamic_slice_in_dim(
        token_variates, req_slot * local_req * tree, local_req * tree, 0
    ).reshape(local_req, tree)
    tree_scores = (
        jnp.einsum("rihd,rjhd->rihj", tree_query, tree_key, preferred_element_type=jnp.float32)
        * scale
    )
    same_tree = group_variates[:, :, None] == group_variates[:, None, :]
    tree_scores = tree_scores + jnp.where(
        same_tree[:, :, None, :], same_bias[None, None, :, None], other_bias[None, None, :, None]
    )
    keep_tree = allowed[:, :, None, :]
    tree_max = jnp.max(jnp.where(keep_tree, tree_scores, masked_score), axis=-1)
    tree_weights = jnp.where(keep_tree, jnp.exp(tree_scores - tree_max[..., None]), 0.0).astype(
        jnp.bfloat16
    )
    tree_total = jnp.sum(tree_weights, axis=-1, dtype=jnp.float32)
    tree_out = jnp.einsum(
        "rihj,rjhd->rihd", tree_weights, tree_value, preferred_element_type=jnp.float32
    )
    final_max, final_total, final_out = merge_parts(cached_part, (tree_max, tree_total, tree_out))
    attended = (
        (final_out / final_total[..., None]).astype(jnp.bfloat16).reshape(local_req * tree, qdl)
    )
    group_rows = local_req * tree
    token_heads = (
        gather_rows(attended, "head", head_parts).transpose(1, 0, 2).reshape(group_rows, -1)
    )
    attention_rows = jnp.dot(token_heads, out_weight, preferred_element_type=jnp.float32)
    hidden_state = (group_tokens.astype(jnp.float32) + attention_rows).astype(jnp.bfloat16)
    normed_two = rms_scaled(hidden_state, gains[1]).astype(jnp.bfloat16)
    both_parts = jnp.einsum(
        "td,cdf->ctf",
        normed_two,
        gate_up_weight,
        preferred_element_type=jnp.float32,
    )
    activated = (jax.nn.silu(both_parts[0]) * both_parts[1]).astype(jnp.bfloat16)
    down_part = jnp.dot(activated, down_weight, preferred_element_type=jnp.float32).astype(
        jnp.bfloat16
    )
    own_rows = tokens.shape[0]
    down_parts = lax.all_to_all(
        down_part.reshape(head_parts, own_rows, -1), "head", 0, 0, tiled=True
    )
    ffn_rows = jnp.sum(down_parts.astype(jnp.float32), axis=0)
    own_hidden = lax.dynamic_slice_in_dim(hidden_state, head_slot * own_rows, own_rows, 0)
    mixed = (own_hidden.astype(jnp.float32) + ffn_rows).astype(jnp.bfloat16)
    chosen = (accepted[:, :, None] == nodes[None, None, :]).astype(jnp.bfloat16)
    stacked = jnp.stack([key_new, value_new]).reshape(2, local_req, tree, qdl)
    new_kv = jnp.einsum(
        "rat,crtq->craq", chosen, stacked, preferred_element_type=jnp.float32
    ).astype(jnp.bfloat16)
    return (mixed, attended, new_kv)


def solution(mesh):
    return jax.shard_map(
        shards,
        mesh=mesh,
        in_specs=(
            P(("req", "head"), None),
            P(),
            P(None, None, "head"),
            P(),
            P(None, None, "head"),
            P("head", None),
            P(),
            P(None, "req", None, "head"),
            P("req", None),
            P(),
            P(),
            P(),
            P("req", None),
            P("req", None),
        ),
        out_specs=(P(("req", "head"), None), P("req", "head"), P(None, "req", None, "head")),
        check_vma=False,
    )
```

```python
import math

import jax
import jax.numpy as jnp
from jax import lax
from jax.sharding import Mesh
from jax.sharding import PartitionSpec as P

HD = 64
REQ = ("req_y", "req_z")
LEVELS = 8


epsilon = 1e-06
masked_score = -1e30
highest = lax.Precision.HIGHEST


def rms_scaled(rows, gain):
    values = rows.astype(jnp.float32)
    return values * lax.rsqrt(jnp.mean(values * values, axis=-1, keepdims=True) + epsilon) * gain


def merge_parts(first, second):
    max_one, total_one, out_one = first
    max_two, total_two, out_two = second
    highest_max = jnp.maximum(max_one, max_two)
    factor_one = jnp.exp(max_one - highest_max)
    factor_two = jnp.exp(max_two - highest_max)
    return (
        highest_max,
        total_one * factor_one + total_two * factor_two,
        out_one * factor_one[..., None] + out_two * factor_two[..., None],
    )


def split_three(values):
    high = lax.reduce_precision(values, exponent_bits=8, mantissa_bits=7)
    rest = values - high
    middle = lax.reduce_precision(rest, exponent_bits=8, mantissa_bits=7)
    low = rest - middle
    return [part.astype(jnp.bfloat16) for part in (high, middle, low)]


def join_three(high, middle, low):
    return (high.astype(jnp.float32) + middle.astype(jnp.float32)) + low.astype(jnp.float32)


def gather_rows(rows, axis_name, parts):
    spread = jnp.broadcast_to(rows[None], (parts,) + rows.shape)
    return lax.all_to_all(spread, axis_name, 0, 0, tiled=True)


def shards(
    tokens,
    gains,
    qkv_weight,
    out_weight,
    gate_up_weight,
    down_weight,
    variate_bias,
    page_cache,
    page_variates,
    token_variates,
    cache_len,
    page_table,
    parents,
    accepted,
):
    scale = 1.0 / math.sqrt(HD)
    local_req, tree = parents.shape
    pool, page = page_variates.shape
    requests = cache_len.shape[0]
    qdl = qkv_weight.shape[2]
    head_local = qdl // HD
    head_slot = lax.axis_index("head")
    req_slot = lax.axis_index(REQ)
    bias_local = lax.dynamic_slice_in_dim(variate_bias, head_slot * head_local, head_local, 1)
    same_bias = bias_local[0]
    other_bias = bias_local[1]
    head_parts = lax.axis_size("head")
    group_tokens = gather_rows(tokens, "head", head_parts).reshape(-1, tokens.shape[1])
    normed = rms_scaled(group_tokens, gains[0]).astype(jnp.bfloat16)
    projected = jnp.einsum(
        "td,cdq->ctq",
        normed,
        qkv_weight,
        preferred_element_type=jnp.float32,
    ).astype(jnp.bfloat16)
    query = projected[0]
    key_new = projected[1]
    value_new = projected[2]
    req_z_parts = lax.axis_size("req_z")
    req_y_parts = lax.axis_size("req_y")
    all_queries = gather_rows(gather_rows(query, "req_z", req_z_parts), "req_y", req_y_parts)
    global_ids = req_slot * pool + jnp.arange(pool, dtype=jnp.int32)
    matching = (page_table[:, :, None] == global_ids[None, None, :]).astype(jnp.int32)
    owner = jnp.sum(matching * jnp.arange(requests, dtype=jnp.int32)[:, None, None], axis=(0, 1))
    page_order = jnp.sum(
        matching * jnp.arange(page_table.shape[1], dtype=jnp.int32)[None, :, None], axis=(0, 1)
    )
    owner_len = jnp.sum(matching * cache_len[:, None, None], axis=(0, 1))
    in_use = jnp.sum(matching, axis=(0, 1))
    filled = jnp.clip(owner_len - page_order * page, 0, page) * in_use
    valid = jnp.arange(page, dtype=jnp.int32)[None, :] < filled[:, None]
    head_of_column = jnp.arange(qdl, dtype=jnp.int32) // HD
    head_mask = jnp.arange(head_local, dtype=jnp.int32)[:, None] == head_of_column[None, :]
    split_rows = head_local * tree
    page_queries = jnp.take(all_queries.reshape(requests, tree, qdl), owner, axis=0)
    split_queries = jnp.where(
        head_mask[None, :, None, :], page_queries[:, None], jnp.zeros((), page_queries.dtype)
    ).reshape(pool, split_rows, qdl)
    query_variates = jnp.take(token_variates.reshape(requests, tree), owner, axis=0)
    scores = (
        jnp.einsum(
            "prd,pkd->prk", split_queries, page_cache[0], preferred_element_type=jnp.float32
        )
        * scale
    )
    same_page = query_variates[:, :, None] == page_variates[:, None, :]
    page_bias = jnp.where(
        same_page[:, None], same_bias[None, :, None, None], other_bias[None, :, None, None]
    ).reshape(pool, split_rows, page)
    scores = scores + page_bias
    keep = valid[:, None, :]
    page_max = jnp.max(jnp.where(keep, scores, masked_score), axis=-1)
    weights = jnp.where(keep, jnp.exp(scores - page_max[..., None]), 0.0).astype(jnp.bfloat16)
    page_total = jnp.sum(weights, axis=-1, dtype=jnp.float32)
    crossed_out = jnp.einsum(
        "prk,pkc->prc", weights, page_cache[1], preferred_element_type=jnp.float32
    ).reshape(pool, head_local, tree, qdl)
    member = (owner[None, :] == jnp.arange(requests, dtype=jnp.int32)[:, None]) & (
        in_use[None, :] > 0
    )
    request_max = jnp.max(jnp.where(member[:, :, None], page_max[None], masked_score), axis=1)
    owner_max = jnp.take(request_max, owner, axis=0)
    factor = jnp.where(in_use[:, None] > 0, jnp.exp(page_max - owner_max), 0.0)
    member_float = member.astype(jnp.float32)
    request_total = jnp.dot(member_float, page_total * factor, precision=highest)
    scaled_out = jnp.sum(
        jnp.where(
            head_mask[None, :, None, :],
            crossed_out * factor.reshape(pool, head_local, tree)[..., None],
            0.0,
        ),
        axis=1,
    )
    request_out = jnp.dot(member_float, scaled_out.reshape(pool, -1), precision=highest)
    stats = jnp.stack([request_total, request_max], axis=1)
    packed = jnp.concatenate(
        [request_out.astype(jnp.bfloat16).reshape(requests, tree, qdl)] + split_three(stats),
        axis=1,
    )
    received = lax.all_to_all(packed, REQ, split_axis=0, concat_axis=0, tiled=True)
    sources = lax.axis_size(REQ)
    received = received.reshape((sources, local_req) + packed.shape[1:])
    source_out = received[:, :, :tree].astype(jnp.float32)
    got_stats = join_three(
        *[received[:, :, tree + 2 * part : tree + 2 * part + 2] for part in range(3)]
    )
    source_total = got_stats[:, :, 0].reshape(sources, local_req, head_local, tree)
    source_max = got_stats[:, :, 1].reshape(sources, local_req, head_local, tree)
    largest = jnp.max(source_max, axis=0)
    source_factor = jnp.exp(source_max - largest[None])
    column_factor = jnp.sum(
        jnp.where(head_mask[None, None, :, None, :], source_factor[..., None], 0.0), axis=2
    )
    cached_part = (
        largest.transpose(0, 2, 1),
        jnp.sum(source_total * source_factor, axis=0).transpose(0, 2, 1),
        jnp.sum(source_out * column_factor, axis=0).reshape(local_req, tree, head_local, HD),
    )
    tree_query = query.reshape(local_req, tree, head_local, HD)
    tree_key = key_new.reshape(local_req, tree, head_local, HD)
    tree_value = value_new.reshape(local_req, tree, head_local, HD)
    nodes = jnp.arange(tree, dtype=jnp.int32)
    reach = (parents[:, :, None] == nodes[None, None, :]).astype(jnp.float32) + jnp.eye(
        tree, dtype=jnp.float32
    )[None]
    for step in range(LEVELS.bit_length()):
        reach = jnp.minimum(jnp.einsum("rij,rjk->rik", reach, reach, precision=highest), 1.0)
    allowed = reach > 0.5
    group_variates = lax.dynamic_slice_in_dim(
        token_variates, req_slot * local_req * tree, local_req * tree, 0
    ).reshape(local_req, tree)
    tree_scores = (
        jnp.einsum("rihd,rjhd->rihj", tree_query, tree_key, preferred_element_type=jnp.float32)
        * scale
    )
    same_tree = group_variates[:, :, None] == group_variates[:, None, :]
    tree_scores = tree_scores + jnp.where(
        same_tree[:, :, None, :], same_bias[None, None, :, None], other_bias[None, None, :, None]
    )
    keep_tree = allowed[:, :, None, :]
    tree_max = jnp.max(jnp.where(keep_tree, tree_scores, masked_score), axis=-1)
    tree_weights = jnp.where(keep_tree, jnp.exp(tree_scores - tree_max[..., None]), 0.0).astype(
        jnp.bfloat16
    )
    tree_total = jnp.sum(tree_weights, axis=-1, dtype=jnp.float32)
    tree_out = jnp.einsum(
        "rihj,rjhd->rihd", tree_weights, tree_value, preferred_element_type=jnp.float32
    )
    final_max, final_total, final_out = merge_parts(cached_part, (tree_max, tree_total, tree_out))
    attended = (
        (final_out / final_total[..., None]).astype(jnp.bfloat16).reshape(local_req * tree, qdl)
    )
    group_rows = local_req * tree
    token_heads = (
        gather_rows(attended, "head", head_parts).transpose(1, 0, 2).reshape(group_rows, -1)
    )
    attention_rows = jnp.dot(token_heads, out_weight, preferred_element_type=jnp.float32)
    hidden_state = (group_tokens.astype(jnp.float32) + attention_rows).astype(jnp.bfloat16)
    normed_two = rms_scaled(hidden_state, gains[1]).astype(jnp.bfloat16)
    both_parts = jnp.einsum(
        "td,cdf->ctf",
        normed_two,
        gate_up_weight,
        preferred_element_type=jnp.float32,
    )
    activated = (jax.nn.silu(both_parts[0]) * both_parts[1]).astype(jnp.bfloat16)
    down_part = jnp.dot(activated, down_weight, preferred_element_type=jnp.float32).astype(
        jnp.bfloat16
    )
    own_rows = tokens.shape[0]
    down_parts = lax.all_to_all(
        down_part.reshape(head_parts, own_rows, -1), "head", 0, 0, tiled=True
    )
    ffn_rows = jnp.sum(down_parts.astype(jnp.float32), axis=0)
    own_hidden = lax.dynamic_slice_in_dim(hidden_state, head_slot * own_rows, own_rows, 0)
    mixed = (own_hidden.astype(jnp.float32) + ffn_rows).astype(jnp.bfloat16)
    chosen = (accepted[:, :, None] == nodes[None, None, :]).astype(jnp.bfloat16)
    stacked = jnp.stack([key_new, value_new]).reshape(2, local_req, tree, qdl)
    new_kv = jnp.einsum(
        "rat,crtq->craq", chosen, stacked, preferred_element_type=jnp.float32
    ).astype(jnp.bfloat16)
    return (mixed, attended, new_kv)


def split_req_mesh(mesh):
    column = mesh.devices[:, 0]
    y_parts = len({device.coords[1] for device in column})
    return Mesh(
        mesh.devices.reshape(y_parts, column.size // y_parts, mesh.devices.shape[1]),
        REQ + ("head",),
    )


def solution(mesh):
    return jax.shard_map(
        shards,
        mesh=split_req_mesh(mesh),
        in_specs=(
            P((REQ + ("head",)), None),
            P(),
            P(None, None, "head"),
            P(),
            P(None, None, "head"),
            P("head", None),
            P(),
            P(None, REQ, None, "head"),
            P(REQ, None),
            P(),
            P(),
            P(),
            P(REQ, None),
            P(REQ, None),
        ),
        out_specs=(P((REQ + ("head",)), None), P(REQ, "head"), P(None, REQ, None, "head")),
        check_vma=False,
    )
```

```python
import functools
import math

import jax
import jax.numpy as jnp
from jax import lax
from jax.experimental import pallas as pl
from jax.experimental.pallas import tpu as pltpu
from jax.sharding import PartitionSpec as P

HD = 64
LEVELS = 8


epsilon = 1e-06
masked_score = -1e30
highest = lax.Precision.HIGHEST


def rms_scaled(rows, gain):
    values = rows.astype(jnp.float32)
    return values * lax.rsqrt(jnp.mean(values * values, axis=-1, keepdims=True) + epsilon) * gain


def merge_parts(first, second):
    max_one, total_one, out_one = first
    max_two, total_two, out_two = second
    highest_max = jnp.maximum(max_one, max_two)
    factor_one = jnp.exp(max_one - highest_max)
    factor_two = jnp.exp(max_two - highest_max)
    return (
        highest_max,
        total_one * factor_one + total_two * factor_two,
        out_one * factor_one[..., None] + out_two * factor_two[..., None],
    )


def page_kernel(owner_ref, filled_ref, q_ref, qv_ref, k_ref, v_ref, pv_ref, bias_ref,
                out_ref, max_ref, total_ref, *, head_local, scale):
    step = pl.program_id(0)

    @pl.when(step == 0)
    def _():
        out_ref[...] = jnp.zeros(out_ref.shape, jnp.float32)
        max_ref[...] = jnp.full(max_ref.shape, masked_score, jnp.float32)
        total_ref[...] = jnp.zeros(total_ref.shape, jnp.float32)

    count = filled_ref[step]

    @pl.when(count > 0)
    def _():
        row = owner_ref[step]
        query = q_ref[row]
        same = qv_ref[row] == pv_ref[...]
        keys = k_ref[...]
        values = v_ref[...]
        valid = lax.broadcasted_iota(jnp.int32, same.shape, 1) < count
        for head in range(head_local):
            cols = slice(head * HD, (head + 1) * HD)
            scores = lax.dot_general(
                query[:, cols], keys[:, cols], (((1,), (1,)), ((), ())),
                preferred_element_type=jnp.float32,
            ) * scale
            scores = scores + jnp.where(same, bias_ref[0, head], bias_ref[1, head])
            block_max = jnp.max(jnp.where(valid, scores, masked_score), axis=1, keepdims=True)
            weights = jnp.where(valid, jnp.exp(scores - block_max), 0.0).astype(jnp.bfloat16)
            block_total = jnp.sum(weights.astype(jnp.float32), axis=1, keepdims=True)
            block_out = jnp.dot(weights, values[:, cols], preferred_element_type=jnp.float32)
            old_max = max_ref[row, :, head : head + 1]
            new_max = jnp.maximum(old_max, block_max)
            keep_old = jnp.exp(old_max - new_max)
            keep_new = jnp.exp(block_max - new_max)
            max_ref[row, :, head : head + 1] = new_max
            total_ref[row, :, head : head + 1] = (
                total_ref[row, :, head : head + 1] * keep_old + block_total * keep_new
            )
            out_ref[row, :, cols] = out_ref[row, :, cols] * keep_old + block_out * keep_new


def page_attention(owner, filled, queries, query_variates, page_cache, page_variates, bias,
                   interpret=False):
    requests, tree, qdl = queries.shape
    pool, page = page_variates.shape
    head_local = qdl // HD
    kernel = functools.partial(page_kernel, head_local=head_local, scale=1.0 / math.sqrt(HD))
    whole3 = lambda shape: pl.BlockSpec(shape, lambda step, *_: (0, 0, 0))
    grid_spec = pltpu.PrefetchScalarGridSpec(
        num_scalar_prefetch=2,
        grid=(pool,),
        in_specs=[
            whole3((requests, tree, qdl)),
            whole3((requests, tree, 1)),
            pl.BlockSpec((None, None, page, qdl), lambda step, *_: (0, step, 0, 0)),
            pl.BlockSpec((None, None, page, qdl), lambda step, *_: (1, step, 0, 0)),
            pl.BlockSpec((None, 1, page), lambda step, *_: (step, 0, 0)),
            pl.BlockSpec(memory_space=pltpu.SMEM),
        ],
        out_specs=[
            whole3((requests, tree, qdl)),
            whole3((requests, tree, head_local)),
            whole3((requests, tree, head_local)),
        ],
    )
    return pl.pallas_call(
        kernel,
        grid_spec=grid_spec,
        out_shape=[
            jax.ShapeDtypeStruct((requests, tree, qdl), jnp.float32),
            jax.ShapeDtypeStruct((requests, tree, head_local), jnp.float32),
            jax.ShapeDtypeStruct((requests, tree, head_local), jnp.float32),
        ],
        compiler_params=pltpu.CompilerParams(dimension_semantics=("arbitrary",)),
        interpret=interpret,
    )(owner, filled, queries, query_variates[..., None], page_cache,
      page_cache, page_variates[:, None, :], bias)


def split_three(values):
    high = lax.reduce_precision(values, exponent_bits=8, mantissa_bits=7)
    rest = values - high
    middle = lax.reduce_precision(rest, exponent_bits=8, mantissa_bits=7)
    low = rest - middle
    return [part.astype(jnp.bfloat16) for part in (high, middle, low)]


def join_three(high, middle, low):
    return (high.astype(jnp.float32) + middle.astype(jnp.float32)) + low.astype(jnp.float32)


def gather_rows(rows, axis_name, parts):
    spread = jnp.broadcast_to(rows[None], (parts,) + rows.shape)
    return lax.all_to_all(spread, axis_name, 0, 0, tiled=True)


def shards(
    tokens,
    gains,
    qkv_weight,
    out_weight,
    gate_up_weight,
    down_weight,
    variate_bias,
    page_cache,
    page_variates,
    token_variates,
    cache_len,
    page_table,
    parents,
    accepted,
):
    scale = 1.0 / math.sqrt(HD)
    local_req, tree = parents.shape
    pool, page = page_variates.shape
    requests = cache_len.shape[0]
    qdl = qkv_weight.shape[2]
    head_local = qdl // HD
    head_slot = lax.axis_index("head")
    req_slot = lax.axis_index("req")
    bias_local = lax.dynamic_slice_in_dim(variate_bias, head_slot * head_local, head_local, 1)
    same_bias = bias_local[0]
    other_bias = bias_local[1]
    head_parts = lax.axis_size("head")
    group_tokens = gather_rows(tokens, "head", head_parts).reshape(-1, tokens.shape[1])
    normed = rms_scaled(group_tokens, gains[0]).astype(jnp.bfloat16)
    projected = jnp.einsum(
        "td,cdq->ctq",
        normed,
        qkv_weight,
        preferred_element_type=jnp.float32,
    ).astype(jnp.bfloat16)
    query = projected[0]
    key_new = projected[1]
    value_new = projected[2]
    all_queries = gather_rows(query, "req", requests // local_req)
    global_ids = req_slot * pool + jnp.arange(pool, dtype=jnp.int32)
    matching = (page_table[:, :, None] == global_ids[None, None, :]).astype(jnp.int32)
    owner = jnp.sum(matching * jnp.arange(requests, dtype=jnp.int32)[:, None, None], axis=(0, 1))
    page_order = jnp.sum(
        matching * jnp.arange(page_table.shape[1], dtype=jnp.int32)[None, :, None], axis=(0, 1)
    )
    owner_len = jnp.sum(matching * cache_len[:, None, None], axis=(0, 1))
    in_use = jnp.sum(matching, axis=(0, 1))
    filled = jnp.clip(owner_len - page_order * page, 0, page) * in_use
    valid = jnp.arange(page, dtype=jnp.int32)[None, :] < filled[:, None]
    head_of_column = jnp.arange(qdl, dtype=jnp.int32) // HD
    head_mask = jnp.arange(head_local, dtype=jnp.int32)[:, None] == head_of_column[None, :]
    request_out, acc_max, acc_total = page_attention(
        jnp.clip(owner, 0, requests - 1),
        filled,
        all_queries.reshape(requests, tree, qdl),
        token_variates.reshape(requests, tree),
        page_cache,
        page_variates,
        bias_local,
    )
    request_max = acc_max.transpose(0, 2, 1).reshape(requests, head_local * tree)
    request_total = acc_total.transpose(0, 2, 1).reshape(requests, head_local * tree)
    stats = jnp.stack([request_total, request_max], axis=1)
    packed = jnp.concatenate(
        [request_out.astype(jnp.bfloat16).reshape(requests, tree, qdl)] + split_three(stats),
        axis=1,
    )
    received = lax.all_to_all(packed, "req", split_axis=0, concat_axis=0, tiled=True)
    sources = lax.axis_size("req")
    received = received.reshape((sources, local_req) + packed.shape[1:])
    source_out = received[:, :, :tree].astype(jnp.float32)
    got_stats = join_three(
        *[received[:, :, tree + 2 * part : tree + 2 * part + 2] for part in range(3)]
    )
    source_total = got_stats[:, :, 0].reshape(sources, local_req, head_local, tree)
    source_max = got_stats[:, :, 1].reshape(sources, local_req, head_local, tree)
    largest = jnp.max(source_max, axis=0)
    source_factor = jnp.exp(source_max - largest[None])
    column_factor = jnp.sum(
        jnp.where(head_mask[None, None, :, None, :], source_factor[..., None], 0.0), axis=2
    )
    cached_part = (
        largest.transpose(0, 2, 1),
        jnp.sum(source_total * source_factor, axis=0).transpose(0, 2, 1),
        jnp.sum(source_out * column_factor, axis=0).reshape(local_req, tree, head_local, HD),
    )
    tree_query = query.reshape(local_req, tree, head_local, HD)
    tree_key = key_new.reshape(local_req, tree, head_local, HD)
    tree_value = value_new.reshape(local_req, tree, head_local, HD)
    nodes = jnp.arange(tree, dtype=jnp.int32)
    reach = (parents[:, :, None] == nodes[None, None, :]).astype(jnp.float32) + jnp.eye(
        tree, dtype=jnp.float32
    )[None]
    for step in range(LEVELS.bit_length()):
        reach = jnp.minimum(jnp.einsum("rij,rjk->rik", reach, reach, precision=highest), 1.0)
    allowed = reach > 0.5
    group_variates = lax.dynamic_slice_in_dim(
        token_variates, req_slot * local_req * tree, local_req * tree, 0
    ).reshape(local_req, tree)
    tree_scores = (
        jnp.einsum("rihd,rjhd->rihj", tree_query, tree_key, preferred_element_type=jnp.float32)
        * scale
    )
    same_tree = group_variates[:, :, None] == group_variates[:, None, :]
    tree_scores = tree_scores + jnp.where(
        same_tree[:, :, None, :], same_bias[None, None, :, None], other_bias[None, None, :, None]
    )
    keep_tree = allowed[:, :, None, :]
    tree_max = jnp.max(jnp.where(keep_tree, tree_scores, masked_score), axis=-1)
    tree_weights = jnp.where(keep_tree, jnp.exp(tree_scores - tree_max[..., None]), 0.0).astype(
        jnp.bfloat16
    )
    tree_total = jnp.sum(tree_weights, axis=-1, dtype=jnp.float32)
    tree_out = jnp.einsum(
        "rihj,rjhd->rihd", tree_weights, tree_value, preferred_element_type=jnp.float32
    )
    final_max, final_total, final_out = merge_parts(cached_part, (tree_max, tree_total, tree_out))
    attended = (
        (final_out / final_total[..., None]).astype(jnp.bfloat16).reshape(local_req * tree, qdl)
    )
    group_rows = local_req * tree
    token_heads = (
        gather_rows(attended, "head", head_parts).transpose(1, 0, 2).reshape(group_rows, -1)
    )
    attention_rows = jnp.dot(token_heads, out_weight, preferred_element_type=jnp.float32)
    hidden_state = (group_tokens.astype(jnp.float32) + attention_rows).astype(jnp.bfloat16)
    normed_two = rms_scaled(hidden_state, gains[1]).astype(jnp.bfloat16)
    both_parts = jnp.einsum(
        "td,cdf->ctf",
        normed_two,
        gate_up_weight,
        preferred_element_type=jnp.float32,
    )
    activated = (jax.nn.silu(both_parts[0]) * both_parts[1]).astype(jnp.bfloat16)
    down_part = jnp.dot(activated, down_weight, preferred_element_type=jnp.float32).astype(
        jnp.bfloat16
    )
    own_rows = tokens.shape[0]
    down_parts = lax.all_to_all(
        down_part.reshape(head_parts, own_rows, -1), "head", 0, 0, tiled=True
    )
    ffn_rows = jnp.sum(down_parts.astype(jnp.float32), axis=0)
    own_hidden = lax.dynamic_slice_in_dim(hidden_state, head_slot * own_rows, own_rows, 0)
    mixed = (own_hidden.astype(jnp.float32) + ffn_rows).astype(jnp.bfloat16)
    chosen = (accepted[:, :, None] == nodes[None, None, :]).astype(jnp.bfloat16)
    stacked = jnp.stack([key_new, value_new]).reshape(2, local_req, tree, qdl)
    new_kv = jnp.einsum(
        "rat,crtq->craq", chosen, stacked, preferred_element_type=jnp.float32
    ).astype(jnp.bfloat16)
    return (mixed, attended, new_kv)


def solution(mesh):
    return jax.shard_map(
        shards,
        mesh=mesh,
        in_specs=(
            P(("req", "head"), None),
            P(),
            P(None, None, "head"),
            P(),
            P(None, None, "head"),
            P("head", None),
            P(),
            P(None, "req", None, "head"),
            P("req", None),
            P(),
            P(),
            P(),
            P("req", None),
            P("req", None),
        ),
        out_specs=(P(("req", "head"), None), P("req", "head"), P(None, "req", None, "head")),
        check_vma=False,
    )
```

```python
import functools
import math

import jax
import jax.numpy as jnp
from jax import lax
from jax.experimental import pallas as pl
from jax.experimental.pallas import tpu as pltpu
from jax.sharding import PartitionSpec as P

HD = 64
LEVELS = 8


epsilon = 1e-06
masked_score = -1e30
highest = lax.Precision.HIGHEST


def rms_scaled(rows, gain):
    values = rows.astype(jnp.float32)
    return values * lax.rsqrt(jnp.mean(values * values, axis=-1, keepdims=True) + epsilon) * gain


def merge_parts(first, second):
    max_one, total_one, out_one = first
    max_two, total_two, out_two = second
    highest_max = jnp.maximum(max_one, max_two)
    factor_one = jnp.exp(max_one - highest_max)
    factor_two = jnp.exp(max_two - highest_max)
    return (
        highest_max,
        total_one * factor_one + total_two * factor_two,
        out_one * factor_one[..., None] + out_two * factor_two[..., None],
    )


def page_kernel(owner_ref, filled_ref, q_ref, qv_ref, cache_ref, pv_ref, bias_ref,
                out_ref, max_ref, total_ref, *, head_local, scale, pool):
    out_ref[...] = jnp.zeros(out_ref.shape, jnp.float32)
    max_ref[...] = jnp.full(max_ref.shape, masked_score, jnp.float32)
    total_ref[...] = jnp.zeros(total_ref.shape, jnp.float32)

    def one_page(step, carry):
        count = filled_ref[step]

        @pl.when(count > 0)
        def _():
            row = owner_ref[step]
            query = q_ref[row]
            same = qv_ref[row] == pv_ref[step]
            keys = cache_ref[0, step]
            values = cache_ref[1, step]
            valid = lax.broadcasted_iota(jnp.int32, same.shape, 1) < count
            for head in range(head_local):
                cols = slice(head * HD, (head + 1) * HD)
                scores = lax.dot_general(
                    query[:, cols], keys[:, cols], (((1,), (1,)), ((), ())),
                    preferred_element_type=jnp.float32,
                ) * scale
                scores = scores + jnp.where(same, bias_ref[0, head], bias_ref[1, head])
                block_max = jnp.max(
                    jnp.where(valid, scores, masked_score), axis=1, keepdims=True
                )
                weights = jnp.where(valid, jnp.exp(scores - block_max), 0.0).astype(
                    jnp.bfloat16
                )
                block_total = jnp.sum(weights.astype(jnp.float32), axis=1, keepdims=True)
                block_out = jnp.dot(weights, values[:, cols], preferred_element_type=jnp.float32)
                old_max = max_ref[row, :, head : head + 1]
                new_max = jnp.maximum(old_max, block_max)
                keep_old = jnp.exp(old_max - new_max)
                keep_new = jnp.exp(block_max - new_max)
                max_ref[row, :, head : head + 1] = new_max
                total_ref[row, :, head : head + 1] = (
                    total_ref[row, :, head : head + 1] * keep_old + block_total * keep_new
                )
                out_ref[row, :, cols] = out_ref[row, :, cols] * keep_old + block_out * keep_new

        return carry

    lax.fori_loop(0, pool, one_page, 0)


def page_attention(owner, filled, queries, query_variates, page_cache, page_variates, bias,
                   interpret=False):
    requests, tree, qdl = queries.shape
    pool, page = page_variates.shape
    head_local = qdl // HD
    kernel = functools.partial(
        page_kernel, head_local=head_local, scale=1.0 / math.sqrt(HD), pool=pool
    )

    def whole(shape):
        return pl.BlockSpec(shape, lambda step, *_: (0,) * len(shape))

    grid_spec = pltpu.PrefetchScalarGridSpec(
        num_scalar_prefetch=2,
        grid=(1,),
        in_specs=[
            whole((requests, tree, qdl)),
            whole((requests, tree, 1)),
            whole(page_cache.shape),
            whole((pool, 1, page)),
            pl.BlockSpec(memory_space=pltpu.SMEM),
        ],
        out_specs=[
            whole((requests, tree, qdl)),
            whole((requests, tree, head_local)),
            whole((requests, tree, head_local)),
        ],
    )
    return pl.pallas_call(
        kernel,
        grid_spec=grid_spec,
        out_shape=[
            jax.ShapeDtypeStruct((requests, tree, qdl), jnp.float32),
            jax.ShapeDtypeStruct((requests, tree, head_local), jnp.float32),
            jax.ShapeDtypeStruct((requests, tree, head_local), jnp.float32),
        ],
        compiler_params=pltpu.CompilerParams(dimension_semantics=("arbitrary",)),
        interpret=interpret,
    )(owner, filled, queries, query_variates[..., None], page_cache,
      page_variates[:, None, :], bias)


def split_three(values):
    high = lax.reduce_precision(values, exponent_bits=8, mantissa_bits=7)
    rest = values - high
    middle = lax.reduce_precision(rest, exponent_bits=8, mantissa_bits=7)
    low = rest - middle
    return [part.astype(jnp.bfloat16) for part in (high, middle, low)]


def join_three(high, middle, low):
    return (high.astype(jnp.float32) + middle.astype(jnp.float32)) + low.astype(jnp.float32)


def gather_rows(rows, axis_name, parts):
    spread = jnp.broadcast_to(rows[None], (parts,) + rows.shape)
    return lax.all_to_all(spread, axis_name, 0, 0, tiled=True)


def shards(
    tokens,
    gains,
    qkv_weight,
    out_weight,
    gate_up_weight,
    down_weight,
    variate_bias,
    page_cache,
    page_variates,
    token_variates,
    cache_len,
    page_table,
    parents,
    accepted,
):
    scale = 1.0 / math.sqrt(HD)
    local_req, tree = parents.shape
    pool, page = page_variates.shape
    requests = cache_len.shape[0]
    qdl = qkv_weight.shape[2]
    head_local = qdl // HD
    head_slot = lax.axis_index("head")
    req_slot = lax.axis_index("req")
    bias_local = lax.dynamic_slice_in_dim(variate_bias, head_slot * head_local, head_local, 1)
    same_bias = bias_local[0]
    other_bias = bias_local[1]
    head_parts = lax.axis_size("head")
    group_tokens = gather_rows(tokens, "head", head_parts).reshape(-1, tokens.shape[1])
    normed = rms_scaled(group_tokens, gains[0]).astype(jnp.bfloat16)
    projected = jnp.einsum(
        "td,cdq->ctq",
        normed,
        qkv_weight,
        preferred_element_type=jnp.float32,
    ).astype(jnp.bfloat16)
    query = projected[0]
    key_new = projected[1]
    value_new = projected[2]
    all_queries = gather_rows(query, "req", requests // local_req)
    global_ids = req_slot * pool + jnp.arange(pool, dtype=jnp.int32)
    matching = (page_table[:, :, None] == global_ids[None, None, :]).astype(jnp.int32)
    owner = jnp.sum(matching * jnp.arange(requests, dtype=jnp.int32)[:, None, None], axis=(0, 1))
    page_order = jnp.sum(
        matching * jnp.arange(page_table.shape[1], dtype=jnp.int32)[None, :, None], axis=(0, 1)
    )
    owner_len = jnp.sum(matching * cache_len[:, None, None], axis=(0, 1))
    in_use = jnp.sum(matching, axis=(0, 1))
    filled = jnp.clip(owner_len - page_order * page, 0, page) * in_use
    valid = jnp.arange(page, dtype=jnp.int32)[None, :] < filled[:, None]
    head_of_column = jnp.arange(qdl, dtype=jnp.int32) // HD
    head_mask = jnp.arange(head_local, dtype=jnp.int32)[:, None] == head_of_column[None, :]
    request_out, acc_max, acc_total = page_attention(
        jnp.clip(owner, 0, requests - 1),
        filled,
        all_queries.reshape(requests, tree, qdl),
        token_variates.reshape(requests, tree),
        page_cache,
        page_variates,
        bias_local,
    )
    request_max = acc_max.transpose(0, 2, 1).reshape(requests, head_local * tree)
    request_total = acc_total.transpose(0, 2, 1).reshape(requests, head_local * tree)
    stats = jnp.stack([request_total, request_max], axis=1)
    packed = jnp.concatenate(
        [request_out.astype(jnp.bfloat16).reshape(requests, tree, qdl)] + split_three(stats),
        axis=1,
    )
    received = lax.all_to_all(packed, "req", split_axis=0, concat_axis=0, tiled=True)
    sources = lax.axis_size("req")
    received = received.reshape((sources, local_req) + packed.shape[1:])
    source_out = received[:, :, :tree].astype(jnp.float32)
    got_stats = join_three(
        *[received[:, :, tree + 2 * part : tree + 2 * part + 2] for part in range(3)]
    )
    source_total = got_stats[:, :, 0].reshape(sources, local_req, head_local, tree)
    source_max = got_stats[:, :, 1].reshape(sources, local_req, head_local, tree)
    largest = jnp.max(source_max, axis=0)
    source_factor = jnp.exp(source_max - largest[None])
    column_factor = jnp.sum(
        jnp.where(head_mask[None, None, :, None, :], source_factor[..., None], 0.0), axis=2
    )
    cached_part = (
        largest.transpose(0, 2, 1),
        jnp.sum(source_total * source_factor, axis=0).transpose(0, 2, 1),
        jnp.sum(source_out * column_factor, axis=0).reshape(local_req, tree, head_local, HD),
    )
    tree_query = query.reshape(local_req, tree, head_local, HD)
    tree_key = key_new.reshape(local_req, tree, head_local, HD)
    tree_value = value_new.reshape(local_req, tree, head_local, HD)
    nodes = jnp.arange(tree, dtype=jnp.int32)
    reach = (parents[:, :, None] == nodes[None, None, :]).astype(jnp.float32) + jnp.eye(
        tree, dtype=jnp.float32
    )[None]
    for step in range(LEVELS.bit_length()):
        reach = jnp.minimum(jnp.einsum("rij,rjk->rik", reach, reach, precision=highest), 1.0)
    allowed = reach > 0.5
    group_variates = lax.dynamic_slice_in_dim(
        token_variates, req_slot * local_req * tree, local_req * tree, 0
    ).reshape(local_req, tree)
    tree_scores = (
        jnp.einsum("rihd,rjhd->rihj", tree_query, tree_key, preferred_element_type=jnp.float32)
        * scale
    )
    same_tree = group_variates[:, :, None] == group_variates[:, None, :]
    tree_scores = tree_scores + jnp.where(
        same_tree[:, :, None, :], same_bias[None, None, :, None], other_bias[None, None, :, None]
    )
    keep_tree = allowed[:, :, None, :]
    tree_max = jnp.max(jnp.where(keep_tree, tree_scores, masked_score), axis=-1)
    tree_weights = jnp.where(keep_tree, jnp.exp(tree_scores - tree_max[..., None]), 0.0).astype(
        jnp.bfloat16
    )
    tree_total = jnp.sum(tree_weights, axis=-1, dtype=jnp.float32)
    tree_out = jnp.einsum(
        "rihj,rjhd->rihd", tree_weights, tree_value, preferred_element_type=jnp.float32
    )
    final_max, final_total, final_out = merge_parts(cached_part, (tree_max, tree_total, tree_out))
    attended = (
        (final_out / final_total[..., None]).astype(jnp.bfloat16).reshape(local_req * tree, qdl)
    )
    group_rows = local_req * tree
    token_heads = (
        gather_rows(attended, "head", head_parts).transpose(1, 0, 2).reshape(group_rows, -1)
    )
    attention_rows = jnp.dot(token_heads, out_weight, preferred_element_type=jnp.float32)
    hidden_state = (group_tokens.astype(jnp.float32) + attention_rows).astype(jnp.bfloat16)
    normed_two = rms_scaled(hidden_state, gains[1]).astype(jnp.bfloat16)
    both_parts = jnp.einsum(
        "td,cdf->ctf",
        normed_two,
        gate_up_weight,
        preferred_element_type=jnp.float32,
    )
    activated = (jax.nn.silu(both_parts[0]) * both_parts[1]).astype(jnp.bfloat16)
    down_part = jnp.dot(activated, down_weight, preferred_element_type=jnp.float32).astype(
        jnp.bfloat16
    )
    own_rows = tokens.shape[0]
    down_parts = lax.all_to_all(
        down_part.reshape(head_parts, own_rows, -1), "head", 0, 0, tiled=True
    )
    ffn_rows = jnp.sum(down_parts.astype(jnp.float32), axis=0)
    own_hidden = lax.dynamic_slice_in_dim(hidden_state, head_slot * own_rows, own_rows, 0)
    mixed = (own_hidden.astype(jnp.float32) + ffn_rows).astype(jnp.bfloat16)
    chosen = (accepted[:, :, None] == nodes[None, None, :]).astype(jnp.bfloat16)
    stacked = jnp.stack([key_new, value_new]).reshape(2, local_req, tree, qdl)
    new_kv = jnp.einsum(
        "rat,crtq->craq", chosen, stacked, preferred_element_type=jnp.float32
    ).astype(jnp.bfloat16)
    return (mixed, attended, new_kv)


def solution(mesh):
    return jax.shard_map(
        shards,
        mesh=mesh,
        in_specs=(
            P(("req", "head"), None),
            P(),
            P(None, None, "head"),
            P(),
            P(None, None, "head"),
            P("head", None),
            P(),
            P(None, "req", None, "head"),
            P("req", None),
            P(),
            P(),
            P(),
            P("req", None),
            P("req", None),
        ),
        out_specs=(P(("req", "head"), None), P("req", "head"), P(None, "req", None, "head")),
        check_vma=False,
    )
```

```python
import functools
import math

import jax
import jax.numpy as jnp
from jax import lax
from jax.experimental import pallas as pl
from jax.experimental.pallas import tpu as pltpu
from jax.sharding import PartitionSpec as P

HD = 64
LEVELS = 8


epsilon = 1e-06
masked_score = -1e30
highest = lax.Precision.HIGHEST


def rms_scaled(rows, gain):
    values = rows.astype(jnp.float32)
    return values * lax.rsqrt(jnp.mean(values * values, axis=-1, keepdims=True) + epsilon) * gain


def merge_parts(first, second):
    max_one, total_one, out_one = first
    max_two, total_two, out_two = second
    highest_max = jnp.maximum(max_one, max_two)
    factor_one = jnp.exp(max_one - highest_max)
    factor_two = jnp.exp(max_two - highest_max)
    return (
        highest_max,
        total_one * factor_one + total_two * factor_two,
        out_one * factor_one[..., None] + out_two * factor_two[..., None],
    )


def page_kernel(owner_ref, filled_ref, q_ref, qv_ref, cache_ref, pv_ref, bias_ref,
                out_ref, total_ref, max_ref, max_acc, total_acc,
                *, head_local, tree, scale, pool):
    rows, page = q_ref.shape[1], cache_ref.shape[2]
    out_ref[...] = jnp.zeros(out_ref.shape, jnp.float32)
    max_acc[...] = jnp.full(max_acc.shape, masked_score, jnp.float32)
    total_acc[...] = jnp.zeros(total_acc.shape, jnp.float32)
    request_lane = lax.broadcasted_iota(jnp.int32, max_acc.shape, 1)
    column_head = lax.broadcasted_iota(jnp.int32, out_ref.shape[1:], 1) // HD

    def pick_heads(values):
        picked = jnp.zeros(out_ref.shape[1:], jnp.float32)
        for head in range(head_local):
            picked = picked + jnp.where(
                column_head == head, values[head * tree : (head + 1) * tree], 0.0
            )
        return picked

    def one_page(step, carry):
        count = filled_ref[step]

        @pl.when(count > 0)
        def _():
            row = owner_ref[step]
            same = qv_ref[row] == pv_ref[step]
            valid = lax.broadcasted_iota(jnp.int32, (rows, page), 1) < count
            scores = lax.dot_general(
                q_ref[row], cache_ref[0, step], (((1,), (1,)), ((), ())),
                preferred_element_type=jnp.float32,
            ) * scale
            scores = scores + jnp.where(same, bias_ref[0], bias_ref[1])
            block_max = jnp.max(jnp.where(valid, scores, masked_score), axis=1, keepdims=True)
            weights = jnp.where(valid, jnp.exp(scores - block_max), 0.0).astype(jnp.bfloat16)
            block_total = jnp.sum(weights.astype(jnp.float32), axis=1, keepdims=True)
            crossed = jnp.dot(weights, cache_ref[1, step], preferred_element_type=jnp.float32)
            is_row = request_lane == row
            old_max = jnp.sum(jnp.where(is_row, max_acc[...], 0.0), axis=1, keepdims=True)
            old_total = jnp.sum(jnp.where(is_row, total_acc[...], 0.0), axis=1, keepdims=True)
            new_max = jnp.maximum(old_max, block_max)
            keep_old = jnp.exp(old_max - new_max)
            keep_new = jnp.exp(block_max - new_max)
            max_acc[...] = jnp.where(is_row, new_max, max_acc[...])
            total_acc[...] = jnp.where(
                is_row, old_total * keep_old + block_total * keep_new, total_acc[...]
            )
            out_ref[row] = out_ref[row] * pick_heads(
                jnp.broadcast_to(keep_old, crossed.shape)
            ) + pick_heads(crossed * keep_new)

        return carry

    lax.fori_loop(0, pool, one_page, 0)
    requests = out_ref.shape[0]
    total_ref[...] = jnp.transpose(total_acc[...])[:requests]
    max_ref[...] = jnp.transpose(max_acc[...])[:requests]


def page_attention(owner, filled, split_queries, row_variates, page_cache, page_variates,
                   row_bias, interpret=False):
    requests, rows, qdl = split_queries.shape
    pool, page = page_variates.shape
    head_local = qdl // HD
    tree = rows // head_local
    lanes = 128 * ((requests + 127) // 128)
    kernel = functools.partial(
        page_kernel, head_local=head_local, tree=tree, scale=1.0 / math.sqrt(HD), pool=pool
    )

    def whole(shape):
        return pl.BlockSpec(shape, lambda step, *_: (0,) * len(shape))

    grid_spec = pltpu.PrefetchScalarGridSpec(
        num_scalar_prefetch=2,
        grid=(1,),
        in_specs=[
            whole((requests, rows, qdl)),
            whole((requests, rows, 1)),
            whole(page_cache.shape),
            whole((pool, 1, page)),
            whole((2, rows, 1)),
        ],
        out_specs=[
            whole((requests, tree, qdl)),
            whole((requests, rows)),
            whole((requests, rows)),
        ],
        scratch_shapes=[pltpu.VMEM((rows, lanes), jnp.float32)] * 2,
    )
    return pl.pallas_call(
        kernel,
        grid_spec=grid_spec,
        out_shape=[
            jax.ShapeDtypeStruct((requests, tree, qdl), jnp.float32),
            jax.ShapeDtypeStruct((requests, rows), jnp.float32),
            jax.ShapeDtypeStruct((requests, rows), jnp.float32),
        ],
        compiler_params=pltpu.CompilerParams(dimension_semantics=("arbitrary",)),
        interpret=interpret,
    )(owner, filled, split_queries, row_variates[..., None], page_cache,
      page_variates[:, None, :], row_bias[..., None])


def split_three(values):
    high = lax.reduce_precision(values, exponent_bits=8, mantissa_bits=7)
    rest = values - high
    middle = lax.reduce_precision(rest, exponent_bits=8, mantissa_bits=7)
    low = rest - middle
    return [part.astype(jnp.bfloat16) for part in (high, middle, low)]


def join_three(high, middle, low):
    return (high.astype(jnp.float32) + middle.astype(jnp.float32)) + low.astype(jnp.float32)


def gather_rows(rows, axis_name, parts):
    spread = jnp.broadcast_to(rows[None], (parts,) + rows.shape)
    return lax.all_to_all(spread, axis_name, 0, 0, tiled=True)


def shards(
    tokens,
    gains,
    qkv_weight,
    out_weight,
    gate_up_weight,
    down_weight,
    variate_bias,
    page_cache,
    page_variates,
    token_variates,
    cache_len,
    page_table,
    parents,
    accepted,
):
    scale = 1.0 / math.sqrt(HD)
    local_req, tree = parents.shape
    pool, page = page_variates.shape
    requests = cache_len.shape[0]
    qdl = qkv_weight.shape[2]
    head_local = qdl // HD
    head_slot = lax.axis_index("head")
    req_slot = lax.axis_index("req")
    bias_local = lax.dynamic_slice_in_dim(variate_bias, head_slot * head_local, head_local, 1)
    same_bias = bias_local[0]
    other_bias = bias_local[1]
    head_parts = lax.axis_size("head")
    group_tokens = gather_rows(tokens, "head", head_parts).reshape(-1, tokens.shape[1])
    normed = rms_scaled(group_tokens, gains[0]).astype(jnp.bfloat16)
    projected = jnp.einsum(
        "td,cdq->ctq",
        normed,
        qkv_weight,
        preferred_element_type=jnp.float32,
    ).astype(jnp.bfloat16)
    query = projected[0]
    key_new = projected[1]
    value_new = projected[2]
    all_queries = gather_rows(query, "req", requests // local_req)
    global_ids = req_slot * pool + jnp.arange(pool, dtype=jnp.int32)
    matching = (page_table[:, :, None] == global_ids[None, None, :]).astype(jnp.int32)
    owner = jnp.sum(matching * jnp.arange(requests, dtype=jnp.int32)[:, None, None], axis=(0, 1))
    page_order = jnp.sum(
        matching * jnp.arange(page_table.shape[1], dtype=jnp.int32)[None, :, None], axis=(0, 1)
    )
    owner_len = jnp.sum(matching * cache_len[:, None, None], axis=(0, 1))
    in_use = jnp.sum(matching, axis=(0, 1))
    filled = jnp.clip(owner_len - page_order * page, 0, page) * in_use
    valid = jnp.arange(page, dtype=jnp.int32)[None, :] < filled[:, None]
    head_of_column = jnp.arange(qdl, dtype=jnp.int32) // HD
    head_mask = jnp.arange(head_local, dtype=jnp.int32)[:, None] == head_of_column[None, :]
    split_rows = head_local * tree
    split_queries = jnp.where(
        head_mask[None, :, None, :],
        all_queries.reshape(requests, 1, tree, qdl),
        jnp.zeros((), all_queries.dtype),
    ).reshape(requests, split_rows, qdl)
    row_variates = jnp.broadcast_to(
        token_variates.reshape(requests, 1, tree), (requests, head_local, tree)
    ).reshape(requests, split_rows)
    row_bias = jnp.broadcast_to(bias_local[:, :, None], (2, head_local, tree)).reshape(
        2, split_rows
    )
    request_out, request_total, request_max = page_attention(
        jnp.clip(owner, 0, requests - 1),
        filled,
        split_queries,
        row_variates,
        page_cache,
        page_variates,
        row_bias,
    )
    stats = jnp.stack([request_total, request_max], axis=1)
    packed = jnp.concatenate(
        [request_out.astype(jnp.bfloat16).reshape(requests, tree, qdl)] + split_three(stats),
        axis=1,
    )
    received = lax.all_to_all(packed, "req", split_axis=0, concat_axis=0, tiled=True)
    sources = lax.axis_size("req")
    received = received.reshape((sources, local_req) + packed.shape[1:])
    source_out = received[:, :, :tree].astype(jnp.float32)
    got_stats = join_three(
        *[received[:, :, tree + 2 * part : tree + 2 * part + 2] for part in range(3)]
    )
    source_total = got_stats[:, :, 0].reshape(sources, local_req, head_local, tree)
    source_max = got_stats[:, :, 1].reshape(sources, local_req, head_local, tree)
    largest = jnp.max(source_max, axis=0)
    source_factor = jnp.exp(source_max - largest[None])
    column_factor = jnp.sum(
        jnp.where(head_mask[None, None, :, None, :], source_factor[..., None], 0.0), axis=2
    )
    cached_part = (
        largest.transpose(0, 2, 1),
        jnp.sum(source_total * source_factor, axis=0).transpose(0, 2, 1),
        jnp.sum(source_out * column_factor, axis=0).reshape(local_req, tree, head_local, HD),
    )
    tree_query = query.reshape(local_req, tree, head_local, HD)
    tree_key = key_new.reshape(local_req, tree, head_local, HD)
    tree_value = value_new.reshape(local_req, tree, head_local, HD)
    nodes = jnp.arange(tree, dtype=jnp.int32)
    reach = (parents[:, :, None] == nodes[None, None, :]).astype(jnp.float32) + jnp.eye(
        tree, dtype=jnp.float32
    )[None]
    for step in range(LEVELS.bit_length()):
        reach = jnp.minimum(jnp.einsum("rij,rjk->rik", reach, reach, precision=highest), 1.0)
    allowed = reach > 0.5
    group_variates = lax.dynamic_slice_in_dim(
        token_variates, req_slot * local_req * tree, local_req * tree, 0
    ).reshape(local_req, tree)
    tree_scores = (
        jnp.einsum("rihd,rjhd->rihj", tree_query, tree_key, preferred_element_type=jnp.float32)
        * scale
    )
    same_tree = group_variates[:, :, None] == group_variates[:, None, :]
    tree_scores = tree_scores + jnp.where(
        same_tree[:, :, None, :], same_bias[None, None, :, None], other_bias[None, None, :, None]
    )
    keep_tree = allowed[:, :, None, :]
    tree_max = jnp.max(jnp.where(keep_tree, tree_scores, masked_score), axis=-1)
    tree_weights = jnp.where(keep_tree, jnp.exp(tree_scores - tree_max[..., None]), 0.0).astype(
        jnp.bfloat16
    )
    tree_total = jnp.sum(tree_weights, axis=-1, dtype=jnp.float32)
    tree_out = jnp.einsum(
        "rihj,rjhd->rihd", tree_weights, tree_value, preferred_element_type=jnp.float32
    )
    final_max, final_total, final_out = merge_parts(cached_part, (tree_max, tree_total, tree_out))
    attended = (
        (final_out / final_total[..., None]).astype(jnp.bfloat16).reshape(local_req * tree, qdl)
    )
    group_rows = local_req * tree
    token_heads = (
        gather_rows(attended, "head", head_parts).transpose(1, 0, 2).reshape(group_rows, -1)
    )
    attention_rows = jnp.dot(token_heads, out_weight, preferred_element_type=jnp.float32)
    hidden_state = (group_tokens.astype(jnp.float32) + attention_rows).astype(jnp.bfloat16)
    normed_two = rms_scaled(hidden_state, gains[1]).astype(jnp.bfloat16)
    both_parts = jnp.einsum(
        "td,cdf->ctf",
        normed_two,
        gate_up_weight,
        preferred_element_type=jnp.float32,
    )
    activated = (jax.nn.silu(both_parts[0]) * both_parts[1]).astype(jnp.bfloat16)
    down_part = jnp.dot(activated, down_weight, preferred_element_type=jnp.float32).astype(
        jnp.bfloat16
    )
    own_rows = tokens.shape[0]
    down_parts = lax.all_to_all(
        down_part.reshape(head_parts, own_rows, -1), "head", 0, 0, tiled=True
    )
    ffn_rows = jnp.sum(down_parts.astype(jnp.float32), axis=0)
    own_hidden = lax.dynamic_slice_in_dim(hidden_state, head_slot * own_rows, own_rows, 0)
    mixed = (own_hidden.astype(jnp.float32) + ffn_rows).astype(jnp.bfloat16)
    chosen = (accepted[:, :, None] == nodes[None, None, :]).astype(jnp.bfloat16)
    stacked = jnp.stack([key_new, value_new]).reshape(2, local_req, tree, qdl)
    new_kv = jnp.einsum(
        "rat,crtq->craq", chosen, stacked, preferred_element_type=jnp.float32
    ).astype(jnp.bfloat16)
    return (mixed, attended, new_kv)


def solution(mesh):
    return jax.shard_map(
        shards,
        mesh=mesh,
        in_specs=(
            P(("req", "head"), None),
            P(),
            P(None, None, "head"),
            P(),
            P(None, None, "head"),
            P("head", None),
            P(),
            P(None, "req", None, "head"),
            P("req", None),
            P(),
            P(),
            P(),
            P("req", None),
            P("req", None),
        ),
        out_specs=(P(("req", "head"), None), P("req", "head"), P(None, "req", None, "head")),
        check_vma=False,
    )
```

```python
import functools
import math

import jax
import jax.numpy as jnp
from jax import lax
from jax.experimental import pallas as pl
from jax.experimental.pallas import tpu as pltpu
from jax.sharding import PartitionSpec as P

HD = 64
LEVELS = 8


epsilon = 1e-06
masked_score = -1e30
highest = lax.Precision.HIGHEST


def rms_scaled(rows, gain):
    values = rows.astype(jnp.float32)
    return values * lax.rsqrt(jnp.mean(values * values, axis=-1, keepdims=True) + epsilon) * gain


def merge_parts(first, second):
    max_one, total_one, out_one = first
    max_two, total_two, out_two = second
    highest_max = jnp.maximum(max_one, max_two)
    factor_one = jnp.exp(max_one - highest_max)
    factor_two = jnp.exp(max_two - highest_max)
    return (
        highest_max,
        total_one * factor_one + total_two * factor_two,
        out_one * factor_one[..., None] + out_two * factor_two[..., None],
    )


def page_kernel(owner_ref, filled_ref, q_ref, aux_ref, cache_ref, pv_ref,
                out_ref, total_ref, max_ref, out_acc, max_acc, total_acc,
                *, head_local, tree, scale, pool):
    rows, page = q_ref.shape[1], cache_ref.shape[2]
    lanes = aux_ref.shape[0]
    out_acc[...] = jnp.zeros(out_acc.shape, jnp.float32)
    max_acc[...] = jnp.full(max_acc.shape, masked_score, jnp.float32)
    total_acc[...] = jnp.zeros(total_acc.shape, jnp.float32)
    request_lane = lax.broadcasted_iota(jnp.int32, max_acc.shape, 1)
    column_head = lax.broadcasted_iota(jnp.int32, out_acc.shape[1:], 1) // HD
    aux_columns = jnp.transpose(aux_ref[...])

    def column_of(index):
        return jnp.sum(jnp.where(request_lane == index, aux_columns, 0.0), axis=1, keepdims=True)

    same_bias = column_of(lanes - 2)
    other_bias = column_of(lanes - 1)

    def pick_heads(values):
        picked = jnp.zeros(out_acc.shape[1:], jnp.float32)
        for head in range(head_local):
            picked = picked + jnp.where(
                column_head == head, values[head * tree : (head + 1) * tree], 0.0
            )
        return picked

    def one_page(step, carry):
        count = filled_ref[step]

        @pl.when(count > 0)
        def _():
            row = owner_ref[step]
            same = column_of(row) == pv_ref[step]
            valid = lax.broadcasted_iota(jnp.int32, (rows, page), 1) < count
            scores = lax.dot_general(
                q_ref[row], cache_ref[0, step], (((1,), (1,)), ((), ())),
                preferred_element_type=jnp.float32,
            ) * scale
            scores = scores + jnp.where(same, same_bias, other_bias)
            block_max = jnp.max(jnp.where(valid, scores, masked_score), axis=1, keepdims=True)
            weights = jnp.where(valid, jnp.exp(scores - block_max), 0.0).astype(jnp.bfloat16)
            block_total = jnp.sum(weights.astype(jnp.float32), axis=1, keepdims=True)
            crossed = jnp.dot(weights, cache_ref[1, step], preferred_element_type=jnp.float32)
            is_row = request_lane == row
            old_max = jnp.sum(jnp.where(is_row, max_acc[...], 0.0), axis=1, keepdims=True)
            old_total = jnp.sum(jnp.where(is_row, total_acc[...], 0.0), axis=1, keepdims=True)
            new_max = jnp.maximum(old_max, block_max)
            keep_old = jnp.exp(old_max - new_max)
            keep_new = jnp.exp(block_max - new_max)
            max_acc[...] = jnp.where(is_row, new_max, max_acc[...])
            total_acc[...] = jnp.where(
                is_row, old_total * keep_old + block_total * keep_new, total_acc[...]
            )
            out_acc[row] = out_acc[row] * pick_heads(
                jnp.broadcast_to(keep_old, crossed.shape)
            ) + pick_heads(crossed * keep_new)

        return carry

    lax.fori_loop(0, pool, one_page, 0)
    requests = out_ref.shape[0]
    out_ref[...] = out_acc[...].astype(out_ref.dtype)
    total_ref[...] = jnp.transpose(total_acc[...])[:requests]
    max_ref[...] = jnp.transpose(max_acc[...])[:requests]


def page_attention(owner, filled, split_queries, row_variates, page_cache, page_variates,
                   row_bias, interpret=False):
    requests, rows, qdl = split_queries.shape
    pool, page = page_variates.shape
    head_local = qdl // HD
    tree = rows // head_local
    lanes = 128 * ((requests + 2 + 127) // 128)
    aux = jnp.concatenate(
        [
            row_variates.astype(jnp.float32),
            jnp.zeros((lanes - requests - 2, rows), jnp.float32),
            row_bias,
        ],
        axis=0,
    )
    kernel = functools.partial(
        page_kernel, head_local=head_local, tree=tree, scale=1.0 / math.sqrt(HD), pool=pool
    )

    def whole(shape):
        return pl.BlockSpec(shape, lambda step, *_: (0,) * len(shape))

    grid_spec = pltpu.PrefetchScalarGridSpec(
        num_scalar_prefetch=2,
        grid=(1,),
        in_specs=[
            whole((requests, rows, qdl)),
            whole((lanes, rows)),
            whole(page_cache.shape),
            whole((pool, 1, page)),
        ],
        out_specs=[
            whole((requests, tree, qdl)),
            whole((requests, rows)),
            whole((requests, rows)),
        ],
        scratch_shapes=[
            pltpu.VMEM((requests, tree, qdl), jnp.float32),
            pltpu.VMEM((rows, lanes), jnp.float32),
            pltpu.VMEM((rows, lanes), jnp.float32),
        ],
    )
    return pl.pallas_call(
        kernel,
        grid_spec=grid_spec,
        out_shape=[
            jax.ShapeDtypeStruct((requests, tree, qdl), jnp.bfloat16),
            jax.ShapeDtypeStruct((requests, rows), jnp.float32),
            jax.ShapeDtypeStruct((requests, rows), jnp.float32),
        ],
        compiler_params=pltpu.CompilerParams(dimension_semantics=("arbitrary",)),
        interpret=interpret,
    )(owner, filled, split_queries, aux, page_cache, page_variates[:, None, :])


def split_three(values):
    high = lax.reduce_precision(values, exponent_bits=8, mantissa_bits=7)
    rest = values - high
    middle = lax.reduce_precision(rest, exponent_bits=8, mantissa_bits=7)
    low = rest - middle
    return [part.astype(jnp.bfloat16) for part in (high, middle, low)]


def join_three(high, middle, low):
    return (high.astype(jnp.float32) + middle.astype(jnp.float32)) + low.astype(jnp.float32)


def gather_rows(rows, axis_name, parts):
    spread = jnp.broadcast_to(rows[None], (parts,) + rows.shape)
    return lax.all_to_all(spread, axis_name, 0, 0, tiled=True)


def shards(
    tokens,
    gains,
    qkv_weight,
    out_weight,
    gate_up_weight,
    down_weight,
    variate_bias,
    page_cache,
    page_variates,
    token_variates,
    cache_len,
    page_table,
    parents,
    accepted,
):
    scale = 1.0 / math.sqrt(HD)
    local_req, tree = parents.shape
    pool, page = page_variates.shape
    requests = cache_len.shape[0]
    qdl = qkv_weight.shape[2]
    head_local = qdl // HD
    head_slot = lax.axis_index("head")
    req_slot = lax.axis_index("req")
    bias_local = lax.dynamic_slice_in_dim(variate_bias, head_slot * head_local, head_local, 1)
    same_bias = bias_local[0]
    other_bias = bias_local[1]
    head_parts = lax.axis_size("head")
    group_tokens = gather_rows(tokens, "head", head_parts).reshape(-1, tokens.shape[1])
    normed = rms_scaled(group_tokens, gains[0]).astype(jnp.bfloat16)
    projected = jnp.einsum(
        "td,cdq->ctq",
        normed,
        qkv_weight,
        preferred_element_type=jnp.float32,
    ).astype(jnp.bfloat16)
    query = projected[0]
    key_new = projected[1]
    value_new = projected[2]
    all_queries = gather_rows(query, "req", requests // local_req)
    global_ids = req_slot * pool + jnp.arange(pool, dtype=jnp.int32)
    matching = (page_table[:, :, None] == global_ids[None, None, :]).astype(jnp.int32)
    owner = jnp.sum(matching * jnp.arange(requests, dtype=jnp.int32)[:, None, None], axis=(0, 1))
    page_order = jnp.sum(
        matching * jnp.arange(page_table.shape[1], dtype=jnp.int32)[None, :, None], axis=(0, 1)
    )
    owner_len = jnp.sum(matching * cache_len[:, None, None], axis=(0, 1))
    in_use = jnp.sum(matching, axis=(0, 1))
    filled = jnp.clip(owner_len - page_order * page, 0, page) * in_use
    valid = jnp.arange(page, dtype=jnp.int32)[None, :] < filled[:, None]
    head_of_column = jnp.arange(qdl, dtype=jnp.int32) // HD
    head_mask = jnp.arange(head_local, dtype=jnp.int32)[:, None] == head_of_column[None, :]
    split_rows = head_local * tree
    split_queries = jnp.where(
        head_mask[None, :, None, :],
        all_queries.reshape(requests, 1, tree, qdl),
        jnp.zeros((), all_queries.dtype),
    ).reshape(requests, split_rows, qdl)
    row_variates = jnp.broadcast_to(
        token_variates.reshape(requests, 1, tree), (requests, head_local, tree)
    ).reshape(requests, split_rows)
    row_bias = jnp.broadcast_to(bias_local[:, :, None], (2, head_local, tree)).reshape(
        2, split_rows
    )
    request_out, request_total, request_max = page_attention(
        jnp.clip(owner, 0, requests - 1),
        filled,
        split_queries,
        row_variates,
        page_cache,
        page_variates,
        row_bias,
    )
    stats = jnp.stack([request_total, request_max], axis=1)
    packed = jnp.concatenate(
        [request_out.astype(jnp.bfloat16).reshape(requests, tree, qdl)] + split_three(stats),
        axis=1,
    )
    received = lax.all_to_all(packed, "req", split_axis=0, concat_axis=0, tiled=True)
    sources = lax.axis_size("req")
    received = received.reshape((sources, local_req) + packed.shape[1:])
    source_out = received[:, :, :tree].astype(jnp.float32)
    got_stats = join_three(
        *[received[:, :, tree + 2 * part : tree + 2 * part + 2] for part in range(3)]
    )
    source_total = got_stats[:, :, 0].reshape(sources, local_req, head_local, tree)
    source_max = got_stats[:, :, 1].reshape(sources, local_req, head_local, tree)
    largest = jnp.max(source_max, axis=0)
    source_factor = jnp.exp(source_max - largest[None])
    column_factor = jnp.sum(
        jnp.where(head_mask[None, None, :, None, :], source_factor[..., None], 0.0), axis=2
    )
    cached_part = (
        largest.transpose(0, 2, 1),
        jnp.sum(source_total * source_factor, axis=0).transpose(0, 2, 1),
        jnp.sum(source_out * column_factor, axis=0).reshape(local_req, tree, head_local, HD),
    )
    tree_query = query.reshape(local_req, tree, head_local, HD)
    tree_key = key_new.reshape(local_req, tree, head_local, HD)
    tree_value = value_new.reshape(local_req, tree, head_local, HD)
    nodes = jnp.arange(tree, dtype=jnp.int32)
    reach = (parents[:, :, None] == nodes[None, None, :]).astype(jnp.float32) + jnp.eye(
        tree, dtype=jnp.float32
    )[None]
    for step in range(LEVELS.bit_length()):
        reach = jnp.minimum(jnp.einsum("rij,rjk->rik", reach, reach, precision=highest), 1.0)
    allowed = reach > 0.5
    group_variates = lax.dynamic_slice_in_dim(
        token_variates, req_slot * local_req * tree, local_req * tree, 0
    ).reshape(local_req, tree)
    tree_scores = (
        jnp.einsum("rihd,rjhd->rihj", tree_query, tree_key, preferred_element_type=jnp.float32)
        * scale
    )
    same_tree = group_variates[:, :, None] == group_variates[:, None, :]
    tree_scores = tree_scores + jnp.where(
        same_tree[:, :, None, :], same_bias[None, None, :, None], other_bias[None, None, :, None]
    )
    keep_tree = allowed[:, :, None, :]
    tree_max = jnp.max(jnp.where(keep_tree, tree_scores, masked_score), axis=-1)
    tree_weights = jnp.where(keep_tree, jnp.exp(tree_scores - tree_max[..., None]), 0.0).astype(
        jnp.bfloat16
    )
    tree_total = jnp.sum(tree_weights, axis=-1, dtype=jnp.float32)
    tree_out = jnp.einsum(
        "rihj,rjhd->rihd", tree_weights, tree_value, preferred_element_type=jnp.float32
    )
    final_max, final_total, final_out = merge_parts(cached_part, (tree_max, tree_total, tree_out))
    attended = (
        (final_out / final_total[..., None]).astype(jnp.bfloat16).reshape(local_req * tree, qdl)
    )
    group_rows = local_req * tree
    token_heads = (
        gather_rows(attended, "head", head_parts).transpose(1, 0, 2).reshape(group_rows, -1)
    )
    attention_rows = jnp.dot(token_heads, out_weight, preferred_element_type=jnp.float32)
    hidden_state = (group_tokens.astype(jnp.float32) + attention_rows).astype(jnp.bfloat16)
    normed_two = rms_scaled(hidden_state, gains[1]).astype(jnp.bfloat16)
    both_parts = jnp.einsum(
        "td,cdf->ctf",
        normed_two,
        gate_up_weight,
        preferred_element_type=jnp.float32,
    )
    activated = (jax.nn.silu(both_parts[0]) * both_parts[1]).astype(jnp.bfloat16)
    down_part = jnp.dot(activated, down_weight, preferred_element_type=jnp.float32).astype(
        jnp.bfloat16
    )
    own_rows = tokens.shape[0]
    down_parts = lax.all_to_all(
        down_part.reshape(head_parts, own_rows, -1), "head", 0, 0, tiled=True
    )
    ffn_rows = jnp.sum(down_parts.astype(jnp.float32), axis=0)
    own_hidden = lax.dynamic_slice_in_dim(hidden_state, head_slot * own_rows, own_rows, 0)
    mixed = (own_hidden.astype(jnp.float32) + ffn_rows).astype(jnp.bfloat16)
    chosen = (accepted[:, :, None] == nodes[None, None, :]).astype(jnp.bfloat16)
    stacked = jnp.stack([key_new, value_new]).reshape(2, local_req, tree, qdl)
    new_kv = jnp.einsum(
        "rat,crtq->craq", chosen, stacked, preferred_element_type=jnp.float32
    ).astype(jnp.bfloat16)
    return (mixed, attended, new_kv)


def solution(mesh):
    return jax.shard_map(
        shards,
        mesh=mesh,
        in_specs=(
            P(("req", "head"), None),
            P(),
            P(None, None, "head"),
            P(),
            P(None, None, "head"),
            P("head", None),
            P(),
            P(None, "req", None, "head"),
            P("req", None),
            P(),
            P(),
            P(),
            P("req", None),
            P("req", None),
        ),
        out_specs=(P(("req", "head"), None), P("req", "head"), P(None, "req", None, "head")),
        check_vma=False,
    )
```

```python
import functools
import math

import jax
import jax.numpy as jnp
from jax import lax
from jax.experimental import pallas as pl
from jax.experimental.pallas import tpu as pltpu
from jax.sharding import PartitionSpec as P

HD = 64
LEVELS = 8


epsilon = 1e-06
masked_score = -1e30
highest = lax.Precision.HIGHEST


def rms_scaled(rows, gain):
    values = rows.astype(jnp.float32)
    return values * lax.rsqrt(jnp.mean(values * values, axis=-1, keepdims=True) + epsilon) * gain


def merge_parts(first, second):
    max_one, total_one, out_one = first
    max_two, total_two, out_two = second
    highest_max = jnp.maximum(max_one, max_two)
    factor_one = jnp.exp(max_one - highest_max)
    factor_two = jnp.exp(max_two - highest_max)
    return (
        highest_max,
        total_one * factor_one + total_two * factor_two,
        out_one * factor_one[..., None] + out_two * factor_two[..., None],
    )


def page_kernel(owner_ref, filled_ref, q_ref, aux_ref, cache_ref, pv_ref,
                out_ref, out_acc, max_acc, total_acc,
                *, head_local, tree, scale, pool):
    rows, page = q_ref.shape[1], cache_ref.shape[2]
    lanes = aux_ref.shape[0]
    out_acc[...] = jnp.zeros(out_acc.shape, jnp.float32)
    max_acc[...] = jnp.full(max_acc.shape, masked_score, jnp.float32)
    total_acc[...] = jnp.zeros(total_acc.shape, jnp.float32)
    request_lane = lax.broadcasted_iota(jnp.int32, max_acc.shape, 1)
    column_head = lax.broadcasted_iota(jnp.int32, out_acc.shape[1:], 1) // HD
    aux_columns = jnp.transpose(aux_ref[...])

    def column_of(index):
        return jnp.sum(jnp.where(request_lane == index, aux_columns, 0.0), axis=1, keepdims=True)

    same_bias = column_of(lanes - 2)
    other_bias = column_of(lanes - 1)

    def pick_heads(values):
        picked = jnp.zeros(out_acc.shape[1:], jnp.float32)
        for head in range(head_local):
            picked = picked + jnp.where(
                column_head == head, values[head * tree : (head + 1) * tree], 0.0
            )
        return picked

    def one_page(step, carry):
        count = filled_ref[step]

        @pl.when(count > 0)
        def _():
            row = owner_ref[step]
            same = column_of(row) == pv_ref[step]
            valid = lax.broadcasted_iota(jnp.int32, (rows, page), 1) < count
            scores = lax.dot_general(
                q_ref[row], cache_ref[0, step], (((1,), (1,)), ((), ())),
                preferred_element_type=jnp.float32,
            ) * scale
            scores = scores + jnp.where(same, same_bias, other_bias)
            block_max = jnp.max(jnp.where(valid, scores, masked_score), axis=1, keepdims=True)
            weights = jnp.where(valid, jnp.exp(scores - block_max), 0.0).astype(jnp.bfloat16)
            block_total = jnp.sum(weights.astype(jnp.float32), axis=1, keepdims=True)
            crossed = jnp.dot(weights, cache_ref[1, step], preferred_element_type=jnp.float32)
            is_row = request_lane == row
            old_max = jnp.sum(jnp.where(is_row, max_acc[...], 0.0), axis=1, keepdims=True)
            old_total = jnp.sum(jnp.where(is_row, total_acc[...], 0.0), axis=1, keepdims=True)
            new_max = jnp.maximum(old_max, block_max)
            keep_old = jnp.exp(old_max - new_max)
            keep_new = jnp.exp(block_max - new_max)
            max_acc[...] = jnp.where(is_row, new_max, max_acc[...])
            total_acc[...] = jnp.where(
                is_row, old_total * keep_old + block_total * keep_new, total_acc[...]
            )
            out_acc[row] = out_acc[row] * pick_heads(
                jnp.broadcast_to(keep_old, crossed.shape)
            ) + pick_heads(crossed * keep_new)

        return carry

    lax.fori_loop(0, pool, one_page, 0)
    requests = out_ref.shape[0]
    out_ref[:, :tree, :] = out_acc[...].astype(out_ref.dtype)
    stats = (
        jnp.transpose(total_acc[...])[:requests],
        jnp.transpose(max_acc[...])[:requests],
    )
    for kind, values in enumerate(stats):
        for part in range(3):
            rounded = values.astype(out_ref.dtype)
            out_ref[:, tree + 2 * part + kind, :] = rounded
            values = values - rounded.astype(jnp.float32)


def page_attention(owner, filled, split_queries, row_variates, page_cache, page_variates,
                   row_bias, interpret=False):
    requests, rows, qdl = split_queries.shape
    pool, page = page_variates.shape
    head_local = qdl // HD
    tree = rows // head_local
    lanes = 128 * ((requests + 2 + 127) // 128)
    aux = jnp.concatenate(
        [
            row_variates.astype(jnp.float32),
            jnp.zeros((lanes - requests - 2, rows), jnp.float32),
            row_bias,
        ],
        axis=0,
    )
    kernel = functools.partial(
        page_kernel, head_local=head_local, tree=tree, scale=1.0 / math.sqrt(HD), pool=pool
    )

    def whole(shape):
        return pl.BlockSpec(shape, lambda step, *_: (0,) * len(shape))

    grid_spec = pltpu.PrefetchScalarGridSpec(
        num_scalar_prefetch=2,
        grid=(1,),
        in_specs=[
            whole((requests, rows, qdl)),
            whole((lanes, rows)),
            whole(page_cache.shape),
            whole((pool, 1, page)),
        ],
        out_specs=whole((requests, tree + 6, qdl)),
        scratch_shapes=[
            pltpu.VMEM((requests, tree, qdl), jnp.float32),
            pltpu.VMEM((rows, lanes), jnp.float32),
            pltpu.VMEM((rows, lanes), jnp.float32),
        ],
    )
    return pl.pallas_call(
        kernel,
        grid_spec=grid_spec,
        out_shape=jax.ShapeDtypeStruct((requests, tree + 6, qdl), jnp.bfloat16),
        compiler_params=pltpu.CompilerParams(dimension_semantics=("arbitrary",)),
        interpret=interpret,
    )(owner, filled, split_queries, aux, page_cache, page_variates[:, None, :])


def join_three(high, middle, low):
    return (high.astype(jnp.float32) + middle.astype(jnp.float32)) + low.astype(jnp.float32)


def gather_rows(rows, axis_name, parts):
    spread = jnp.broadcast_to(rows[None], (parts,) + rows.shape)
    return lax.all_to_all(spread, axis_name, 0, 0, tiled=True)


def shards(
    tokens,
    gains,
    qkv_weight,
    out_weight,
    gate_up_weight,
    down_weight,
    variate_bias,
    page_cache,
    page_variates,
    token_variates,
    cache_len,
    page_table,
    parents,
    accepted,
):
    scale = 1.0 / math.sqrt(HD)
    local_req, tree = parents.shape
    pool, page = page_variates.shape
    requests = cache_len.shape[0]
    qdl = qkv_weight.shape[2]
    head_local = qdl // HD
    head_slot = lax.axis_index("head")
    req_slot = lax.axis_index("req")
    bias_local = lax.dynamic_slice_in_dim(variate_bias, head_slot * head_local, head_local, 1)
    same_bias = bias_local[0]
    other_bias = bias_local[1]
    head_parts = lax.axis_size("head")
    group_tokens = gather_rows(tokens, "head", head_parts).reshape(-1, tokens.shape[1])
    normed = rms_scaled(group_tokens, gains[0]).astype(jnp.bfloat16)
    projected = jnp.einsum(
        "td,cdq->ctq",
        normed,
        qkv_weight,
        preferred_element_type=jnp.float32,
    ).astype(jnp.bfloat16)
    query = projected[0]
    key_new = projected[1]
    value_new = projected[2]
    all_queries = gather_rows(query, "req", requests // local_req)
    global_ids = req_slot * pool + jnp.arange(pool, dtype=jnp.int32)
    matching = (page_table[:, :, None] == global_ids[None, None, :]).astype(jnp.int32)
    owner = jnp.sum(matching * jnp.arange(requests, dtype=jnp.int32)[:, None, None], axis=(0, 1))
    page_order = jnp.sum(
        matching * jnp.arange(page_table.shape[1], dtype=jnp.int32)[None, :, None], axis=(0, 1)
    )
    owner_len = jnp.sum(matching * cache_len[:, None, None], axis=(0, 1))
    in_use = jnp.sum(matching, axis=(0, 1))
    filled = jnp.clip(owner_len - page_order * page, 0, page) * in_use
    valid = jnp.arange(page, dtype=jnp.int32)[None, :] < filled[:, None]
    head_of_column = jnp.arange(qdl, dtype=jnp.int32) // HD
    head_mask = jnp.arange(head_local, dtype=jnp.int32)[:, None] == head_of_column[None, :]
    split_rows = head_local * tree
    split_queries = jnp.where(
        head_mask[None, :, None, :],
        all_queries.reshape(requests, 1, tree, qdl),
        jnp.zeros((), all_queries.dtype),
    ).reshape(requests, split_rows, qdl)
    row_variates = jnp.broadcast_to(
        token_variates.reshape(requests, 1, tree), (requests, head_local, tree)
    ).reshape(requests, split_rows)
    row_bias = jnp.broadcast_to(bias_local[:, :, None], (2, head_local, tree)).reshape(
        2, split_rows
    )
    packed = page_attention(
        jnp.clip(owner, 0, requests - 1),
        filled,
        split_queries,
        row_variates,
        page_cache,
        page_variates,
        row_bias,
    )
    received = lax.all_to_all(packed, "req", split_axis=0, concat_axis=0, tiled=True)
    sources = lax.axis_size("req")
    received = received.reshape((sources, local_req) + packed.shape[1:])
    source_out = received[:, :, :tree].astype(jnp.float32)
    got_stats = join_three(
        *[received[:, :, tree + 2 * part : tree + 2 * part + 2] for part in range(3)]
    )
    source_total = got_stats[:, :, 0].reshape(sources, local_req, head_local, tree)
    source_max = got_stats[:, :, 1].reshape(sources, local_req, head_local, tree)
    largest = jnp.max(source_max, axis=0)
    source_factor = jnp.exp(source_max - largest[None])
    column_factor = jnp.sum(
        jnp.where(head_mask[None, None, :, None, :], source_factor[..., None], 0.0), axis=2
    )
    cached_part = (
        largest.transpose(0, 2, 1),
        jnp.sum(source_total * source_factor, axis=0).transpose(0, 2, 1),
        jnp.sum(source_out * column_factor, axis=0).reshape(local_req, tree, head_local, HD),
    )
    tree_query = query.reshape(local_req, tree, head_local, HD)
    tree_key = key_new.reshape(local_req, tree, head_local, HD)
    tree_value = value_new.reshape(local_req, tree, head_local, HD)
    nodes = jnp.arange(tree, dtype=jnp.int32)
    reach = (parents[:, :, None] == nodes[None, None, :]).astype(jnp.float32) + jnp.eye(
        tree, dtype=jnp.float32
    )[None]
    for step in range(LEVELS.bit_length()):
        reach = jnp.minimum(jnp.einsum("rij,rjk->rik", reach, reach, precision=highest), 1.0)
    allowed = reach > 0.5
    group_variates = lax.dynamic_slice_in_dim(
        token_variates, req_slot * local_req * tree, local_req * tree, 0
    ).reshape(local_req, tree)
    tree_scores = (
        jnp.einsum("rihd,rjhd->rihj", tree_query, tree_key, preferred_element_type=jnp.float32)
        * scale
    )
    same_tree = group_variates[:, :, None] == group_variates[:, None, :]
    tree_scores = tree_scores + jnp.where(
        same_tree[:, :, None, :], same_bias[None, None, :, None], other_bias[None, None, :, None]
    )
    keep_tree = allowed[:, :, None, :]
    tree_max = jnp.max(jnp.where(keep_tree, tree_scores, masked_score), axis=-1)
    tree_weights = jnp.where(keep_tree, jnp.exp(tree_scores - tree_max[..., None]), 0.0).astype(
        jnp.bfloat16
    )
    tree_total = jnp.sum(tree_weights, axis=-1, dtype=jnp.float32)
    tree_out = jnp.einsum(
        "rihj,rjhd->rihd", tree_weights, tree_value, preferred_element_type=jnp.float32
    )
    final_max, final_total, final_out = merge_parts(cached_part, (tree_max, tree_total, tree_out))
    attended = (
        (final_out / final_total[..., None]).astype(jnp.bfloat16).reshape(local_req * tree, qdl)
    )
    group_rows = local_req * tree
    token_heads = (
        gather_rows(attended, "head", head_parts).transpose(1, 0, 2).reshape(group_rows, -1)
    )
    attention_rows = jnp.dot(token_heads, out_weight, preferred_element_type=jnp.float32)
    hidden_state = (group_tokens.astype(jnp.float32) + attention_rows).astype(jnp.bfloat16)
    normed_two = rms_scaled(hidden_state, gains[1]).astype(jnp.bfloat16)
    both_parts = jnp.einsum(
        "td,cdf->ctf",
        normed_two,
        gate_up_weight,
        preferred_element_type=jnp.float32,
    )
    activated = (jax.nn.silu(both_parts[0]) * both_parts[1]).astype(jnp.bfloat16)
    down_part = jnp.dot(activated, down_weight, preferred_element_type=jnp.float32).astype(
        jnp.bfloat16
    )
    own_rows = tokens.shape[0]
    down_parts = lax.all_to_all(
        down_part.reshape(head_parts, own_rows, -1), "head", 0, 0, tiled=True
    )
    ffn_rows = jnp.sum(down_parts.astype(jnp.float32), axis=0)
    own_hidden = lax.dynamic_slice_in_dim(hidden_state, head_slot * own_rows, own_rows, 0)
    mixed = (own_hidden.astype(jnp.float32) + ffn_rows).astype(jnp.bfloat16)
    chosen = (accepted[:, :, None] == nodes[None, None, :]).astype(jnp.bfloat16)
    stacked = jnp.stack([key_new, value_new]).reshape(2, local_req, tree, qdl)
    new_kv = jnp.einsum(
        "rat,crtq->craq", chosen, stacked, preferred_element_type=jnp.float32
    ).astype(jnp.bfloat16)
    return (mixed, attended, new_kv)


def solution(mesh):
    return jax.shard_map(
        shards,
        mesh=mesh,
        in_specs=(
            P(("req", "head"), None),
            P(),
            P(None, None, "head"),
            P(),
            P(None, None, "head"),
            P("head", None),
            P(),
            P(None, "req", None, "head"),
            P("req", None),
            P(),
            P(),
            P(),
            P("req", None),
            P("req", None),
        ),
        out_specs=(P(("req", "head"), None), P("req", "head"), P(None, "req", None, "head")),
        check_vma=False,
    )
```

```python
import functools
import math

import jax
import jax.numpy as jnp
from jax import lax
from jax.experimental import pallas as pl
from jax.experimental.pallas import tpu as pltpu
from jax.sharding import PartitionSpec as P

HD = 64
LEVELS = 8


epsilon = 1e-06
masked_score = -1e30
highest = lax.Precision.HIGHEST


def rms_scaled(rows, gain):
    values = rows.astype(jnp.float32)
    return values * lax.rsqrt(jnp.mean(values * values, axis=-1, keepdims=True) + epsilon) * gain


def merge_parts(first, second):
    max_one, total_one, out_one = first
    max_two, total_two, out_two = second
    highest_max = jnp.maximum(max_one, max_two)
    factor_one = jnp.exp(max_one - highest_max)
    factor_two = jnp.exp(max_two - highest_max)
    return (
        highest_max,
        total_one * factor_one + total_two * factor_two,
        out_one * factor_one[..., None] + out_two * factor_two[..., None],
    )


def page_kernel(owner_ref, filled_ref, q_ref, aux_ref, cache_ref, pv_ref,
                out_ref, out_acc, max_acc, total_acc,
                *, head_local, tree, scale, pool):
    rows, page = head_local * tree, cache_ref.shape[2]
    lanes = aux_ref.shape[0]
    out_acc[...] = jnp.zeros(out_acc.shape, jnp.float32)
    max_acc[...] = jnp.full(max_acc.shape, masked_score, jnp.float32)
    total_acc[...] = jnp.zeros(total_acc.shape, jnp.float32)
    request_lane = lax.broadcasted_iota(jnp.int32, max_acc.shape, 1)
    column_head = lax.broadcasted_iota(jnp.int32, out_acc.shape[1:], 1) // HD
    aux_columns = jnp.transpose(aux_ref[...])

    def column_of(index):
        return jnp.sum(jnp.where(request_lane == index, aux_columns, 0.0), axis=1, keepdims=True)

    same_bias = column_of(lanes - 2)
    other_bias = column_of(lanes - 1)

    def pick_heads(values):
        picked = jnp.zeros(out_acc.shape[1:], jnp.float32)
        for head in range(head_local):
            picked = picked + jnp.where(
                column_head == head, values[head * tree : (head + 1) * tree], 0.0
            )
        return picked

    def one_page(step, carry):
        count = filled_ref[step]

        @pl.when(count > 0)
        def _():
            row = owner_ref[step]
            same = column_of(row) == pv_ref[step]
            valid = lax.broadcasted_iota(jnp.int32, (rows, page), 1) < count
            query = q_ref[row]
            stacked = jnp.concatenate(
                [
                    jnp.where(column_head == head, query, jnp.zeros_like(query))
                    for head in range(head_local)
                ],
                axis=0,
            )
            scores = lax.dot_general(
                stacked, cache_ref[0, step], (((1,), (1,)), ((), ())),
                preferred_element_type=jnp.float32,
            ) * scale
            scores = scores + jnp.where(same, same_bias, other_bias)
            block_max = jnp.max(jnp.where(valid, scores, masked_score), axis=1, keepdims=True)
            weights = jnp.where(valid, jnp.exp(scores - block_max), 0.0).astype(jnp.bfloat16)
            block_total = jnp.sum(weights.astype(jnp.float32), axis=1, keepdims=True)
            crossed = jnp.dot(weights, cache_ref[1, step], preferred_element_type=jnp.float32)
            is_row = request_lane == row
            old_max = jnp.sum(jnp.where(is_row, max_acc[...], 0.0), axis=1, keepdims=True)
            old_total = jnp.sum(jnp.where(is_row, total_acc[...], 0.0), axis=1, keepdims=True)
            new_max = jnp.maximum(old_max, block_max)
            keep_old = jnp.exp(old_max - new_max)
            keep_new = jnp.exp(block_max - new_max)
            max_acc[...] = jnp.where(is_row, new_max, max_acc[...])
            total_acc[...] = jnp.where(
                is_row, old_total * keep_old + block_total * keep_new, total_acc[...]
            )
            out_acc[row] = out_acc[row] * pick_heads(
                jnp.broadcast_to(keep_old, crossed.shape)
            ) + pick_heads(crossed * keep_new)

        return carry

    lax.fori_loop(0, pool, one_page, 0)
    requests = out_ref.shape[0]
    out_ref[:, :tree, :] = out_acc[...].astype(out_ref.dtype)
    stats = (
        jnp.transpose(total_acc[...])[:requests],
        jnp.transpose(max_acc[...])[:requests],
    )
    for kind, values in enumerate(stats):
        for part in range(3):
            rounded = values.astype(out_ref.dtype)
            out_ref[:, tree + 2 * part + kind, :] = rounded
            values = values - rounded.astype(jnp.float32)


def page_attention(owner, filled, queries, row_variates, page_cache, page_variates,
                   row_bias, interpret=False):
    requests, tree, qdl = queries.shape
    pool, page = page_variates.shape
    head_local = qdl // HD
    rows = head_local * tree
    lanes = 128 * ((requests + 2 + 127) // 128)
    aux = jnp.concatenate(
        [
            row_variates.astype(jnp.float32),
            jnp.zeros((lanes - requests - 2, rows), jnp.float32),
            row_bias,
        ],
        axis=0,
    )
    kernel = functools.partial(
        page_kernel, head_local=head_local, tree=tree, scale=1.0 / math.sqrt(HD), pool=pool
    )

    def whole(shape):
        return pl.BlockSpec(shape, lambda step, *_: (0,) * len(shape))

    grid_spec = pltpu.PrefetchScalarGridSpec(
        num_scalar_prefetch=2,
        grid=(1,),
        in_specs=[
            whole((requests, tree, qdl)),
            whole((lanes, rows)),
            whole(page_cache.shape),
            whole((pool, 1, page)),
        ],
        out_specs=whole((requests, tree + 6, qdl)),
        scratch_shapes=[
            pltpu.VMEM((requests, tree, qdl), jnp.float32),
            pltpu.VMEM((rows, lanes), jnp.float32),
            pltpu.VMEM((rows, lanes), jnp.float32),
        ],
    )
    return pl.pallas_call(
        kernel,
        grid_spec=grid_spec,
        out_shape=jax.ShapeDtypeStruct((requests, tree + 6, qdl), jnp.bfloat16),
        compiler_params=pltpu.CompilerParams(dimension_semantics=("arbitrary",)),
        interpret=interpret,
    )(owner, filled, queries, aux, page_cache, page_variates[:, None, :])


def join_three(high, middle, low):
    return (high.astype(jnp.float32) + middle.astype(jnp.float32)) + low.astype(jnp.float32)


def gather_rows(rows, axis_name, parts):
    spread = jnp.broadcast_to(rows[None], (parts,) + rows.shape)
    return lax.all_to_all(spread, axis_name, 0, 0, tiled=True)


def shards(
    tokens,
    gains,
    qkv_weight,
    out_weight,
    gate_up_weight,
    down_weight,
    variate_bias,
    page_cache,
    page_variates,
    token_variates,
    cache_len,
    page_table,
    parents,
    accepted,
):
    scale = 1.0 / math.sqrt(HD)
    local_req, tree = parents.shape
    pool, page = page_variates.shape
    requests = cache_len.shape[0]
    qdl = qkv_weight.shape[2]
    head_local = qdl // HD
    head_slot = lax.axis_index("head")
    req_slot = lax.axis_index("req")
    bias_local = lax.dynamic_slice_in_dim(variate_bias, head_slot * head_local, head_local, 1)
    same_bias = bias_local[0]
    other_bias = bias_local[1]
    head_parts = lax.axis_size("head")
    group_tokens = gather_rows(tokens, "head", head_parts).reshape(-1, tokens.shape[1])
    normed = rms_scaled(group_tokens, gains[0]).astype(jnp.bfloat16)
    projected = jnp.einsum(
        "td,cdq->ctq",
        normed,
        qkv_weight,
        preferred_element_type=jnp.float32,
    ).astype(jnp.bfloat16)
    query = projected[0]
    key_new = projected[1]
    value_new = projected[2]
    all_queries = gather_rows(query, "req", requests // local_req)
    global_ids = req_slot * pool + jnp.arange(pool, dtype=jnp.int32)
    matching = (page_table[:, :, None] == global_ids[None, None, :]).astype(jnp.int32)
    owner = jnp.sum(matching * jnp.arange(requests, dtype=jnp.int32)[:, None, None], axis=(0, 1))
    page_order = jnp.sum(
        matching * jnp.arange(page_table.shape[1], dtype=jnp.int32)[None, :, None], axis=(0, 1)
    )
    owner_len = jnp.sum(matching * cache_len[:, None, None], axis=(0, 1))
    in_use = jnp.sum(matching, axis=(0, 1))
    filled = jnp.clip(owner_len - page_order * page, 0, page) * in_use
    valid = jnp.arange(page, dtype=jnp.int32)[None, :] < filled[:, None]
    head_of_column = jnp.arange(qdl, dtype=jnp.int32) // HD
    head_mask = jnp.arange(head_local, dtype=jnp.int32)[:, None] == head_of_column[None, :]
    split_rows = head_local * tree
    row_variates = jnp.broadcast_to(
        token_variates.reshape(requests, 1, tree), (requests, head_local, tree)
    ).reshape(requests, split_rows)
    row_bias = jnp.broadcast_to(bias_local[:, :, None], (2, head_local, tree)).reshape(
        2, split_rows
    )
    packed = page_attention(
        jnp.clip(owner, 0, requests - 1),
        filled,
        all_queries.reshape(requests, tree, qdl),
        row_variates,
        page_cache,
        page_variates,
        row_bias,
    )
    received = lax.all_to_all(packed, "req", split_axis=0, concat_axis=0, tiled=True)
    sources = lax.axis_size("req")
    received = received.reshape((sources, local_req) + packed.shape[1:])
    source_out = received[:, :, :tree].astype(jnp.float32)
    got_stats = join_three(
        *[received[:, :, tree + 2 * part : tree + 2 * part + 2] for part in range(3)]
    )
    source_total = got_stats[:, :, 0].reshape(sources, local_req, head_local, tree)
    source_max = got_stats[:, :, 1].reshape(sources, local_req, head_local, tree)
    largest = jnp.max(source_max, axis=0)
    source_factor = jnp.exp(source_max - largest[None])
    column_factor = jnp.sum(
        jnp.where(head_mask[None, None, :, None, :], source_factor[..., None], 0.0), axis=2
    )
    cached_part = (
        largest.transpose(0, 2, 1),
        jnp.sum(source_total * source_factor, axis=0).transpose(0, 2, 1),
        jnp.sum(source_out * column_factor, axis=0).reshape(local_req, tree, head_local, HD),
    )
    tree_query = query.reshape(local_req, tree, head_local, HD)
    tree_key = key_new.reshape(local_req, tree, head_local, HD)
    tree_value = value_new.reshape(local_req, tree, head_local, HD)
    nodes = jnp.arange(tree, dtype=jnp.int32)
    reach = (parents[:, :, None] == nodes[None, None, :]).astype(jnp.float32) + jnp.eye(
        tree, dtype=jnp.float32
    )[None]
    for step in range(LEVELS.bit_length()):
        reach = jnp.minimum(jnp.einsum("rij,rjk->rik", reach, reach, precision=highest), 1.0)
    allowed = reach > 0.5
    group_variates = lax.dynamic_slice_in_dim(
        token_variates, req_slot * local_req * tree, local_req * tree, 0
    ).reshape(local_req, tree)
    tree_scores = (
        jnp.einsum("rihd,rjhd->rihj", tree_query, tree_key, preferred_element_type=jnp.float32)
        * scale
    )
    same_tree = group_variates[:, :, None] == group_variates[:, None, :]
    tree_scores = tree_scores + jnp.where(
        same_tree[:, :, None, :], same_bias[None, None, :, None], other_bias[None, None, :, None]
    )
    keep_tree = allowed[:, :, None, :]
    tree_max = jnp.max(jnp.where(keep_tree, tree_scores, masked_score), axis=-1)
    tree_weights = jnp.where(keep_tree, jnp.exp(tree_scores - tree_max[..., None]), 0.0).astype(
        jnp.bfloat16
    )
    tree_total = jnp.sum(tree_weights, axis=-1, dtype=jnp.float32)
    tree_out = jnp.einsum(
        "rihj,rjhd->rihd", tree_weights, tree_value, preferred_element_type=jnp.float32
    )
    final_max, final_total, final_out = merge_parts(cached_part, (tree_max, tree_total, tree_out))
    attended = (
        (final_out / final_total[..., None]).astype(jnp.bfloat16).reshape(local_req * tree, qdl)
    )
    group_rows = local_req * tree
    token_heads = (
        gather_rows(attended, "head", head_parts).transpose(1, 0, 2).reshape(group_rows, -1)
    )
    attention_rows = jnp.dot(token_heads, out_weight, preferred_element_type=jnp.float32)
    hidden_state = (group_tokens.astype(jnp.float32) + attention_rows).astype(jnp.bfloat16)
    normed_two = rms_scaled(hidden_state, gains[1]).astype(jnp.bfloat16)
    both_parts = jnp.einsum(
        "td,cdf->ctf",
        normed_two,
        gate_up_weight,
        preferred_element_type=jnp.float32,
    )
    activated = (jax.nn.silu(both_parts[0]) * both_parts[1]).astype(jnp.bfloat16)
    down_part = jnp.dot(activated, down_weight, preferred_element_type=jnp.float32).astype(
        jnp.bfloat16
    )
    own_rows = tokens.shape[0]
    down_parts = lax.all_to_all(
        down_part.reshape(head_parts, own_rows, -1), "head", 0, 0, tiled=True
    )
    ffn_rows = jnp.sum(down_parts.astype(jnp.float32), axis=0)
    own_hidden = lax.dynamic_slice_in_dim(hidden_state, head_slot * own_rows, own_rows, 0)
    mixed = (own_hidden.astype(jnp.float32) + ffn_rows).astype(jnp.bfloat16)
    chosen = (accepted[:, :, None] == nodes[None, None, :]).astype(jnp.bfloat16)
    stacked = jnp.stack([key_new, value_new]).reshape(2, local_req, tree, qdl)
    new_kv = jnp.einsum(
        "rat,crtq->craq", chosen, stacked, preferred_element_type=jnp.float32
    ).astype(jnp.bfloat16)
    return (mixed, attended, new_kv)


def solution(mesh):
    return jax.shard_map(
        shards,
        mesh=mesh,
        in_specs=(
            P(("req", "head"), None),
            P(),
            P(None, None, "head"),
            P(),
            P(None, None, "head"),
            P("head", None),
            P(),
            P(None, "req", None, "head"),
            P("req", None),
            P(),
            P(),
            P(),
            P("req", None),
            P("req", None),
        ),
        out_specs=(P(("req", "head"), None), P("req", "head"), P(None, "req", None, "head")),
        check_vma=False,
    )
```

```python
import functools
import math

import jax
import jax.numpy as jnp
from jax import lax
from jax.experimental import pallas as pl
from jax.experimental.pallas import tpu as pltpu
from jax.sharding import PartitionSpec as P

HD = 64
LEVELS = 8


epsilon = 1e-06
masked_score = -1e30
highest = lax.Precision.HIGHEST


def rms_scaled(rows, gain):
    values = rows.astype(jnp.float32)
    return values * lax.rsqrt(jnp.mean(values * values, axis=-1, keepdims=True) + epsilon) * gain


def merge_parts(first, second):
    max_one, total_one, out_one = first
    max_two, total_two, out_two = second
    highest_max = jnp.maximum(max_one, max_two)
    factor_one = jnp.exp(max_one - highest_max)
    factor_two = jnp.exp(max_two - highest_max)
    return (
        highest_max,
        total_one * factor_one + total_two * factor_two,
        out_one * factor_one[..., None] + out_two * factor_two[..., None],
    )


def page_kernel(owner_ref, filled_ref, q_ref, aux_ref, cache_ref, pv_ref,
                out_ref, out_acc, max_acc, total_acc,
                *, head_local, tree, scale, pool):
    rows, page = head_local * tree, cache_ref.shape[2]
    lanes = aux_ref.shape[0]
    out_acc[...] = jnp.zeros(out_acc.shape, jnp.float32)
    max_acc[...] = jnp.full(max_acc.shape, masked_score, jnp.float32)
    total_acc[...] = jnp.zeros(total_acc.shape, jnp.float32)
    request_lane = lax.broadcasted_iota(jnp.int32, max_acc.shape, 1)
    column_head = lax.broadcasted_iota(jnp.int32, out_acc.shape[1:], 1) // HD
    aux_columns = jnp.transpose(aux_ref[...])

    def column_of(index):
        return jnp.sum(jnp.where(request_lane == index, aux_columns, 0.0), axis=1, keepdims=True)

    same_bias = column_of(lanes - 2)
    other_bias = column_of(lanes - 1)

    def pick_heads(values):
        picked = jnp.zeros(out_acc.shape[1:], jnp.float32)
        for head in range(head_local):
            picked = picked + jnp.where(
                column_head == head, values[head * tree : (head + 1) * tree], 0.0
            )
        return picked

    def one_page(step, carry):
        count = filled_ref[step]

        @pl.when(count > 0)
        def _():
            row = owner_ref[step]
            same = column_of(row) == pv_ref[step]
            valid = lax.broadcasted_iota(jnp.int32, (rows, page), 1) < count
            query = q_ref[row]
            stacked = jnp.concatenate(
                [
                    jnp.where(column_head == head, query, jnp.zeros_like(query))
                    for head in range(head_local)
                ],
                axis=0,
            )
            scores = lax.dot_general(
                stacked, cache_ref[0, step], (((1,), (1,)), ((), ())),
                preferred_element_type=jnp.float32,
            ) * scale
            scores = scores + jnp.where(same, same_bias, other_bias)
            block_max = jnp.max(jnp.where(valid, scores, masked_score), axis=1, keepdims=True)
            weights = jnp.where(valid, jnp.exp(scores - block_max), 0.0).astype(jnp.bfloat16)
            block_total = jnp.sum(weights.astype(jnp.float32), axis=1, keepdims=True)
            crossed = jnp.dot(weights, cache_ref[1, step], preferred_element_type=jnp.float32)
            is_row = request_lane == row
            old_max = jnp.sum(jnp.where(is_row, max_acc[...], 0.0), axis=1, keepdims=True)
            old_total = jnp.sum(jnp.where(is_row, total_acc[...], 0.0), axis=1, keepdims=True)
            new_max = jnp.maximum(old_max, block_max)
            keep_old = jnp.exp(old_max - new_max)
            keep_new = jnp.exp(block_max - new_max)
            max_acc[...] = jnp.where(is_row, new_max, max_acc[...])
            total_acc[...] = jnp.where(
                is_row, old_total * keep_old + block_total * keep_new, total_acc[...]
            )
            out_acc[row] = out_acc[row] * pick_heads(
                jnp.broadcast_to(keep_old, crossed.shape)
            ) + pick_heads(crossed * keep_new)

        return carry

    lax.fori_loop(0, pool, one_page, 0)
    requests = out_ref.shape[0]
    out_ref[:, :tree, :] = out_acc[...].astype(out_ref.dtype)
    stats = (
        jnp.transpose(total_acc[...])[:requests],
        jnp.transpose(max_acc[...])[:requests],
    )
    for kind, values in enumerate(stats):
        for part in range(3):
            rounded = values.astype(out_ref.dtype)
            out_ref[:, tree + 2 * part + kind, :] = rounded
            values = values - rounded.astype(jnp.float32)


def page_attention(owner, filled, queries, row_variates, page_cache, page_variates,
                   row_bias, interpret=False):
    requests, tree, qdl = queries.shape
    pool, page = page_variates.shape
    head_local = qdl // HD
    rows = head_local * tree
    lanes = 128 * ((requests + 2 + 127) // 128)
    aux = jnp.concatenate(
        [
            row_variates.astype(jnp.float32),
            jnp.zeros((lanes - requests - 2, rows), jnp.float32),
            row_bias,
        ],
        axis=0,
    )
    kernel = functools.partial(
        page_kernel, head_local=head_local, tree=tree, scale=1.0 / math.sqrt(HD), pool=pool
    )

    def whole(shape):
        return pl.BlockSpec(shape, lambda step, *_: (0,) * len(shape))

    grid_spec = pltpu.PrefetchScalarGridSpec(
        num_scalar_prefetch=2,
        grid=(1,),
        in_specs=[
            whole((requests, tree, qdl)),
            whole((lanes, rows)),
            whole(page_cache.shape),
            whole((pool, 1, page)),
        ],
        out_specs=whole((requests, tree + 6, qdl)),
        scratch_shapes=[
            pltpu.VMEM((requests, tree, qdl), jnp.float32),
            pltpu.VMEM((rows, lanes), jnp.float32),
            pltpu.VMEM((rows, lanes), jnp.float32),
        ],
    )
    return pl.pallas_call(
        kernel,
        grid_spec=grid_spec,
        out_shape=jax.ShapeDtypeStruct((requests, tree + 6, qdl), jnp.bfloat16),
        compiler_params=pltpu.CompilerParams(dimension_semantics=("arbitrary",)),
        interpret=interpret,
    )(owner, filled, queries, aux, page_cache, page_variates[:, None, :])


def join_three(high, middle, low):
    return (high.astype(jnp.float32) + middle.astype(jnp.float32)) + low.astype(jnp.float32)


def gather_rows(rows, axis_name, parts):
    spread = jnp.broadcast_to(rows[None], (parts,) + rows.shape)
    return lax.all_to_all(spread, axis_name, 0, 0, tiled=True)


def shards(
    tokens,
    gains,
    qkv_weight,
    out_weight,
    gate_up_weight,
    down_weight,
    variate_bias,
    page_cache,
    page_variates,
    token_variates,
    cache_len,
    page_table,
    parents,
    accepted,
):
    scale = 1.0 / math.sqrt(HD)
    local_req, tree = parents.shape
    pool, page = page_variates.shape
    requests = cache_len.shape[0]
    qdl = qkv_weight.shape[2]
    head_local = qdl // HD
    head_slot = lax.axis_index("head")
    req_slot = lax.axis_index("req")
    bias_local = lax.dynamic_slice_in_dim(variate_bias, head_slot * head_local, head_local, 1)
    same_bias = bias_local[0]
    other_bias = bias_local[1]
    head_parts = lax.axis_size("head")
    lane_rows = tokens.shape[0] * tokens.shape[1] // 128
    group_tokens = gather_rows(tokens.reshape(lane_rows, 128), "head", head_parts).reshape(
        -1, tokens.shape[1]
    )
    normed = rms_scaled(group_tokens, gains[0]).astype(jnp.bfloat16)
    projected = jnp.einsum(
        "td,cdq->ctq",
        normed,
        qkv_weight,
        preferred_element_type=jnp.float32,
    ).astype(jnp.bfloat16)
    query = projected[0]
    key_new = projected[1]
    value_new = projected[2]
    all_queries = gather_rows(query, "req", requests // local_req)
    global_ids = req_slot * pool + jnp.arange(pool, dtype=jnp.int32)
    matching = (page_table[:, :, None] == global_ids[None, None, :]).astype(jnp.int32)
    owner = jnp.sum(matching * jnp.arange(requests, dtype=jnp.int32)[:, None, None], axis=(0, 1))
    page_order = jnp.sum(
        matching * jnp.arange(page_table.shape[1], dtype=jnp.int32)[None, :, None], axis=(0, 1)
    )
    owner_len = jnp.sum(matching * cache_len[:, None, None], axis=(0, 1))
    in_use = jnp.sum(matching, axis=(0, 1))
    filled = jnp.clip(owner_len - page_order * page, 0, page) * in_use
    valid = jnp.arange(page, dtype=jnp.int32)[None, :] < filled[:, None]
    head_of_column = jnp.arange(qdl, dtype=jnp.int32) // HD
    head_mask = jnp.arange(head_local, dtype=jnp.int32)[:, None] == head_of_column[None, :]
    split_rows = head_local * tree
    row_variates = jnp.broadcast_to(
        token_variates.reshape(requests, 1, tree), (requests, head_local, tree)
    ).reshape(requests, split_rows)
    row_bias = jnp.broadcast_to(bias_local[:, :, None], (2, head_local, tree)).reshape(
        2, split_rows
    )
    packed = page_attention(
        jnp.clip(owner, 0, requests - 1),
        filled,
        all_queries.reshape(requests, tree, qdl),
        row_variates,
        page_cache,
        page_variates,
        row_bias,
    )
    received = lax.all_to_all(packed, "req", split_axis=0, concat_axis=0, tiled=True)
    sources = lax.axis_size("req")
    received = received.reshape((sources, local_req) + packed.shape[1:])
    source_out = received[:, :, :tree].astype(jnp.float32)
    got_stats = join_three(
        *[received[:, :, tree + 2 * part : tree + 2 * part + 2] for part in range(3)]
    )
    source_total = got_stats[:, :, 0].reshape(sources, local_req, head_local, tree)
    source_max = got_stats[:, :, 1].reshape(sources, local_req, head_local, tree)
    largest = jnp.max(source_max, axis=0)
    source_factor = jnp.exp(source_max - largest[None])
    column_factor = jnp.sum(
        jnp.where(head_mask[None, None, :, None, :], source_factor[..., None], 0.0), axis=2
    )
    cached_part = (
        largest.transpose(0, 2, 1),
        jnp.sum(source_total * source_factor, axis=0).transpose(0, 2, 1),
        jnp.sum(source_out * column_factor, axis=0).reshape(local_req, tree, head_local, HD),
    )
    tree_query = query.reshape(local_req, tree, head_local, HD)
    tree_key = key_new.reshape(local_req, tree, head_local, HD)
    tree_value = value_new.reshape(local_req, tree, head_local, HD)
    nodes = jnp.arange(tree, dtype=jnp.int32)
    reach = (parents[:, :, None] == nodes[None, None, :]).astype(jnp.float32) + jnp.eye(
        tree, dtype=jnp.float32
    )[None]
    for step in range(LEVELS.bit_length()):
        reach = jnp.minimum(jnp.einsum("rij,rjk->rik", reach, reach, precision=highest), 1.0)
    allowed = reach > 0.5
    group_variates = lax.dynamic_slice_in_dim(
        token_variates, req_slot * local_req * tree, local_req * tree, 0
    ).reshape(local_req, tree)
    tree_scores = (
        jnp.einsum("rihd,rjhd->rihj", tree_query, tree_key, preferred_element_type=jnp.float32)
        * scale
    )
    same_tree = group_variates[:, :, None] == group_variates[:, None, :]
    tree_scores = tree_scores + jnp.where(
        same_tree[:, :, None, :], same_bias[None, None, :, None], other_bias[None, None, :, None]
    )
    keep_tree = allowed[:, :, None, :]
    tree_max = jnp.max(jnp.where(keep_tree, tree_scores, masked_score), axis=-1)
    tree_weights = jnp.where(keep_tree, jnp.exp(tree_scores - tree_max[..., None]), 0.0).astype(
        jnp.bfloat16
    )
    tree_total = jnp.sum(tree_weights, axis=-1, dtype=jnp.float32)
    tree_out = jnp.einsum(
        "rihj,rjhd->rihd", tree_weights, tree_value, preferred_element_type=jnp.float32
    )
    final_max, final_total, final_out = merge_parts(cached_part, (tree_max, tree_total, tree_out))
    attended = (
        (final_out / final_total[..., None]).astype(jnp.bfloat16).reshape(local_req * tree, qdl)
    )
    group_rows = local_req * tree
    token_heads = (
        gather_rows(attended, "head", head_parts).transpose(1, 0, 2).reshape(group_rows, -1)
    )
    attention_rows = jnp.dot(token_heads, out_weight, preferred_element_type=jnp.float32)
    hidden_state = (group_tokens.astype(jnp.float32) + attention_rows).astype(jnp.bfloat16)
    normed_two = rms_scaled(hidden_state, gains[1]).astype(jnp.bfloat16)
    both_parts = jnp.einsum(
        "td,cdf->ctf",
        normed_two,
        gate_up_weight,
        preferred_element_type=jnp.float32,
    )
    activated = (jax.nn.silu(both_parts[0]) * both_parts[1]).astype(jnp.bfloat16)
    down_part = jnp.dot(activated, down_weight, preferred_element_type=jnp.float32).astype(
        jnp.bfloat16
    )
    own_rows = tokens.shape[0]
    down_parts = lax.all_to_all(
        down_part.reshape(head_parts, lane_rows, 128), "head", 0, 0, tiled=True
    )
    ffn_rows = jnp.sum(down_parts.astype(jnp.float32), axis=0).reshape(own_rows, -1)
    own_hidden = lax.dynamic_slice_in_dim(hidden_state, head_slot * own_rows, own_rows, 0)
    mixed = (own_hidden.astype(jnp.float32) + ffn_rows).astype(jnp.bfloat16)
    chosen = (accepted[:, :, None] == nodes[None, None, :]).astype(jnp.bfloat16)
    stacked = jnp.stack([key_new, value_new]).reshape(2, local_req, tree, qdl)
    new_kv = jnp.einsum(
        "rat,crtq->craq", chosen, stacked, preferred_element_type=jnp.float32
    ).astype(jnp.bfloat16)
    return (mixed, attended, new_kv)


def solution(mesh):
    return jax.shard_map(
        shards,
        mesh=mesh,
        in_specs=(
            P(("req", "head"), None),
            P(),
            P(None, None, "head"),
            P(),
            P(None, None, "head"),
            P("head", None),
            P(),
            P(None, "req", None, "head"),
            P("req", None),
            P(),
            P(),
            P(),
            P("req", None),
            P("req", None),
        ),
        out_specs=(P(("req", "head"), None), P("req", "head"), P(None, "req", None, "head")),
        check_vma=False,
    )
```

```python
import functools
import math

import jax
import jax.numpy as jnp
from jax import lax
from jax.experimental import pallas as pl
from jax.experimental.pallas import tpu as pltpu
from jax.sharding import PartitionSpec as P

HD = 64
LEVELS = 8


epsilon = 1e-06
masked_score = -1e30
highest = lax.Precision.HIGHEST


def rms_scaled(rows, gain):
    values = rows.astype(jnp.float32)
    return values * lax.rsqrt(jnp.mean(values * values, axis=-1, keepdims=True) + epsilon) * gain


def merge_parts(first, second):
    max_one, total_one, out_one = first
    max_two, total_two, out_two = second
    highest_max = jnp.maximum(max_one, max_two)
    factor_one = jnp.exp(max_one - highest_max)
    factor_two = jnp.exp(max_two - highest_max)
    return (
        highest_max,
        total_one * factor_one + total_two * factor_two,
        out_one * factor_one[..., None] + out_two * factor_two[..., None],
    )


def page_kernel(owner_ref, filled_ref, q_ref, aux_ref, cache_ref, pv_ref,
                out_ref, out_acc, max_acc, total_acc,
                *, head_local, tree, scale, pool):
    rows, page = head_local * tree, cache_ref.shape[2]
    lanes = aux_ref.shape[0]
    out_acc[...] = jnp.zeros(out_acc.shape, jnp.float32)
    max_acc[...] = jnp.full(max_acc.shape, masked_score, jnp.float32)
    total_acc[...] = jnp.zeros(total_acc.shape, jnp.float32)
    request_lane = lax.broadcasted_iota(jnp.int32, max_acc.shape, 1)
    column_head = lax.broadcasted_iota(jnp.int32, out_acc.shape[1:], 1) // HD
    aux_columns = jnp.transpose(aux_ref[...])

    def column_of(index):
        return jnp.sum(jnp.where(request_lane == index, aux_columns, 0.0), axis=1, keepdims=True)

    same_bias = column_of(lanes - 2)
    other_bias = column_of(lanes - 1)

    def pick_heads(values):
        picked = jnp.zeros(out_acc.shape[1:], jnp.float32)
        for head in range(head_local):
            picked = picked + jnp.where(
                column_head == head, values[head * tree : (head + 1) * tree], 0.0
            )
        return picked

    def one_page(step, carry):
        count = filled_ref[step]

        row = owner_ref[step]
        same = column_of(row) == pv_ref[step]
        valid = lax.broadcasted_iota(jnp.int32, (rows, page), 1) < count
        query = q_ref[row]
        stacked = jnp.concatenate(
            [
                jnp.where(column_head == head, query, jnp.zeros_like(query))
                for head in range(head_local)
            ],
            axis=0,
        )
        scores = lax.dot_general(
            stacked, cache_ref[0, step], (((1,), (1,)), ((), ())),
            preferred_element_type=jnp.float32,
        ) * scale
        scores = scores + jnp.where(same, same_bias, other_bias)
        block_max = jnp.max(jnp.where(valid, scores, masked_score), axis=1, keepdims=True)
        weights = jnp.where(valid, jnp.exp(scores - block_max), 0.0).astype(jnp.bfloat16)
        block_total = jnp.sum(weights.astype(jnp.float32), axis=1, keepdims=True)
        crossed = jnp.dot(weights, cache_ref[1, step], preferred_element_type=jnp.float32)
        is_row = request_lane == row
        old_max = jnp.sum(jnp.where(is_row, max_acc[...], 0.0), axis=1, keepdims=True)
        old_total = jnp.sum(jnp.where(is_row, total_acc[...], 0.0), axis=1, keepdims=True)
        new_max = jnp.maximum(old_max, block_max)
        keep_old = jnp.exp(old_max - new_max)
        keep_new = jnp.exp(block_max - new_max)
        max_acc[...] = jnp.where(is_row, new_max, max_acc[...])
        total_acc[...] = jnp.where(
            is_row, old_total * keep_old + block_total * keep_new, total_acc[...]
        )
        out_acc[row] = out_acc[row] * pick_heads(
            jnp.broadcast_to(keep_old, crossed.shape)
        ) + pick_heads(crossed * keep_new)

        return carry

    lax.fori_loop(0, pool, one_page, 0, unroll=True)
    requests = out_ref.shape[0]
    out_ref[:, :tree, :] = out_acc[...].astype(out_ref.dtype)
    stats = (
        jnp.transpose(total_acc[...])[:requests],
        jnp.transpose(max_acc[...])[:requests],
    )
    for kind, values in enumerate(stats):
        for part in range(3):
            rounded = values.astype(out_ref.dtype)
            out_ref[:, tree + 2 * part + kind, :] = rounded
            values = values - rounded.astype(jnp.float32)


def page_attention(owner, filled, queries, row_variates, page_cache, page_variates,
                   row_bias, interpret=False):
    requests, tree, qdl = queries.shape
    pool, page = page_variates.shape
    head_local = qdl // HD
    rows = head_local * tree
    lanes = 128 * ((requests + 2 + 127) // 128)
    aux = jnp.concatenate(
        [
            row_variates.astype(jnp.float32),
            jnp.zeros((lanes - requests - 2, rows), jnp.float32),
            row_bias,
        ],
        axis=0,
    )
    kernel = functools.partial(
        page_kernel, head_local=head_local, tree=tree, scale=1.0 / math.sqrt(HD), pool=pool
    )

    def whole(shape):
        return pl.BlockSpec(shape, lambda step, *_: (0,) * len(shape))

    grid_spec = pltpu.PrefetchScalarGridSpec(
        num_scalar_prefetch=2,
        grid=(1,),
        in_specs=[
            whole((requests, tree, qdl)),
            whole((lanes, rows)),
            whole(page_cache.shape),
            whole((pool, 1, page)),
        ],
        out_specs=whole((requests, tree + 6, qdl)),
        scratch_shapes=[
            pltpu.VMEM((requests, tree, qdl), jnp.float32),
            pltpu.VMEM((rows, lanes), jnp.float32),
            pltpu.VMEM((rows, lanes), jnp.float32),
        ],
    )
    return pl.pallas_call(
        kernel,
        grid_spec=grid_spec,
        out_shape=jax.ShapeDtypeStruct((requests, tree + 6, qdl), jnp.bfloat16),
        compiler_params=pltpu.CompilerParams(dimension_semantics=("arbitrary",)),
        interpret=interpret,
    )(owner, filled, queries, aux, page_cache, page_variates[:, None, :])


def join_three(high, middle, low):
    return (high.astype(jnp.float32) + middle.astype(jnp.float32)) + low.astype(jnp.float32)


def gather_rows(rows, axis_name, parts):
    spread = jnp.broadcast_to(rows[None], (parts,) + rows.shape)
    return lax.all_to_all(spread, axis_name, 0, 0, tiled=True)


def shards(
    tokens,
    gains,
    qkv_weight,
    out_weight,
    gate_up_weight,
    down_weight,
    variate_bias,
    page_cache,
    page_variates,
    token_variates,
    cache_len,
    page_table,
    parents,
    accepted,
):
    scale = 1.0 / math.sqrt(HD)
    local_req, tree = parents.shape
    pool, page = page_variates.shape
    requests = cache_len.shape[0]
    qdl = qkv_weight.shape[2]
    head_local = qdl // HD
    head_slot = lax.axis_index("head")
    req_slot = lax.axis_index("req")
    bias_local = lax.dynamic_slice_in_dim(variate_bias, head_slot * head_local, head_local, 1)
    same_bias = bias_local[0]
    other_bias = bias_local[1]
    head_parts = lax.axis_size("head")
    group_tokens = gather_rows(tokens, "head", head_parts).reshape(-1, tokens.shape[1])
    normed = rms_scaled(group_tokens, gains[0]).astype(jnp.bfloat16)
    projected = jnp.einsum(
        "td,cdq->ctq",
        normed,
        qkv_weight,
        preferred_element_type=jnp.float32,
    ).astype(jnp.bfloat16)
    query = projected[0]
    key_new = projected[1]
    value_new = projected[2]
    all_queries = gather_rows(query, "req", requests // local_req)
    global_ids = req_slot * pool + jnp.arange(pool, dtype=jnp.int32)
    matching = (page_table[:, :, None] == global_ids[None, None, :]).astype(jnp.int32)
    owner = jnp.sum(matching * jnp.arange(requests, dtype=jnp.int32)[:, None, None], axis=(0, 1))
    page_order = jnp.sum(
        matching * jnp.arange(page_table.shape[1], dtype=jnp.int32)[None, :, None], axis=(0, 1)
    )
    owner_len = jnp.sum(matching * cache_len[:, None, None], axis=(0, 1))
    in_use = jnp.sum(matching, axis=(0, 1))
    filled = jnp.clip(owner_len - page_order * page, 0, page) * in_use
    valid = jnp.arange(page, dtype=jnp.int32)[None, :] < filled[:, None]
    head_of_column = jnp.arange(qdl, dtype=jnp.int32) // HD
    head_mask = jnp.arange(head_local, dtype=jnp.int32)[:, None] == head_of_column[None, :]
    split_rows = head_local * tree
    row_variates = jnp.broadcast_to(
        token_variates.reshape(requests, 1, tree), (requests, head_local, tree)
    ).reshape(requests, split_rows)
    row_bias = jnp.broadcast_to(bias_local[:, :, None], (2, head_local, tree)).reshape(
        2, split_rows
    )
    packed = page_attention(
        jnp.clip(owner, 0, requests - 1),
        filled,
        all_queries.reshape(requests, tree, qdl),
        row_variates,
        page_cache,
        page_variates,
        row_bias,
    )
    received = lax.all_to_all(packed, "req", split_axis=0, concat_axis=0, tiled=True)
    sources = lax.axis_size("req")
    received = received.reshape((sources, local_req) + packed.shape[1:])
    source_out = received[:, :, :tree].astype(jnp.float32)
    got_stats = join_three(
        *[received[:, :, tree + 2 * part : tree + 2 * part + 2] for part in range(3)]
    )
    source_total = got_stats[:, :, 0].reshape(sources, local_req, head_local, tree)
    source_max = got_stats[:, :, 1].reshape(sources, local_req, head_local, tree)
    largest = jnp.max(source_max, axis=0)
    source_factor = jnp.exp(source_max - largest[None])
    column_factor = jnp.sum(
        jnp.where(head_mask[None, None, :, None, :], source_factor[..., None], 0.0), axis=2
    )
    cached_part = (
        largest.transpose(0, 2, 1),
        jnp.sum(source_total * source_factor, axis=0).transpose(0, 2, 1),
        jnp.sum(source_out * column_factor, axis=0).reshape(local_req, tree, head_local, HD),
    )
    tree_query = query.reshape(local_req, tree, head_local, HD)
    tree_key = key_new.reshape(local_req, tree, head_local, HD)
    tree_value = value_new.reshape(local_req, tree, head_local, HD)
    nodes = jnp.arange(tree, dtype=jnp.int32)
    reach = (parents[:, :, None] == nodes[None, None, :]).astype(jnp.float32) + jnp.eye(
        tree, dtype=jnp.float32
    )[None]
    for step in range(LEVELS.bit_length()):
        reach = jnp.minimum(jnp.einsum("rij,rjk->rik", reach, reach, precision=highest), 1.0)
    allowed = reach > 0.5
    group_variates = lax.dynamic_slice_in_dim(
        token_variates, req_slot * local_req * tree, local_req * tree, 0
    ).reshape(local_req, tree)
    tree_scores = (
        jnp.einsum("rihd,rjhd->rihj", tree_query, tree_key, preferred_element_type=jnp.float32)
        * scale
    )
    same_tree = group_variates[:, :, None] == group_variates[:, None, :]
    tree_scores = tree_scores + jnp.where(
        same_tree[:, :, None, :], same_bias[None, None, :, None], other_bias[None, None, :, None]
    )
    keep_tree = allowed[:, :, None, :]
    tree_max = jnp.max(jnp.where(keep_tree, tree_scores, masked_score), axis=-1)
    tree_weights = jnp.where(keep_tree, jnp.exp(tree_scores - tree_max[..., None]), 0.0).astype(
        jnp.bfloat16
    )
    tree_total = jnp.sum(tree_weights, axis=-1, dtype=jnp.float32)
    tree_out = jnp.einsum(
        "rihj,rjhd->rihd", tree_weights, tree_value, preferred_element_type=jnp.float32
    )
    final_max, final_total, final_out = merge_parts(cached_part, (tree_max, tree_total, tree_out))
    attended = (
        (final_out / final_total[..., None]).astype(jnp.bfloat16).reshape(local_req * tree, qdl)
    )
    group_rows = local_req * tree
    token_heads = (
        gather_rows(attended, "head", head_parts).transpose(1, 0, 2).reshape(group_rows, -1)
    )
    attention_rows = jnp.dot(token_heads, out_weight, preferred_element_type=jnp.float32)
    hidden_state = (group_tokens.astype(jnp.float32) + attention_rows).astype(jnp.bfloat16)
    normed_two = rms_scaled(hidden_state, gains[1]).astype(jnp.bfloat16)
    both_parts = jnp.einsum(
        "td,cdf->ctf",
        normed_two,
        gate_up_weight,
        preferred_element_type=jnp.float32,
    )
    activated = (jax.nn.silu(both_parts[0]) * both_parts[1]).astype(jnp.bfloat16)
    down_part = jnp.dot(activated, down_weight, preferred_element_type=jnp.float32).astype(
        jnp.bfloat16
    )
    own_rows = tokens.shape[0]
    down_parts = lax.all_to_all(
        down_part.reshape(head_parts, own_rows, -1), "head", 0, 0, tiled=True
    )
    ffn_rows = jnp.sum(down_parts.astype(jnp.float32), axis=0)
    own_hidden = lax.dynamic_slice_in_dim(hidden_state, head_slot * own_rows, own_rows, 0)
    mixed = (own_hidden.astype(jnp.float32) + ffn_rows).astype(jnp.bfloat16)
    chosen = (accepted[:, :, None] == nodes[None, None, :]).astype(jnp.bfloat16)
    stacked = jnp.stack([key_new, value_new]).reshape(2, local_req, tree, qdl)
    new_kv = jnp.einsum(
        "rat,crtq->craq", chosen, stacked, preferred_element_type=jnp.float32
    ).astype(jnp.bfloat16)
    return (mixed, attended, new_kv)


def solution(mesh):
    return jax.shard_map(
        shards,
        mesh=mesh,
        in_specs=(
            P(("req", "head"), None),
            P(),
            P(None, None, "head"),
            P(),
            P(None, None, "head"),
            P("head", None),
            P(),
            P(None, "req", None, "head"),
            P("req", None),
            P(),
            P(),
            P(),
            P("req", None),
            P("req", None),
        ),
        out_specs=(P(("req", "head"), None), P("req", "head"), P(None, "req", None, "head")),
        check_vma=False,
    )
```

```python
import functools
import math

import jax
import jax.numpy as jnp
from jax import lax
from jax.experimental import pallas as pl
from jax.experimental.pallas import tpu as pltpu
from jax.sharding import PartitionSpec as P

HD = 64
LEVELS = 8


epsilon = 1e-06
masked_score = -1e30
highest = lax.Precision.HIGHEST


def rms_scaled(rows, gain):
    values = rows.astype(jnp.float32)
    return values * lax.rsqrt(jnp.mean(values * values, axis=-1, keepdims=True) + epsilon) * gain


def merge_parts(first, second):
    max_one, total_one, out_one = first
    max_two, total_two, out_two = second
    highest_max = jnp.maximum(max_one, max_two)
    factor_one = jnp.exp(max_one - highest_max)
    factor_two = jnp.exp(max_two - highest_max)
    return (
        highest_max,
        total_one * factor_one + total_two * factor_two,
        out_one * factor_one[..., None] + out_two * factor_two[..., None],
    )


def page_kernel(owner_ref, filled_ref, q_ref, aux_ref, cache_ref, pv_ref,
                out_ref, out_acc, max_acc, total_acc,
                *, head_local, tree, scale, pool):
    rows, page = head_local * tree, cache_ref.shape[2]
    lanes = aux_ref.shape[0]
    out_acc[...] = jnp.zeros(out_acc.shape, jnp.float32)
    max_acc[...] = jnp.full(max_acc.shape, masked_score, jnp.float32)
    total_acc[...] = jnp.zeros(total_acc.shape, jnp.float32)
    request_lane = lax.broadcasted_iota(jnp.int32, (rows, lanes), 1)
    column_head = lax.broadcasted_iota(jnp.int32, out_acc.shape[1:], 1) // HD
    aux_columns = jnp.transpose(aux_ref[...])

    def column_of(index):
        return jnp.sum(jnp.where(request_lane == index, aux_columns, 0.0), axis=1, keepdims=True)

    same_bias = column_of(lanes - 2)
    other_bias = column_of(lanes - 1)

    def pick_heads(values):
        picked = jnp.zeros(out_acc.shape[1:], jnp.float32)
        for head in range(head_local):
            picked = picked + jnp.where(
                column_head == head, values[head * tree : (head + 1) * tree], 0.0
            )
        return picked

    def one_page(step, carry):
        count = filled_ref[step]

        row = owner_ref[step]
        same = column_of(row) == pv_ref[step]
        valid = lax.broadcasted_iota(jnp.int32, (rows, page), 1) < count
        query = q_ref[row]
        stacked = jnp.concatenate(
            [
                jnp.where(column_head == head, query, jnp.zeros_like(query))
                for head in range(head_local)
            ],
            axis=0,
        )
        scores = lax.dot_general(
            stacked, cache_ref[0, step], (((1,), (1,)), ((), ())),
            preferred_element_type=jnp.float32,
        ) * scale
        scores = scores + jnp.where(same, same_bias, other_bias)
        block_max = jnp.max(jnp.where(valid, scores, masked_score), axis=1, keepdims=True)
        weights = jnp.where(valid, jnp.exp(scores - block_max), 0.0).astype(jnp.bfloat16)
        block_total = jnp.sum(weights.astype(jnp.float32), axis=1, keepdims=True)
        crossed = jnp.dot(weights, cache_ref[1, step], preferred_element_type=jnp.float32)
        old_max = max_acc[row]
        old_total = total_acc[row]
        new_max = jnp.maximum(old_max, block_max)
        keep_old = jnp.exp(old_max - new_max)
        keep_new = jnp.exp(block_max - new_max)
        max_acc[row] = new_max
        total_acc[row] = old_total * keep_old + block_total * keep_new
        out_acc[row] = out_acc[row] * pick_heads(
            jnp.broadcast_to(keep_old, crossed.shape)
        ) + pick_heads(crossed * keep_new)

        return carry

    lax.fori_loop(0, pool, one_page, 0, unroll=True)
    requests = out_ref.shape[0]
    out_ref[:, :tree, :] = out_acc[...].astype(out_ref.dtype)
    def lane_table(columns, fill):
        table = jnp.full((rows, lanes), fill, jnp.float32)
        for request in range(requests):
            table = jnp.where(request_lane == request, columns[request], table)
        return jnp.transpose(table)[:requests]

    stats = (lane_table(total_acc, 0.0), lane_table(max_acc, masked_score))
    for kind, values in enumerate(stats):
        for part in range(3):
            rounded = values.astype(out_ref.dtype)
            out_ref[:, tree + 2 * part + kind, :] = rounded
            values = values - rounded.astype(jnp.float32)


def page_attention(owner, filled, queries, row_variates, page_cache, page_variates,
                   row_bias, interpret=False):
    requests, tree, qdl = queries.shape
    pool, page = page_variates.shape
    head_local = qdl // HD
    rows = head_local * tree
    lanes = 128 * ((requests + 2 + 127) // 128)
    aux = jnp.concatenate(
        [
            row_variates.astype(jnp.float32),
            jnp.zeros((lanes - requests - 2, rows), jnp.float32),
            row_bias,
        ],
        axis=0,
    )
    kernel = functools.partial(
        page_kernel, head_local=head_local, tree=tree, scale=1.0 / math.sqrt(HD), pool=pool
    )

    def whole(shape):
        return pl.BlockSpec(shape, lambda step, *_: (0,) * len(shape))

    grid_spec = pltpu.PrefetchScalarGridSpec(
        num_scalar_prefetch=2,
        grid=(1,),
        in_specs=[
            whole((requests, tree, qdl)),
            whole((lanes, rows)),
            whole(page_cache.shape),
            whole((pool, 1, page)),
        ],
        out_specs=whole((requests, tree + 6, qdl)),
        scratch_shapes=[
            pltpu.VMEM((requests, tree, qdl), jnp.float32),
            pltpu.VMEM((requests, rows, 1), jnp.float32),
            pltpu.VMEM((requests, rows, 1), jnp.float32),
        ],
    )
    return pl.pallas_call(
        kernel,
        grid_spec=grid_spec,
        out_shape=jax.ShapeDtypeStruct((requests, tree + 6, qdl), jnp.bfloat16),
        compiler_params=pltpu.CompilerParams(dimension_semantics=("arbitrary",)),
        interpret=interpret,
    )(owner, filled, queries, aux, page_cache, page_variates[:, None, :])


def join_three(high, middle, low):
    return (high.astype(jnp.float32) + middle.astype(jnp.float32)) + low.astype(jnp.float32)


def gather_rows(rows, axis_name, parts):
    spread = jnp.broadcast_to(rows[None], (parts,) + rows.shape)
    return lax.all_to_all(spread, axis_name, 0, 0, tiled=True)


def shards(
    tokens,
    gains,
    qkv_weight,
    out_weight,
    gate_up_weight,
    down_weight,
    variate_bias,
    page_cache,
    page_variates,
    token_variates,
    cache_len,
    page_table,
    parents,
    accepted,
):
    scale = 1.0 / math.sqrt(HD)
    local_req, tree = parents.shape
    pool, page = page_variates.shape
    requests = cache_len.shape[0]
    qdl = qkv_weight.shape[2]
    head_local = qdl // HD
    head_slot = lax.axis_index("head")
    req_slot = lax.axis_index("req")
    bias_local = lax.dynamic_slice_in_dim(variate_bias, head_slot * head_local, head_local, 1)
    same_bias = bias_local[0]
    other_bias = bias_local[1]
    head_parts = lax.axis_size("head")
    group_tokens = gather_rows(tokens, "head", head_parts).reshape(-1, tokens.shape[1])
    normed = rms_scaled(group_tokens, gains[0]).astype(jnp.bfloat16)
    projected = jnp.einsum(
        "td,cdq->ctq",
        normed,
        qkv_weight,
        preferred_element_type=jnp.float32,
    ).astype(jnp.bfloat16)
    query = projected[0]
    key_new = projected[1]
    value_new = projected[2]
    all_queries = gather_rows(query, "req", requests // local_req)
    global_ids = req_slot * pool + jnp.arange(pool, dtype=jnp.int32)
    matching = (page_table[:, :, None] == global_ids[None, None, :]).astype(jnp.int32)
    owner = jnp.sum(matching * jnp.arange(requests, dtype=jnp.int32)[:, None, None], axis=(0, 1))
    page_order = jnp.sum(
        matching * jnp.arange(page_table.shape[1], dtype=jnp.int32)[None, :, None], axis=(0, 1)
    )
    owner_len = jnp.sum(matching * cache_len[:, None, None], axis=(0, 1))
    in_use = jnp.sum(matching, axis=(0, 1))
    filled = jnp.clip(owner_len - page_order * page, 0, page) * in_use
    valid = jnp.arange(page, dtype=jnp.int32)[None, :] < filled[:, None]
    head_of_column = jnp.arange(qdl, dtype=jnp.int32) // HD
    head_mask = jnp.arange(head_local, dtype=jnp.int32)[:, None] == head_of_column[None, :]
    split_rows = head_local * tree
    row_variates = jnp.broadcast_to(
        token_variates.reshape(requests, 1, tree), (requests, head_local, tree)
    ).reshape(requests, split_rows)
    row_bias = jnp.broadcast_to(bias_local[:, :, None], (2, head_local, tree)).reshape(
        2, split_rows
    )
    packed = page_attention(
        jnp.clip(owner, 0, requests - 1),
        filled,
        all_queries.reshape(requests, tree, qdl),
        row_variates,
        page_cache,
        page_variates,
        row_bias,
    )
    received = lax.all_to_all(packed, "req", split_axis=0, concat_axis=0, tiled=True)
    sources = lax.axis_size("req")
    received = received.reshape((sources, local_req) + packed.shape[1:])
    source_out = received[:, :, :tree].astype(jnp.float32)
    got_stats = join_three(
        *[received[:, :, tree + 2 * part : tree + 2 * part + 2] for part in range(3)]
    )
    source_total = got_stats[:, :, 0].reshape(sources, local_req, head_local, tree)
    source_max = got_stats[:, :, 1].reshape(sources, local_req, head_local, tree)
    largest = jnp.max(source_max, axis=0)
    source_factor = jnp.exp(source_max - largest[None])
    column_factor = jnp.sum(
        jnp.where(head_mask[None, None, :, None, :], source_factor[..., None], 0.0), axis=2
    )
    cached_part = (
        largest.transpose(0, 2, 1),
        jnp.sum(source_total * source_factor, axis=0).transpose(0, 2, 1),
        jnp.sum(source_out * column_factor, axis=0).reshape(local_req, tree, head_local, HD),
    )
    tree_query = query.reshape(local_req, tree, head_local, HD)
    tree_key = key_new.reshape(local_req, tree, head_local, HD)
    tree_value = value_new.reshape(local_req, tree, head_local, HD)
    nodes = jnp.arange(tree, dtype=jnp.int32)
    reach = (parents[:, :, None] == nodes[None, None, :]).astype(jnp.float32) + jnp.eye(
        tree, dtype=jnp.float32
    )[None]
    for step in range(LEVELS.bit_length()):
        reach = jnp.minimum(jnp.einsum("rij,rjk->rik", reach, reach, precision=highest), 1.0)
    allowed = reach > 0.5
    group_variates = lax.dynamic_slice_in_dim(
        token_variates, req_slot * local_req * tree, local_req * tree, 0
    ).reshape(local_req, tree)
    tree_scores = (
        jnp.einsum("rihd,rjhd->rihj", tree_query, tree_key, preferred_element_type=jnp.float32)
        * scale
    )
    same_tree = group_variates[:, :, None] == group_variates[:, None, :]
    tree_scores = tree_scores + jnp.where(
        same_tree[:, :, None, :], same_bias[None, None, :, None], other_bias[None, None, :, None]
    )
    keep_tree = allowed[:, :, None, :]
    tree_max = jnp.max(jnp.where(keep_tree, tree_scores, masked_score), axis=-1)
    tree_weights = jnp.where(keep_tree, jnp.exp(tree_scores - tree_max[..., None]), 0.0).astype(
        jnp.bfloat16
    )
    tree_total = jnp.sum(tree_weights, axis=-1, dtype=jnp.float32)
    tree_out = jnp.einsum(
        "rihj,rjhd->rihd", tree_weights, tree_value, preferred_element_type=jnp.float32
    )
    final_max, final_total, final_out = merge_parts(cached_part, (tree_max, tree_total, tree_out))
    attended = (
        (final_out / final_total[..., None]).astype(jnp.bfloat16).reshape(local_req * tree, qdl)
    )
    group_rows = local_req * tree
    token_heads = (
        gather_rows(attended, "head", head_parts).transpose(1, 0, 2).reshape(group_rows, -1)
    )
    attention_rows = jnp.dot(token_heads, out_weight, preferred_element_type=jnp.float32)
    hidden_state = (group_tokens.astype(jnp.float32) + attention_rows).astype(jnp.bfloat16)
    normed_two = rms_scaled(hidden_state, gains[1]).astype(jnp.bfloat16)
    both_parts = jnp.einsum(
        "td,cdf->ctf",
        normed_two,
        gate_up_weight,
        preferred_element_type=jnp.float32,
    )
    activated = (jax.nn.silu(both_parts[0]) * both_parts[1]).astype(jnp.bfloat16)
    down_part = jnp.dot(activated, down_weight, preferred_element_type=jnp.float32).astype(
        jnp.bfloat16
    )
    own_rows = tokens.shape[0]
    down_parts = lax.all_to_all(
        down_part.reshape(head_parts, own_rows, -1), "head", 0, 0, tiled=True
    )
    ffn_rows = jnp.sum(down_parts.astype(jnp.float32), axis=0)
    own_hidden = lax.dynamic_slice_in_dim(hidden_state, head_slot * own_rows, own_rows, 0)
    mixed = (own_hidden.astype(jnp.float32) + ffn_rows).astype(jnp.bfloat16)
    chosen = (accepted[:, :, None] == nodes[None, None, :]).astype(jnp.bfloat16)
    stacked = jnp.stack([key_new, value_new]).reshape(2, local_req, tree, qdl)
    new_kv = jnp.einsum(
        "rat,crtq->craq", chosen, stacked, preferred_element_type=jnp.float32
    ).astype(jnp.bfloat16)
    return (mixed, attended, new_kv)


def solution(mesh):
    return jax.shard_map(
        shards,
        mesh=mesh,
        in_specs=(
            P(("req", "head"), None),
            P(),
            P(None, None, "head"),
            P(),
            P(None, None, "head"),
            P("head", None),
            P(),
            P(None, "req", None, "head"),
            P("req", None),
            P(),
            P(),
            P(),
            P("req", None),
            P("req", None),
        ),
        out_specs=(P(("req", "head"), None), P("req", "head"), P(None, "req", None, "head")),
        check_vma=False,
    )
```

```python
import functools
import math

import jax
import jax.numpy as jnp
from jax import lax
from jax.experimental import pallas as pl
from jax.experimental.pallas import tpu as pltpu
from jax.sharding import PartitionSpec as P

HD = 64
LEVELS = 8


epsilon = 1e-06
masked_score = -1e30
highest = lax.Precision.HIGHEST


def rms_scaled(rows, gain):
    values = rows.astype(jnp.float32)
    return values * lax.rsqrt(jnp.mean(values * values, axis=-1, keepdims=True) + epsilon) * gain


def merge_parts(first, second):
    max_one, total_one, out_one = first
    max_two, total_two, out_two = second
    highest_max = jnp.maximum(max_one, max_two)
    factor_one = jnp.exp(max_one - highest_max)
    factor_two = jnp.exp(max_two - highest_max)
    return (
        highest_max,
        total_one * factor_one + total_two * factor_two,
        out_one * factor_one[..., None] + out_two * factor_two[..., None],
    )


def page_kernel(owner_ref, filled_ref, q_ref, aux_ref, cache_ref, pv_ref,
                out_ref, out_acc, max_acc, total_acc,
                *, head_local, tree, scale, pool):
    rows, page = head_local * tree, cache_ref.shape[2]
    lanes = aux_ref.shape[0]
    out_acc[...] = jnp.zeros(out_acc.shape, jnp.float32)
    max_acc[...] = jnp.full(max_acc.shape, masked_score, jnp.float32)
    total_acc[...] = jnp.zeros(total_acc.shape, jnp.float32)
    request_lane = lax.broadcasted_iota(jnp.int32, max_acc.shape, 1)
    column_head = lax.broadcasted_iota(jnp.int32, out_acc.shape[1:], 1) // HD
    aux_columns = jnp.transpose(aux_ref[...])

    def column_of(index):
        return jnp.sum(jnp.where(request_lane == index, aux_columns, 0.0), axis=1, keepdims=True)

    same_bias = column_of(lanes - 2)
    other_bias = column_of(lanes - 1)

    def pick_heads(values):
        picked = jnp.zeros(out_acc.shape[1:], jnp.float32)
        for head in range(head_local):
            picked = picked + jnp.where(
                column_head == head, values[head * tree : (head + 1) * tree], 0.0
            )
        return picked

    def one_page(step, carry):
        count = filled_ref[step]

        row = owner_ref[step]
        same = column_of(row) == pv_ref[step]
        valid = lax.broadcasted_iota(jnp.int32, (rows, page), 1) < count
        query = q_ref[row]
        stacked = jnp.concatenate(
            [
                jnp.where(column_head == head, query, jnp.zeros_like(query))
                for head in range(head_local)
            ],
            axis=0,
        )
        scores = lax.dot_general(
            stacked, cache_ref[0, step], (((1,), (1,)), ((), ())),
            preferred_element_type=jnp.float32,
        ) * scale
        scores = scores + jnp.where(same, same_bias, other_bias)
        block_max = jnp.max(jnp.where(valid, scores, masked_score), axis=1, keepdims=True)
        weights = jnp.where(valid, jnp.exp(scores - block_max), 0.0).astype(jnp.bfloat16)
        block_total = jnp.sum(weights.astype(jnp.float32), axis=1, keepdims=True)
        crossed = jnp.dot(weights, cache_ref[1, step], preferred_element_type=jnp.float32)
        is_row = request_lane == row
        old_max = jnp.sum(jnp.where(is_row, max_acc[...], 0.0), axis=1, keepdims=True)
        old_total = jnp.sum(jnp.where(is_row, total_acc[...], 0.0), axis=1, keepdims=True)
        new_max = jnp.maximum(old_max, block_max)
        keep_old = jnp.exp(old_max - new_max)
        keep_new = jnp.exp(block_max - new_max)
        max_acc[...] = jnp.where(is_row, new_max, max_acc[...])
        total_acc[...] = jnp.where(
            is_row, old_total * keep_old + block_total * keep_new, total_acc[...]
        )
        out_acc[row] = out_acc[row] * pick_heads(
            jnp.broadcast_to(keep_old, crossed.shape)
        ) + pick_heads(crossed * keep_new)

        return carry

    lax.fori_loop(0, pool, one_page, 0, unroll=4)
    requests = out_ref.shape[0]
    out_ref[:, :tree, :] = out_acc[...].astype(out_ref.dtype)
    stats = (
        jnp.transpose(total_acc[...])[:requests],
        jnp.transpose(max_acc[...])[:requests],
    )
    for kind, values in enumerate(stats):
        for part in range(3):
            rounded = values.astype(out_ref.dtype)
            out_ref[:, tree + 2 * part + kind, :] = rounded
            values = values - rounded.astype(jnp.float32)


def page_attention(owner, filled, queries, row_variates, page_cache, page_variates,
                   row_bias, interpret=False):
    requests, tree, qdl = queries.shape
    pool, page = page_variates.shape
    head_local = qdl // HD
    rows = head_local * tree
    lanes = 128 * ((requests + 2 + 127) // 128)
    aux = jnp.concatenate(
        [
            row_variates.astype(jnp.float32),
            jnp.zeros((lanes - requests - 2, rows), jnp.float32),
            row_bias,
        ],
        axis=0,
    )
    kernel = functools.partial(
        page_kernel, head_local=head_local, tree=tree, scale=1.0 / math.sqrt(HD), pool=pool
    )

    def whole(shape):
        return pl.BlockSpec(shape, lambda step, *_: (0,) * len(shape))

    grid_spec = pltpu.PrefetchScalarGridSpec(
        num_scalar_prefetch=2,
        grid=(1,),
        in_specs=[
            whole((requests, tree, qdl)),
            whole((lanes, rows)),
            whole(page_cache.shape),
            whole((pool, 1, page)),
        ],
        out_specs=whole((requests, tree + 6, qdl)),
        scratch_shapes=[
            pltpu.VMEM((requests, tree, qdl), jnp.float32),
            pltpu.VMEM((rows, lanes), jnp.float32),
            pltpu.VMEM((rows, lanes), jnp.float32),
        ],
    )
    return pl.pallas_call(
        kernel,
        grid_spec=grid_spec,
        out_shape=jax.ShapeDtypeStruct((requests, tree + 6, qdl), jnp.bfloat16),
        compiler_params=pltpu.CompilerParams(dimension_semantics=("arbitrary",)),
        interpret=interpret,
    )(owner, filled, queries, aux, page_cache, page_variates[:, None, :])


def join_three(high, middle, low):
    return (high.astype(jnp.float32) + middle.astype(jnp.float32)) + low.astype(jnp.float32)


def gather_rows(rows, axis_name, parts):
    spread = jnp.broadcast_to(rows[None], (parts,) + rows.shape)
    return lax.all_to_all(spread, axis_name, 0, 0, tiled=True)


def shards(
    tokens,
    gains,
    qkv_weight,
    out_weight,
    gate_up_weight,
    down_weight,
    variate_bias,
    page_cache,
    page_variates,
    token_variates,
    cache_len,
    page_table,
    parents,
    accepted,
):
    scale = 1.0 / math.sqrt(HD)
    local_req, tree = parents.shape
    pool, page = page_variates.shape
    requests = cache_len.shape[0]
    qdl = qkv_weight.shape[2]
    head_local = qdl // HD
    head_slot = lax.axis_index("head")
    req_slot = lax.axis_index("req")
    bias_local = lax.dynamic_slice_in_dim(variate_bias, head_slot * head_local, head_local, 1)
    same_bias = bias_local[0]
    other_bias = bias_local[1]
    head_parts = lax.axis_size("head")
    group_tokens = gather_rows(tokens, "head", head_parts).reshape(-1, tokens.shape[1])
    normed = rms_scaled(group_tokens, gains[0]).astype(jnp.bfloat16)
    projected = jnp.einsum(
        "td,cdq->ctq",
        normed,
        qkv_weight,
        preferred_element_type=jnp.float32,
    ).astype(jnp.bfloat16)
    query = projected[0]
    key_new = projected[1]
    value_new = projected[2]
    all_queries = gather_rows(query, "req", requests // local_req)
    global_ids = req_slot * pool + jnp.arange(pool, dtype=jnp.int32)
    matching = (page_table[:, :, None] == global_ids[None, None, :]).astype(jnp.int32)
    owner = jnp.sum(matching * jnp.arange(requests, dtype=jnp.int32)[:, None, None], axis=(0, 1))
    page_order = jnp.sum(
        matching * jnp.arange(page_table.shape[1], dtype=jnp.int32)[None, :, None], axis=(0, 1)
    )
    owner_len = jnp.sum(matching * cache_len[:, None, None], axis=(0, 1))
    in_use = jnp.sum(matching, axis=(0, 1))
    filled = jnp.clip(owner_len - page_order * page, 0, page) * in_use
    valid = jnp.arange(page, dtype=jnp.int32)[None, :] < filled[:, None]
    head_of_column = jnp.arange(qdl, dtype=jnp.int32) // HD
    head_mask = jnp.arange(head_local, dtype=jnp.int32)[:, None] == head_of_column[None, :]
    split_rows = head_local * tree
    row_variates = jnp.broadcast_to(
        token_variates.reshape(requests, 1, tree), (requests, head_local, tree)
    ).reshape(requests, split_rows)
    row_bias = jnp.broadcast_to(bias_local[:, :, None], (2, head_local, tree)).reshape(
        2, split_rows
    )
    packed = page_attention(
        jnp.clip(owner, 0, requests - 1),
        filled,
        all_queries.reshape(requests, tree, qdl),
        row_variates,
        page_cache,
        page_variates,
        row_bias,
    )
    received = lax.all_to_all(packed, "req", split_axis=0, concat_axis=0, tiled=True)
    sources = lax.axis_size("req")
    received = received.reshape((sources, local_req) + packed.shape[1:])
    source_out = received[:, :, :tree].astype(jnp.float32)
    got_stats = join_three(
        *[received[:, :, tree + 2 * part : tree + 2 * part + 2] for part in range(3)]
    )
    source_total = got_stats[:, :, 0].reshape(sources, local_req, head_local, tree)
    source_max = got_stats[:, :, 1].reshape(sources, local_req, head_local, tree)
    largest = jnp.max(source_max, axis=0)
    source_factor = jnp.exp(source_max - largest[None])
    column_factor = jnp.sum(
        jnp.where(head_mask[None, None, :, None, :], source_factor[..., None], 0.0), axis=2
    )
    cached_part = (
        largest.transpose(0, 2, 1),
        jnp.sum(source_total * source_factor, axis=0).transpose(0, 2, 1),
        jnp.sum(source_out * column_factor, axis=0).reshape(local_req, tree, head_local, HD),
    )
    tree_query = query.reshape(local_req, tree, head_local, HD)
    tree_key = key_new.reshape(local_req, tree, head_local, HD)
    tree_value = value_new.reshape(local_req, tree, head_local, HD)
    nodes = jnp.arange(tree, dtype=jnp.int32)
    reach = (parents[:, :, None] == nodes[None, None, :]).astype(jnp.float32) + jnp.eye(
        tree, dtype=jnp.float32
    )[None]
    for step in range(LEVELS.bit_length()):
        reach = jnp.minimum(jnp.einsum("rij,rjk->rik", reach, reach, precision=highest), 1.0)
    allowed = reach > 0.5
    group_variates = lax.dynamic_slice_in_dim(
        token_variates, req_slot * local_req * tree, local_req * tree, 0
    ).reshape(local_req, tree)
    tree_scores = (
        jnp.einsum("rihd,rjhd->rihj", tree_query, tree_key, preferred_element_type=jnp.float32)
        * scale
    )
    same_tree = group_variates[:, :, None] == group_variates[:, None, :]
    tree_scores = tree_scores + jnp.where(
        same_tree[:, :, None, :], same_bias[None, None, :, None], other_bias[None, None, :, None]
    )
    keep_tree = allowed[:, :, None, :]
    tree_max = jnp.max(jnp.where(keep_tree, tree_scores, masked_score), axis=-1)
    tree_weights = jnp.where(keep_tree, jnp.exp(tree_scores - tree_max[..., None]), 0.0).astype(
        jnp.bfloat16
    )
    tree_total = jnp.sum(tree_weights, axis=-1, dtype=jnp.float32)
    tree_out = jnp.einsum(
        "rihj,rjhd->rihd", tree_weights, tree_value, preferred_element_type=jnp.float32
    )
    final_max, final_total, final_out = merge_parts(cached_part, (tree_max, tree_total, tree_out))
    attended = (
        (final_out / final_total[..., None]).astype(jnp.bfloat16).reshape(local_req * tree, qdl)
    )
    group_rows = local_req * tree
    token_heads = (
        gather_rows(attended, "head", head_parts).transpose(1, 0, 2).reshape(group_rows, -1)
    )
    attention_rows = jnp.dot(token_heads, out_weight, preferred_element_type=jnp.float32)
    hidden_state = (group_tokens.astype(jnp.float32) + attention_rows).astype(jnp.bfloat16)
    normed_two = rms_scaled(hidden_state, gains[1]).astype(jnp.bfloat16)
    both_parts = jnp.einsum(
        "td,cdf->ctf",
        normed_two,
        gate_up_weight,
        preferred_element_type=jnp.float32,
    )
    activated = (jax.nn.silu(both_parts[0]) * both_parts[1]).astype(jnp.bfloat16)
    down_part = jnp.dot(activated, down_weight, preferred_element_type=jnp.float32).astype(
        jnp.bfloat16
    )
    own_rows = tokens.shape[0]
    down_parts = lax.all_to_all(
        down_part.reshape(head_parts, own_rows, -1), "head", 0, 0, tiled=True
    )
    ffn_rows = jnp.sum(down_parts.astype(jnp.float32), axis=0)
    own_hidden = lax.dynamic_slice_in_dim(hidden_state, head_slot * own_rows, own_rows, 0)
    mixed = (own_hidden.astype(jnp.float32) + ffn_rows).astype(jnp.bfloat16)
    chosen = (accepted[:, :, None] == nodes[None, None, :]).astype(jnp.bfloat16)
    stacked = jnp.stack([key_new, value_new]).reshape(2, local_req, tree, qdl)
    new_kv = jnp.einsum(
        "rat,crtq->craq", chosen, stacked, preferred_element_type=jnp.float32
    ).astype(jnp.bfloat16)
    return (mixed, attended, new_kv)


def solution(mesh):
    return jax.shard_map(
        shards,
        mesh=mesh,
        in_specs=(
            P(("req", "head"), None),
            P(),
            P(None, None, "head"),
            P(),
            P(None, None, "head"),
            P("head", None),
            P(),
            P(None, "req", None, "head"),
            P("req", None),
            P(),
            P(),
            P(),
            P("req", None),
            P("req", None),
        ),
        out_specs=(P(("req", "head"), None), P("req", "head"), P(None, "req", None, "head")),
        check_vma=False,
    )
```
